32 devices in a mesh: groups: 2 (over x), row: 16 (over z, y, core).
Axes of the slice: x: 2, y: 2, z: 4, core: 2. Of those that a mesh axis runs over, the one named last changes fastest.
Arguments:
- atom_feat: bfloat16 [4096, 2, 128], P(('groups', 'row')), parts along dimension 0, may hold values from -6 to 6
- window_shift: int32 [128], P(('groups', 'row')), parts along dimension 0, may hold values from -16 to 16, as said below
- atom_token: int32 [4096], P('groups'), parts along dimension 0, may hold values from 0 to 255, as said below
- token_in: bfloat16 [512, 2, 768], P(('groups', 'row')), parts along dimension 0, may hold values from -6 to 6
- pair: bfloat16 [512, 256, 128], P(('groups', 'row')), parts along dimension 0, may hold values from -6 to 6
- key_mask: int32 [512], P('groups'), parts along dimension 0, may hold values from 0 to 1, as said below
- w_atom_query: bfloat16 [128, 128], replicated, may hold values from -2 to 2
- w_atom_key: bfloat16 [128, 128], replicated, may hold values from -2 to 2
- w_atom_value: bfloat16 [128, 128], replicated, may hold values from -0.5 to 0.5
- w_atom_out: bfloat16 [128, 128], replicated, may hold values from -0.5 to 0.5
- w_to_token: bfloat16 [128, 768], replicated, may hold values from -0.5 to 0.5
- w_query: bfloat16 [768, 768], replicated, may hold values from -0.21875 to 0.21875
- w_key: bfloat16 [768, 768], replicated, may hold values from -0.21875 to 0.21875
- w_value: bfloat16 [768, 768], replicated, may hold values from -0.21875 to 0.21875
- w_out: bfloat16 [768, 768], replicated, may hold values from -0.21875 to 0.21875
- w_bias: bfloat16 [128, 16], replicated, may hold values from -4 to 4
Outputs:
- atom_out: bfloat16 [4096, 2, 128], P(('groups', 'row')), parts along dimension 0
- token_out: bfloat16 [512, 2, 768], P(('groups', 'row')), parts along dimension 0
The draws below stay inside these ranges and needn't reach their ends.
There are 2 independent parts, one for each index of `groups`. The reference program is written for one: setup_inputs(seed, part) draws one part's arguments, and reference() takes and returns one part's arrays. A program takes and returns all parts, laid end to end along the dimension named above; an argument that names none is the same for every part. Nothing has to cross between parts.
Inputs may be any that keep to these rules, and one draw needn't show every extreme that they name: `window_shift`: one entry per query block, moving its key window. `atom_token`: never falls along the atoms; token 0 starts at atom 0 and token t's first atom is 8 t + r with r from -3 to 3, and with r from 1 to 3 where t is a positive multiple of 16. `key_mask`: token 0 is always kept.
All inputs are finite; a program needn't handle non-finite values.
Results may differ from the reference program's by a relative error of at most 0.0095.
Values may be sent and summed in bfloat16 or wider, within the bound.
No kernel may reach another device: no remote copies, remote signals or barrier semaphores. Data moves between devices by JAX's collectives and lax.ppermute only.
A program may use at most 64 MiB of HBM per device.

```python
import math
import jax
import jax.numpy as jnp
from jax import lax

C_ATOM = 128
ATOM_HEADS = 4
QBLOCK = 32
KWIN = 128
SHIFT = 16
C_TOKEN = 768
TOKEN_HEADS = 16
C_PAIR = 128
SAMPLES = 2
TOK_DEV = 16
ATOMS = 2048
TOKENS = 256


atom_gap = 0.008


pair_gap = 0.0083


bias_lift = 40.0


def sign_rows(width):
    position = jnp.arange(width, dtype=jnp.int32)
    alternate = (1 - 2 * (position % 2)).astype(jnp.float32)
    paired = (1 - 2 * (position // 2 % 2)).astype(jnp.float32)
    return (alternate, paired)


def atom_lift():
    return math.sqrt(255.0 * math.sqrt(C_ATOM // ATOM_HEADS))


def atom_column(key):
    return jax.random.randint(jax.random.fold_in(key, 11), (), 0, C_ATOM)


def clipped_weight(key, fan_rows, out_cols):
    values = jnp.clip(jax.random.normal(key, (fan_rows, out_cols), jnp.float32), -5.0, 5.0)
    return values / math.sqrt(fan_rows)


def draw_w_atom_query(key, part):
    random_part = clipped_weight(jax.random.fold_in(key, 21), C_ATOM, C_ATOM)
    alternate, paired = sign_rows(C_ATOM)
    picked = jnp.arange(C_ATOM, dtype=jnp.int32)[None, :] == atom_column(key)
    special = atom_lift() / C_ATOM * alternate[:, None] + 0.05 * random_part
    return jnp.where(picked, special, random_part).astype(jnp.bfloat16)


def draw_w_atom_key(key, part):
    random_part = clipped_weight(jax.random.fold_in(key, 22), C_ATOM, C_ATOM)
    alternate, paired = sign_rows(C_ATOM)
    picked = jnp.arange(C_ATOM, dtype=jnp.int32)[None, :] == atom_column(key)
    special = atom_lift() / C_ATOM * (alternate + paired)[:, None] + 0.05 * random_part
    return jnp.where(picked, special, random_part).astype(jnp.bfloat16)


def draw_w_bias(key, part):
    random_part = clipped_weight(jax.random.fold_in(key, 31), C_PAIR, TOKEN_HEADS)
    alternate, paired = sign_rows(C_PAIR)
    chosen = jax.random.randint(jax.random.fold_in(key, 32), (), 0, TOKEN_HEADS)
    picked = jnp.arange(TOKEN_HEADS, dtype=jnp.int32)[None, :] == chosen
    lifted = random_part + bias_lift / C_PAIR * alternate[:, None]
    return jnp.where(picked, lifted, random_part).astype(jnp.bfloat16)


def draw_atom_feat(key, part):
    extent = (ATOMS, SAMPLES, C_ATOM)
    values = jax.random.normal(jax.random.fold_in(key, 41), extent, jnp.float32)
    alternate, paired = sign_rows(C_ATOM)
    strength = jnp.array([1.0, 0.85, 0.7, 1.0], jnp.float32)[:, None, None]
    places = jax.random.permutation(jax.random.fold_in(key, 43), ATOMS // 2)[:4] * 2
    noise = jax.random.normal(jax.random.fold_in(key, 44), (2, 4, SAMPLES, C_ATOM), jnp.float32)
    noise = noise - jnp.sum(noise * alternate, axis=-1, keepdims=True) / C_ATOM * alternate
    noise = noise - jnp.sum(noise * paired, axis=-1, keepdims=True) / C_ATOM * paired
    leading = strength * alternate + jnp.sqrt(1.0 - strength ** 2) * noise[0]
    shared = strength * (1.0 - atom_gap) / 2.0
    trailing = shared * (alternate + paired) + jnp.sqrt(1.0 - 2.0 * shared ** 2) * noise[1]
    values = values.at[places].set(1.5 * leading).at[places + 1].set(1.5 * trailing)
    return jnp.clip(values, -6.0, 6.0).astype(jnp.bfloat16)


def draw_pair(key, part):
    extent = (TOKENS, TOKENS, C_PAIR)
    values = jax.random.normal(jax.random.fold_in(key, 51), extent, jnp.float32)
    alternate, paired = sign_rows(C_PAIR)
    strength = jnp.array([6.0, 6.0, 5.0, 4.0], jnp.float32)
    rows_hit = jax.random.permutation(jax.random.fold_in(key, 53), TOKENS)[:4]
    near_cols = jax.random.randint(jax.random.fold_in(key, 54), (4,), 1, TOKENS).at[0].set(0)
    far_cols = (near_cols + jax.random.randint(jax.random.fold_in(key, 55), (4,), 1, TOKENS)) % TOKENS
    values = values.at[rows_hit, near_cols].set(strength[:, None] * alternate[None, :])
    values = values.at[rows_hit, far_cols].set((strength * (1.0 - pair_gap))[:, None] * alternate[None, :])
    return jnp.clip(values, -6.0, 6.0).astype(jnp.bfloat16)


def draw_window_shift(key, part):
    count = ATOMS // QBLOCK
    moves = jax.random.randint(key, (count,), -SHIFT, SHIFT + 1).astype(jnp.int32)
    return moves.at[0].set(SHIFT).at[count - 1].set(-SHIFT)


def draw_atom_token(key, part):
    jitter = jax.random.randint(jax.random.fold_in(key, 61), (TOKENS,), -3, 4).astype(jnp.int32)
    edge = jax.random.randint(jax.random.fold_in(key, 62), (TOKENS,), 1, 4).astype(jnp.int32)
    position = jnp.arange(TOKENS, dtype=jnp.int32)
    jitter = jnp.where(position % TOK_DEV == 0, edge, jitter)
    jitter = jitter.at[0].set(0).at[1].set(-3).at[2].set(3).at[TOK_DEV].set(3).at[2 * TOK_DEV].set(1)
    starts = 8 * position + jitter
    marker = jnp.zeros((ATOMS,), jnp.int32).at[starts[1:]].set(1)
    return jnp.cumsum(marker).astype(jnp.int32)


def draw_key_mask(key, part):
    flags = (jax.random.randint(key, (TOKENS,), 0, 8) < 7).astype(jnp.int32)
    return flags.at[0].set(1)


def levels(key, shape, shards, least, high):
    level, own = 1.0, jax.random.fold_in(key, 6)
    for dim, shards_of in shards:
        steps = jnp.exp(jax.random.uniform(jax.random.fold_in(own, dim), (shards_of,), jnp.float32, least / len(shards), high / len(shards)))
        level = level * jnp.repeat(steps, shape[dim] // shards_of).reshape([-1 if axis == dim else 1 for axis in range(len(shape))])
    return level


def bell_draw(stream_key, shape, scale, limit, shards=(), kind=jnp.bfloat16):
    loudness = levels(stream_key, shape, shards, -0.22, 0.18) if shards else 1.0
    drawn = jax.random.normal(stream_key, shape, jnp.float32) * scale * loudness
    return jnp.minimum(jnp.maximum(drawn, -limit), limit).astype(kind)


def setup_inputs(seed: int = 0, part: int = 0) -> dict:
    keys = jax.random.split(jax.random.key(seed), 17)
    part_splits = jax.random.split(jax.random.fold_in(keys[16], part), 17)
    atom_feat = draw_atom_feat(jax.random.fold_in(jax.random.fold_in(keys[16], part), 71), part)
    window_shift = draw_window_shift(jax.random.fold_in(jax.random.fold_in(keys[16], part), 71), part)
    atom_token = draw_atom_token(jax.random.fold_in(jax.random.fold_in(keys[16], part), 71), part)
    token_in = bell_draw(part_splits[3], (TOKENS, SAMPLES, C_TOKEN), 1.0, 6.0, ((0, 16),))
    pair = draw_pair(jax.random.fold_in(jax.random.fold_in(keys[16], part), 71), part)
    key_mask = draw_key_mask(jax.random.fold_in(jax.random.fold_in(keys[16], part), 71), part)
    w_atom_query = draw_w_atom_query(jax.random.fold_in(keys[16], 71), part)
    w_atom_key = draw_w_atom_key(jax.random.fold_in(keys[16], 71), part)
    w_atom_value = bell_draw(keys[8], (C_ATOM, C_ATOM), C_ATOM ** -0.5, 0.5)
    w_atom_out = bell_draw(keys[9], (C_ATOM, C_ATOM), C_ATOM ** -0.5, 0.5)
    w_to_token = bell_draw(keys[10], (C_ATOM, C_TOKEN), C_ATOM ** -0.5, 0.5)
    w_query = bell_draw(keys[11], (C_TOKEN, C_TOKEN), C_TOKEN ** -0.5, 0.21875)
    w_key = bell_draw(keys[12], (C_TOKEN, C_TOKEN), C_TOKEN ** -0.5, 0.21875)
    w_value = bell_draw(keys[13], (C_TOKEN, C_TOKEN), C_TOKEN ** -0.5, 0.21875)
    w_out = bell_draw(keys[14], (C_TOKEN, C_TOKEN), C_TOKEN ** -0.5, 0.21875)
    w_bias = draw_w_bias(jax.random.fold_in(keys[16], 71), part)
    return {"atom_feat": atom_feat, "window_shift": window_shift, "atom_token": atom_token, "token_in": token_in, "pair": pair, "key_mask": key_mask, "w_atom_query": w_atom_query, "w_atom_key": w_atom_key, "w_atom_value": w_atom_value, "w_atom_out": w_atom_out, "w_to_token": w_to_token, "w_query": w_query, "w_key": w_key, "w_value": w_value, "w_out": w_out, "w_bias": w_bias}


def layer_norm(x):
    x = x.astype(jnp.float32)
    mean = lax.optimization_barrier(jnp.mean(x, axis=-1, keepdims=True))
    var = lax.optimization_barrier(jnp.mean((x - mean) ** 2, axis=-1, keepdims=True))
    return (x - mean) / jnp.sqrt(var + 1e-05)

def project(x, weight):
    return jnp.einsum('asc,cd->asd', x.astype(jnp.float32), weight.astype(jnp.float32), precision=lax.Precision.HIGHEST)

def reference(atom_feat, window_shift, atom_token, token_in, pair, key_mask, w_atom_query, w_atom_key, w_atom_value, w_atom_out, w_to_token, w_query, w_key, w_value, w_out, w_bias):
    high = lax.Precision.HIGHEST
    normed = layer_norm(atom_feat).astype(jnp.bfloat16)
    query = project(normed, w_atom_query).astype(jnp.bfloat16)
    keyed = project(normed, w_atom_key).astype(jnp.bfloat16)
    valued = project(normed, w_atom_value).astype(jnp.bfloat16)
    blocks = ATOMS // QBLOCK
    margin = (KWIN - QBLOCK) // 2
    border = margin + SHIFT
    starts = jnp.arange(blocks, dtype=jnp.int32) * QBLOCK - margin + window_shift
    places = starts[:, None] + jnp.arange(KWIN, dtype=jnp.int32)[None, :]
    valid = (places >= 0) & (places < ATOMS)
    padding = ((border, border), (0, 0), (0, 0))
    window_k = jnp.take(jnp.pad(keyed, padding), places + border, axis=0)
    window_v = jnp.take(jnp.pad(valued, padding), places + border, axis=0)
    head_dim = C_ATOM // ATOM_HEADS
    qblock = query.reshape(blocks, QBLOCK, SAMPLES, ATOM_HEADS, head_dim).astype(jnp.float32)
    kblock = window_k.reshape(blocks, KWIN, SAMPLES, ATOM_HEADS, head_dim).astype(jnp.float32)
    vblock = window_v.reshape(blocks, KWIN, SAMPLES, ATOM_HEADS, head_dim).astype(jnp.float32)
    scores = jnp.einsum('bqshd,bkshd->bshqk', qblock, kblock, precision=high) / jnp.sqrt(jnp.float32(head_dim))
    keep = valid[:, None, None, None, :]
    scores = jnp.where(keep, scores, -1e+30)
    top = lax.optimization_barrier(jnp.max(scores, axis=-1, keepdims=True))
    expo = jnp.where(keep, jnp.exp(scores - top), 0.0)
    total = lax.optimization_barrier(jnp.sum(expo, axis=-1))
    weights = expo.astype(jnp.bfloat16).astype(jnp.float32)
    mixed = jnp.einsum('bshqk,bkshd->bqshd', weights, vblock, precision=high)
    mixed = mixed / jnp.transpose(total, (0, 3, 1, 2))[..., None]
    mixed = mixed.astype(jnp.bfloat16).reshape(ATOMS, SAMPLES, C_ATOM)
    atom_out = (atom_feat.astype(jnp.float32) + project(mixed, w_atom_out)).astype(jnp.bfloat16)
    hidden = jax.nn.relu(project(atom_out, w_to_token))
    sums = jax.ops.segment_sum(hidden, atom_token, num_segments=TOKENS)
    counts = jax.ops.segment_sum(jnp.ones((ATOMS,), jnp.float32), atom_token, num_segments=TOKENS)
    state = (token_in.astype(jnp.float32) + sums / counts[:, None, None]).astype(jnp.bfloat16)
    tnorm = layer_norm(state).astype(jnp.bfloat16)
    tdim = C_TOKEN // TOKEN_HEADS
    tq = project(tnorm, w_query).astype(jnp.bfloat16).reshape(TOKENS, SAMPLES, TOKEN_HEADS, tdim).astype(jnp.float32)
    tk = project(tnorm, w_key).astype(jnp.bfloat16).reshape(TOKENS, SAMPLES, TOKEN_HEADS, tdim).astype(jnp.float32)
    tv = project(tnorm, w_value).astype(jnp.bfloat16).reshape(TOKENS, SAMPLES, TOKEN_HEADS, tdim).astype(jnp.float32)
    bias = jnp.einsum('qkc,ch->hqk', pair.astype(jnp.float32), w_bias.astype(jnp.float32), precision=high)
    tscore = jnp.einsum('qshd,kshd->shqk', tq, tk, precision=high) / jnp.sqrt(jnp.float32(tdim)) + bias[None]
    flags = (key_mask > 0)[None, None, None, :]
    tscore = jnp.where(flags, tscore, -1e+30)
    ttop = lax.optimization_barrier(jnp.max(tscore, axis=-1, keepdims=True))
    texp = jnp.where(flags, jnp.exp(tscore - ttop), 0.0)
    ttotal = lax.optimization_barrier(jnp.sum(texp, axis=-1))
    tmix = jnp.einsum('shqk,kshd->shqd', texp.astype(jnp.bfloat16).astype(jnp.float32), tv, precision=high)
    tmix = (tmix / ttotal[..., None]).astype(jnp.bfloat16)
    tmix = jnp.transpose(tmix, (2, 0, 1, 3)).reshape(TOKENS, SAMPLES, C_TOKEN)
    token_out = (state.astype(jnp.float32) + project(tmix, w_out)).astype(jnp.bfloat16)
    return (atom_out, token_out)
```

```python
import jax
import jax.numpy as jnp
from jax import lax
from jax.sharding import PartitionSpec as P

ATOM_HEADS = 4
QBLOCK = 32
KWIN = 128
SHIFT = 16
TOKEN_HEADS = 16


def layer_norm(values):
    values = values.astype(jnp.float32)
    mean = jnp.mean(values, axis=-1, keepdims=True)
    var = jnp.mean((values - mean) ** 2, axis=-1, keepdims=True)
    return (values - mean) / jnp.sqrt(var + 1e-05)


def project(values, weight):
    return jnp.einsum("asc,cd->asd", values, weight, preferred_element_type=jnp.float32)


def shifted(block, axis, step):
    count = lax.axis_size(axis)
    route = [(i, i + step) for i in range(count) if 0 <= i + step < count]
    return lax.ppermute(block, axis, route)


def on_device(
    atom_feat,
    window_shift,
    atom_token,
    token_in,
    pair,
    key_mask,
    w_atom_query,
    w_atom_key,
    w_atom_value,
    w_atom_out,
    w_to_token,
    w_query,
    w_key,
    w_value,
    w_out,
    w_bias,
):
    high = lax.Precision.HIGHEST
    atom_dev, samples, width = atom_feat.shape
    tok_dev = token_in.shape[0]
    tok_width = token_in.shape[2]
    devices = lax.axis_size("row")
    rank = lax.axis_index("row")
    atom_base = rank * atom_dev
    total_atoms = atom_dev * devices
    margin = (KWIN - QBLOCK) // 2
    low_rows = margin + SHIFT
    span = KWIN + 2 * SHIFT
    high_rows = span - low_rows
    blocks = atom_dev // QBLOCK + 1

    shift_row = jnp.broadcast_to(
        window_shift[0].astype(jnp.bfloat16), (1, samples, width)
    )
    low = shifted(atom_feat[atom_dev - low_rows :], "row", 1)
    upper = shifted(
        jnp.concatenate([atom_feat[:high_rows], shift_row], axis=0), "row", -1
    )
    next_shift = upper[high_rows, 0, 0].astype(jnp.int32)
    upper = upper[:high_rows]

    w_qkv = jnp.concatenate([w_atom_query, w_atom_key, w_atom_value], axis=1)
    w_kv = jnp.concatenate([w_atom_key, w_atom_value], axis=1)
    own_p = project(layer_norm(atom_feat).astype(jnp.bfloat16), w_qkv).astype(jnp.bfloat16)
    low_p = project(layer_norm(low).astype(jnp.bfloat16), w_kv).astype(jnp.bfloat16)
    high_p = project(layer_norm(upper).astype(jnp.bfloat16), w_qkv).astype(jnp.bfloat16)
    query = jnp.concatenate([own_p[..., :width], high_p[:QBLOCK, :, :width]], axis=0)
    kv = jnp.concatenate([low_p, own_p[..., width:], high_p[..., width:]], axis=0)

    head_dim = width // ATOM_HEADS
    shifts = jnp.concatenate([window_shift, next_shift[None]], axis=0)
    kwin = jnp.stack([kv[j * QBLOCK : j * QBLOCK + span] for j in range(blocks)], axis=0)
    position = jnp.arange(span, dtype=jnp.int32)
    first = (SHIFT + shifts)[:, None]
    absolute = (
        atom_base
        + jnp.arange(blocks, dtype=jnp.int32)[:, None] * QBLOCK
        - low_rows
        + position[None, :]
    )
    valid = (
        (position[None, :] >= first)
        & (position[None, :] < first + KWIN)
        & (absolute >= 0)
        & (absolute < total_atoms)
    )
    qblock = query.reshape(blocks, QBLOCK, samples, ATOM_HEADS, head_dim)
    kblock = kwin[..., :width].reshape(blocks, span, samples, ATOM_HEADS, head_dim)
    vblock = kwin[..., width:].reshape(blocks, span, samples, ATOM_HEADS, head_dim)
    scores = jnp.einsum(
        "bqshd,bkshd->bshqk", qblock, kblock, preferred_element_type=jnp.float32
    ) / jnp.sqrt(jnp.float32(head_dim))
    keep = valid[:, None, None, None, :]
    scores = jnp.where(keep, scores, -1e30)
    top = jnp.max(scores, axis=-1, keepdims=True)
    expo = jnp.where(keep, jnp.exp(scores - top), 0.0)
    total = jnp.sum(expo, axis=-1)
    mixed = jnp.einsum(
        "bshqk,bkshd->bqshd", expo.astype(jnp.bfloat16), vblock, preferred_element_type=jnp.float32
    )
    mixed = mixed / jnp.transpose(total, (0, 3, 1, 2))[..., None]
    rows = blocks * QBLOCK
    mixed = mixed.astype(jnp.bfloat16).reshape(rows, samples, width)
    feat = jnp.concatenate([atom_feat, upper[:QBLOCK]], axis=0)
    atom_rows = (feat.astype(jnp.float32) + project(mixed, w_atom_out)).astype(jnp.bfloat16)
    atom_out = atom_rows[:atom_dev]

    own_ids = rank * tok_dev + jnp.arange(tok_dev, dtype=jnp.int32)
    row_ids = lax.dynamic_slice_in_dim(
        jnp.concatenate([atom_token, jnp.full((QBLOCK,), -1, jnp.int32)]), atom_base, rows
    )
    hidden = jax.nn.relu(project(atom_rows, w_to_token))
    onehot = (own_ids[:, None] == row_ids[None, :]).astype(jnp.float32)
    counts = jnp.sum(onehot, axis=1)
    sums = jnp.einsum("ta,asd->tsd", onehot, hidden, precision=high)
    state = (token_in.astype(jnp.float32) + sums / counts[:, None, None]).astype(jnp.bfloat16)

    tdim = tok_width // TOKEN_HEADS
    tq = project(layer_norm(state).astype(jnp.bfloat16), w_query).astype(jnp.bfloat16)
    tq = tq.reshape(tok_dev, samples, TOKEN_HEADS, tdim)
    bias = jnp.einsum("qkc,ch->hqk", pair, w_bias, preferred_element_type=jnp.float32)
    scale = 1.0 / jnp.sqrt(jnp.float32(tdim))

    every = lax.all_gather(state, "row", axis=0, tiled=True)
    count = every.shape[0]
    tkv = project(layer_norm(every).astype(jnp.bfloat16), jnp.concatenate([w_key, w_value], axis=1))
    tkv = tkv.astype(jnp.bfloat16)
    kheads = tkv[..., :tok_width].reshape(count, samples, TOKEN_HEADS, tdim)
    vheads = tkv[..., tok_width:].reshape(count, samples, TOKEN_HEADS, tdim)
    flags = (key_mask > 0)[None, None, None, :]
    score = (
        jnp.einsum("qshd,kshd->shqk", tq, kheads, preferred_element_type=jnp.float32) * scale
        + bias[None]
    )
    score = jnp.where(flags, score, -1e30)
    peak = jnp.max(score, axis=-1)
    expo_t = jnp.where(flags, jnp.exp(score - peak[..., None]), 0.0)
    denom = jnp.sum(expo_t, axis=-1)
    accum = jnp.einsum(
        "shqk,kshd->shqd", expo_t.astype(jnp.bfloat16), vheads, preferred_element_type=jnp.float32
    )
    tmix = (accum / denom[..., None]).astype(jnp.bfloat16)
    tmix = jnp.transpose(tmix, (2, 0, 1, 3)).reshape(tok_dev, samples, tok_width)
    token_out = (state.astype(jnp.float32) + project(tmix, w_out)).astype(jnp.bfloat16)
    return (atom_out, token_out)


def solution(mesh):
    return jax.shard_map(
        on_device,
        mesh=mesh,
        in_specs=(
            P(("groups", "row"), None, None),
            P(("groups", "row")),
            P("groups"),
            P(("groups", "row"), None, None),
            P(("groups", "row"), None, None),
            P("groups"),
            P(),
            P(),
            P(),
            P(),
            P(),
            P(),
            P(),
            P(),
            P(),
            P(),
        ),
        out_specs=(P(("groups", "row"), None, None), P(("groups", "row"), None, None)),
        check_vma=False,
    )
```

```python
import functools
import math

import jax
import jax.numpy as jnp
from jax import lax
from jax.experimental import pallas as pl
from jax.experimental.pallas import tpu as pltpu
from jax.sharding import PartitionSpec as P

ATOM_HEADS = 4
QBLOCK = 32
KWIN = 128
SHIFT = 16
TOKEN_HEADS = 16


def layer_norm(values):
    values = values.astype(jnp.float32)
    mean = jnp.mean(values, axis=-1, keepdims=True)
    var = jnp.mean((values - mean) ** 2, axis=-1, keepdims=True)
    return (values - mean) / jnp.sqrt(var + 1e-05)


def project(values, weight):
    return jnp.einsum("asc,cd->asd", values, weight, preferred_element_type=jnp.float32)


def shifted(block, axis, step):
    count = lax.axis_size(axis)
    route = [(i, i + step) for i in range(count) if 0 <= i + step < count]
    return lax.ppermute(block, axis, route)


def atom_kernel(
    ext_ref,
    keep_ref,
    wq_ref,
    wk_ref,
    wv_ref,
    wo_ref,
    wt_ref,
    onehot_ref,
    count_ref,
    token_ref,
    atom_ref,
    state_ref,
    *,
    atom_dev,
    blocks,
    low_rows,
    span,
    head_dim,
):
    f32, bf16 = jnp.float32, jnp.bfloat16
    samples, _, width = ext_ref.shape
    rows = blocks * QBLOCK
    lane = lax.broadcasted_iota(jnp.int32, (1, width), 1) // head_dim
    head_masks = [(lane == h).astype(f32) for h in range(ATOM_HEADS)]
    root = jnp.float32(math.sqrt(head_dim))
    onehot = onehot_ref[...].astype(bf16)
    counts = count_ref[...]
    for s in range(samples):
        x = ext_ref[s].astype(f32)
        mean = jnp.mean(x, axis=-1, keepdims=True)
        var = jnp.mean((x - mean) ** 2, axis=-1, keepdims=True)
        xn = ((x - mean) / jnp.sqrt(var + 1e-05)).astype(bf16)
        q = jnp.dot(xn[low_rows : low_rows + rows], wq_ref[...], preferred_element_type=f32)
        q = q.astype(bf16)
        k = jnp.dot(xn, wk_ref[...], preferred_element_type=f32).astype(bf16)
        v = jnp.dot(xn, wv_ref[...], preferred_element_type=f32).astype(bf16)
        pieces = []
        for j in range(blocks):
            qj = q[j * QBLOCK : (j + 1) * QBLOCK]
            kj = k[j * QBLOCK : j * QBLOCK + span]
            vj = v[j * QBLOCK : j * QBLOCK + span]
            keep = keep_ref[j : j + 1, :] > 0.5
            acc = jnp.zeros((QBLOCK, width), f32)
            for h in range(ATOM_HEADS):
                qh = qj * head_masks[h].astype(bf16)
                sc = lax.dot_general(
                    qh, kj, (((1,), (1,)), ((), ())), preferred_element_type=f32
                ) / root
                sc = jnp.where(keep, sc, -1e30)
                top = jnp.max(sc, axis=-1, keepdims=True)
                e = jnp.where(keep, jnp.exp(sc - top), 0.0)
                tot = jnp.sum(e, axis=-1, keepdims=True)
                o = jnp.dot(e.astype(bf16), vj, preferred_element_type=f32)
                acc = acc + (o / tot) * head_masks[h]
            pieces.append(acc.astype(bf16))
        mixed = jnp.concatenate(pieces, axis=0)
        base = x[low_rows : low_rows + rows]
        out = (base + jnp.dot(mixed, wo_ref[...], preferred_element_type=f32)).astype(bf16)
        atom_ref[s] = out[:atom_dev]
        hidden = jnp.maximum(jnp.dot(out, wt_ref[...], preferred_element_type=f32), 0.0)
        top_part = hidden.astype(bf16)
        rest = hidden - top_part.astype(f32)
        mid_part = rest.astype(bf16)
        low_part = (rest - mid_part.astype(f32)).astype(bf16)
        sums = (
            jnp.dot(onehot, top_part, preferred_element_type=f32)
            + jnp.dot(onehot, mid_part, preferred_element_type=f32)
            + jnp.dot(onehot, low_part, preferred_element_type=f32)
        )
        state_ref[s] = (token_ref[s].astype(f32) + sums / counts).astype(bf16)


def on_device(
    atom_feat,
    window_shift,
    atom_token,
    token_in,
    pair,
    key_mask,
    w_atom_query,
    w_atom_key,
    w_atom_value,
    w_atom_out,
    w_to_token,
    w_query,
    w_key,
    w_value,
    w_out,
    w_bias,
):
    high = lax.Precision.HIGHEST
    atom_dev, samples, width = atom_feat.shape
    tok_dev = token_in.shape[0]
    tok_width = token_in.shape[2]
    devices = lax.axis_size("row")
    rank = lax.axis_index("row")
    atom_base = rank * atom_dev
    total_atoms = atom_dev * devices
    margin = (KWIN - QBLOCK) // 2
    low_rows = margin + SHIFT
    span = KWIN + 2 * SHIFT
    high_rows = span - low_rows
    blocks = atom_dev // QBLOCK + 1

    shift_row = jnp.broadcast_to(
        window_shift[0].astype(jnp.bfloat16), (1, samples, width)
    )
    low = shifted(atom_feat[atom_dev - low_rows :], "row", 1)
    upper = shifted(
        jnp.concatenate([atom_feat[:high_rows], shift_row], axis=0), "row", -1
    )
    next_shift = upper[high_rows, 0, 0].astype(jnp.int32)
    upper = upper[:high_rows]

    head_dim = width // ATOM_HEADS
    shifts = jnp.concatenate([window_shift, next_shift[None]], axis=0)
    position = jnp.arange(span, dtype=jnp.int32)
    first = (SHIFT + shifts)[:, None]
    absolute = (
        atom_base
        + jnp.arange(blocks, dtype=jnp.int32)[:, None] * QBLOCK
        - low_rows
        + position[None, :]
    )
    valid = (
        (position[None, :] >= first)
        & (position[None, :] < first + KWIN)
        & (absolute >= 0)
        & (absolute < total_atoms)
    )
    rows = blocks * QBLOCK
    own_ids = rank * tok_dev + jnp.arange(tok_dev, dtype=jnp.int32)
    row_ids = lax.dynamic_slice_in_dim(
        jnp.concatenate([atom_token, jnp.full((QBLOCK,), -1, jnp.int32)]), atom_base, rows
    )
    onehot = (own_ids[:, None] == row_ids[None, :]).astype(jnp.float32)
    counts = jnp.sum(onehot, axis=1, keepdims=True)
    extended = jnp.transpose(jnp.concatenate([low, atom_feat, upper], axis=0), (1, 0, 2))
    kernel = functools.partial(
        atom_kernel,
        atom_dev=atom_dev,
        blocks=blocks,
        low_rows=low_rows,
        span=span,
        head_dim=head_dim,
    )
    vmem = pl.BlockSpec(memory_space=pltpu.VMEM)
    ext_rows = extended.shape[1]
    flops = 2 * samples * (
        ext_rows * width * 3 * width
        + rows * width * (width + tok_width)
        + blocks * ATOM_HEADS * QBLOCK * span * width * 2
        + 3 * tok_dev * rows * tok_width
    )
    atom_t, state_t = pl.pallas_call(
        kernel,
        out_shape=(
            jax.ShapeDtypeStruct((samples, atom_dev, width), jnp.bfloat16),
            jax.ShapeDtypeStruct((samples, tok_dev, tok_width), jnp.bfloat16),
        ),
        in_specs=[vmem] * 10,
        out_specs=(vmem, vmem),
        cost_estimate=pl.CostEstimate(
            flops=flops,
            transcendentals=samples * blocks * ATOM_HEADS * QBLOCK * span,
            bytes_accessed=2 * (ext_rows + atom_dev) * samples * width
            + 2 * width * (3 * width + width + tok_width)
            + 4 * samples * tok_dev * tok_width,
        ),
    )(
        extended,
        valid.astype(jnp.float32),
        w_atom_query,
        w_atom_key,
        w_atom_value,
        w_atom_out,
        w_to_token,
        onehot,
        counts,
        jnp.transpose(token_in, (1, 0, 2)),
    )
    atom_out = jnp.transpose(atom_t, (1, 0, 2))
    state = jnp.transpose(state_t, (1, 0, 2))

    tdim = tok_width // TOKEN_HEADS
    tq = project(layer_norm(state).astype(jnp.bfloat16), w_query).astype(jnp.bfloat16)
    tq = tq.reshape(tok_dev, samples, TOKEN_HEADS, tdim)
    bias = jnp.einsum("qkc,ch->hqk", pair, w_bias, preferred_element_type=jnp.float32)
    scale = 1.0 / jnp.sqrt(jnp.float32(tdim))

    every = lax.all_gather(state, "row", axis=0, tiled=True)
    count = every.shape[0]
    tkv = project(layer_norm(every).astype(jnp.bfloat16), jnp.concatenate([w_key, w_value], axis=1))
    tkv = tkv.astype(jnp.bfloat16)
    kheads = tkv[..., :tok_width].reshape(count, samples, TOKEN_HEADS, tdim)
    vheads = tkv[..., tok_width:].reshape(count, samples, TOKEN_HEADS, tdim)
    flags = (key_mask > 0)[None, None, None, :]
    score = (
        jnp.einsum("qshd,kshd->shqk", tq, kheads, preferred_element_type=jnp.float32) * scale
        + bias[None]
    )
    score = jnp.where(flags, score, -1e30)
    peak = jnp.max(score, axis=-1)
    expo_t = jnp.where(flags, jnp.exp(score - peak[..., None]), 0.0)
    denom = jnp.sum(expo_t, axis=-1)
    accum = jnp.einsum(
        "shqk,kshd->shqd", expo_t.astype(jnp.bfloat16), vheads, preferred_element_type=jnp.float32
    )
    tmix = (accum / denom[..., None]).astype(jnp.bfloat16)
    tmix = jnp.transpose(tmix, (2, 0, 1, 3)).reshape(tok_dev, samples, tok_width)
    token_out = (state.astype(jnp.float32) + project(tmix, w_out)).astype(jnp.bfloat16)
    return (atom_out, token_out)


def solution(mesh):
    return jax.shard_map(
        on_device,
        mesh=mesh,
        in_specs=(
            P(("groups", "row"), None, None),
            P(("groups", "row")),
            P("groups"),
            P(("groups", "row"), None, None),
            P(("groups", "row"), None, None),
            P("groups"),
            P(),
            P(),
            P(),
            P(),
            P(),
            P(),
            P(),
            P(),
            P(),
            P(),
        ),
        out_specs=(P(("groups", "row"), None, None), P(("groups", "row"), None, None)),
        check_vma=False,
    )
```

```python
import functools
import math

import jax
import jax.numpy as jnp
from jax import lax
from jax.experimental import pallas as pl
from jax.experimental.pallas import tpu as pltpu
from jax.sharding import PartitionSpec as P

ATOM_HEADS = 4
QBLOCK = 32
KWIN = 128
SHIFT = 16
TOKEN_HEADS = 16


def layer_norm(values):
    values = values.astype(jnp.float32)
    mean = jnp.mean(values, axis=-1, keepdims=True)
    var = jnp.mean((values - mean) ** 2, axis=-1, keepdims=True)
    return (values - mean) / jnp.sqrt(var + 1e-05)


def project(values, weight):
    return jnp.einsum("asc,cd->asd", values, weight, preferred_element_type=jnp.float32)


def shifted(block, axis, step):
    count = lax.axis_size(axis)
    route = [(i, i + step) for i in range(count) if 0 <= i + step < count]
    return lax.ppermute(block, axis, route)


def atom_kernel(
    ext_ref,
    bounds_ref,
    wq_ref,
    wk_ref,
    wv_ref,
    wo_ref,
    wt_ref,
    row_ids_ref,
    own_ids_ref,
    token_ref,
    atom_ref,
    state_ref,
    *,
    atom_dev,
    rows,
    low_rows,
    head_dim,
):
    f32, bf16 = jnp.float32, jnp.bfloat16
    samples, ext_rows, width = ext_ref.shape
    lane = lax.broadcasted_iota(jnp.int32, (1, width), 1) // head_dim
    head_masks = [(lane == h).astype(f32) for h in range(ATOM_HEADS)]
    root = jnp.float32(math.sqrt(head_dim))
    column = lax.broadcasted_iota(jnp.int32, (rows, ext_rows), 1)
    keep = (column >= bounds_ref[:, 0:1]) & (column < bounds_ref[:, 1:2])
    onehot = (own_ids_ref[...] == row_ids_ref[...]).astype(f32)
    counts = jnp.sum(onehot, axis=1, keepdims=True)
    onehot = onehot.astype(bf16)
    for s in range(samples):
        x = ext_ref[s].astype(f32)
        mean = jnp.mean(x, axis=-1, keepdims=True)
        var = jnp.mean((x - mean) ** 2, axis=-1, keepdims=True)
        xn = ((x - mean) / jnp.sqrt(var + 1e-05)).astype(bf16)
        q = jnp.dot(xn[low_rows : low_rows + rows], wq_ref[...], preferred_element_type=f32)
        q = q.astype(bf16)
        k = jnp.dot(xn, wk_ref[...], preferred_element_type=f32).astype(bf16)
        v = jnp.dot(xn, wv_ref[...], preferred_element_type=f32).astype(bf16)
        acc = jnp.zeros((rows, width), f32)
        for h in range(ATOM_HEADS):
            qh = q * head_masks[h].astype(bf16)
            sc = lax.dot_general(
                qh, k, (((1,), (1,)), ((), ())), preferred_element_type=f32
            ) / root
            sc = jnp.where(keep, sc, -1e30)
            top = jnp.max(sc, axis=-1, keepdims=True)
            e = jnp.where(keep, jnp.exp(sc - top), 0.0)
            tot = jnp.sum(e, axis=-1, keepdims=True)
            o = jnp.dot(e.astype(bf16), v, preferred_element_type=f32)
            acc = acc + (o / tot) * head_masks[h]
        mixed = acc.astype(bf16)
        base = x[low_rows : low_rows + rows]
        out = (base + jnp.dot(mixed, wo_ref[...], preferred_element_type=f32)).astype(bf16)
        atom_ref[s] = out[:atom_dev]
        hidden = jnp.maximum(jnp.dot(out, wt_ref[...], preferred_element_type=f32), 0.0)
        top_part = hidden.astype(bf16)
        rest = hidden - top_part.astype(f32)
        mid_part = rest.astype(bf16)
        low_part = (rest - mid_part.astype(f32)).astype(bf16)
        sums = (
            jnp.dot(onehot, top_part, preferred_element_type=f32)
            + jnp.dot(onehot, mid_part, preferred_element_type=f32)
            + jnp.dot(onehot, low_part, preferred_element_type=f32)
        )
        state_ref[s] = (token_ref[s].astype(f32) + sums / counts).astype(bf16)


def on_device(
    atom_feat,
    window_shift,
    atom_token,
    token_in,
    pair,
    key_mask,
    w_atom_query,
    w_atom_key,
    w_atom_value,
    w_atom_out,
    w_to_token,
    w_query,
    w_key,
    w_value,
    w_out,
    w_bias,
):
    high = lax.Precision.HIGHEST
    atom_dev, samples, width = atom_feat.shape
    tok_dev = token_in.shape[0]
    tok_width = token_in.shape[2]
    devices = lax.axis_size("row")
    rank = lax.axis_index("row")
    atom_base = rank * atom_dev
    total_atoms = atom_dev * devices
    margin = (KWIN - QBLOCK) // 2
    low_rows = margin + SHIFT
    span = KWIN + 2 * SHIFT
    high_rows = span - low_rows
    blocks = atom_dev // QBLOCK + 1

    shift_row = jnp.broadcast_to(
        window_shift[0].astype(jnp.bfloat16), (1, samples, width)
    )
    low = shifted(atom_feat[atom_dev - low_rows :], "row", 1)
    upper = shifted(
        jnp.concatenate([atom_feat[:high_rows], shift_row], axis=0), "row", -1
    )
    next_shift = upper[high_rows, 0, 0].astype(jnp.int32)
    upper = upper[:high_rows]

    head_dim = width // ATOM_HEADS
    shifts = jnp.concatenate([window_shift, next_shift[None]], axis=0)
    rows = blocks * QBLOCK
    ext_rows = low_rows + atom_dev + high_rows
    row_block = jnp.arange(rows, dtype=jnp.int32) // QBLOCK
    first = row_block * QBLOCK + SHIFT + jnp.repeat(shifts, QBLOCK)
    bounds = jnp.stack(
        [
            jnp.maximum(first, low_rows - atom_base),
            jnp.minimum(first + KWIN, total_atoms - atom_base + low_rows),
        ],
        axis=1,
    )
    own_ids = rank * tok_dev + jnp.arange(tok_dev, dtype=jnp.int32)
    row_ids = lax.dynamic_slice_in_dim(
        jnp.concatenate([atom_token, jnp.full((QBLOCK,), -1, jnp.int32)]), atom_base, rows
    )
    extended = jnp.transpose(jnp.concatenate([low, atom_feat, upper], axis=0), (1, 0, 2))
    kernel = functools.partial(
        atom_kernel, atom_dev=atom_dev, rows=rows, low_rows=low_rows, head_dim=head_dim
    )
    vmem = pl.BlockSpec(memory_space=pltpu.VMEM)
    flops = 2 * samples * (
        ext_rows * width * 3 * width
        + rows * width * (width + tok_width)
        + ATOM_HEADS * rows * ext_rows * width * 2
        + 3 * tok_dev * rows * tok_width
    )
    atom_t, state_t = pl.pallas_call(
        kernel,
        out_shape=(
            jax.ShapeDtypeStruct((samples, atom_dev, width), jnp.bfloat16),
            jax.ShapeDtypeStruct((samples, tok_dev, tok_width), jnp.bfloat16),
        ),
        in_specs=[vmem] * 10,
        out_specs=(vmem, vmem),
        cost_estimate=pl.CostEstimate(
            flops=flops,
            transcendentals=samples * ATOM_HEADS * rows * ext_rows,
            bytes_accessed=2 * (ext_rows + atom_dev) * samples * width
            + 2 * width * (3 * width + width + tok_width)
            + 4 * samples * tok_dev * tok_width,
        ),
    )(
        extended,
        bounds,
        w_atom_query,
        w_atom_key,
        w_atom_value,
        w_atom_out,
        w_to_token,
        row_ids[None, :],
        own_ids[:, None],
        jnp.transpose(token_in, (1, 0, 2)),
    )
    atom_out = jnp.transpose(atom_t, (1, 0, 2))
    state = jnp.transpose(state_t, (1, 0, 2))

    tdim = tok_width // TOKEN_HEADS
    tq = project(layer_norm(state).astype(jnp.bfloat16), w_query).astype(jnp.bfloat16)
    tq = tq.reshape(tok_dev, samples, TOKEN_HEADS, tdim)
    bias = jnp.einsum("qkc,ch->hqk", pair, w_bias, preferred_element_type=jnp.float32)
    scale = 1.0 / jnp.sqrt(jnp.float32(tdim))

    every = lax.all_gather(state, "row", axis=0, tiled=True)
    count = every.shape[0]
    tkv = project(layer_norm(every).astype(jnp.bfloat16), jnp.concatenate([w_key, w_value], axis=1))
    tkv = tkv.astype(jnp.bfloat16)
    kheads = tkv[..., :tok_width].reshape(count, samples, TOKEN_HEADS, tdim)
    vheads = tkv[..., tok_width:].reshape(count, samples, TOKEN_HEADS, tdim)
    flags = (key_mask > 0)[None, None, None, :]
    score = (
        jnp.einsum("qshd,kshd->shqk", tq, kheads, preferred_element_type=jnp.float32) * scale
        + bias[None]
    )
    score = jnp.where(flags, score, -1e30)
    peak = jnp.max(score, axis=-1)
    expo_t = jnp.where(flags, jnp.exp(score - peak[..., None]), 0.0)
    denom = jnp.sum(expo_t, axis=-1)
    accum = jnp.einsum(
        "shqk,kshd->shqd", expo_t.astype(jnp.bfloat16), vheads, preferred_element_type=jnp.float32
    )
    tmix = (accum / denom[..., None]).astype(jnp.bfloat16)
    tmix = jnp.transpose(tmix, (2, 0, 1, 3)).reshape(tok_dev, samples, tok_width)
    token_out = (state.astype(jnp.float32) + project(tmix, w_out)).astype(jnp.bfloat16)
    return (atom_out, token_out)


def solution(mesh):
    return jax.shard_map(
        on_device,
        mesh=mesh,
        in_specs=(
            P(("groups", "row"), None, None),
            P(("groups", "row")),
            P("groups"),
            P(("groups", "row"), None, None),
            P(("groups", "row"), None, None),
            P("groups"),
            P(),
            P(),
            P(),
            P(),
            P(),
            P(),
            P(),
            P(),
            P(),
            P(),
        ),
        out_specs=(P(("groups", "row"), None, None), P(("groups", "row"), None, None)),
        check_vma=False,
    )
```

```python
import functools
import math

import jax
import jax.numpy as jnp
from jax import lax
from jax.experimental import pallas as pl
from jax.experimental.pallas import tpu as pltpu
from jax.sharding import PartitionSpec as P

ATOM_HEADS = 4
QBLOCK = 32
KWIN = 128
SHIFT = 16
TOKEN_HEADS = 16


def layer_norm(values):
    values = values.astype(jnp.float32)
    mean = jnp.mean(values, axis=-1, keepdims=True)
    var = jnp.mean((values - mean) ** 2, axis=-1, keepdims=True)
    return (values - mean) / jnp.sqrt(var + 1e-05)


def project(values, weight):
    return jnp.einsum("asc,cd->asd", values, weight, preferred_element_type=jnp.float32)


def shifted(block, axis, step):
    count = lax.axis_size(axis)
    route = [(i, i + step) for i in range(count) if 0 <= i + step < count]
    return lax.ppermute(block, axis, route)


def atom_kernel(
    ext_ref,
    bounds_ref,
    wq_ref,
    wk_ref,
    wv_ref,
    wo_ref,
    wt_ref,
    row_ids_ref,
    own_ids_ref,
    token_ref,
    atom_ref,
    state_ref,
    *,
    atom_dev,
    rows,
    low_rows,
    head_dim,
):
    f32, bf16 = jnp.float32, jnp.bfloat16
    samples, ext_rows, width = ext_ref.shape
    lane = lax.broadcasted_iota(jnp.int32, (1, width), 1) // head_dim
    head_masks = [(lane == h).astype(f32) for h in range(ATOM_HEADS)]
    root = jnp.float32(math.sqrt(head_dim))
    column = lax.broadcasted_iota(jnp.int32, (rows, ext_rows), 1)
    keep = (column >= bounds_ref[:, 0:1]) & (column < bounds_ref[:, 1:2])
    onehot = (own_ids_ref[...] == row_ids_ref[...]).astype(f32)
    counts = jnp.sum(onehot, axis=1, keepdims=True)
    onehot = onehot.astype(bf16)
    for s in range(samples):
        x = ext_ref[s].astype(f32)
        mean = jnp.mean(x, axis=-1, keepdims=True)
        var = jnp.mean((x - mean) ** 2, axis=-1, keepdims=True)
        xn = ((x - mean) / jnp.sqrt(var + 1e-05)).astype(bf16)
        q = jnp.dot(xn[low_rows : low_rows + rows], wq_ref[...], preferred_element_type=f32)
        q = q.astype(bf16)
        k = jnp.dot(xn, wk_ref[...], preferred_element_type=f32).astype(bf16)
        v = jnp.dot(xn, wv_ref[...], preferred_element_type=f32).astype(bf16)
        acc = jnp.zeros((rows, width), f32)
        for h in range(ATOM_HEADS):
            qh = q * head_masks[h].astype(bf16)
            sc = lax.dot_general(
                qh, k, (((1,), (1,)), ((), ())), preferred_element_type=f32
            ) / root
            sc = jnp.where(keep, sc, -1e30)
            top = jnp.max(sc, axis=-1, keepdims=True)
            e = jnp.where(keep, jnp.exp(sc - top), 0.0)
            tot = jnp.sum(e, axis=-1, keepdims=True)
            o = jnp.dot(e.astype(bf16), v, preferred_element_type=f32)
            acc = acc + (o / tot) * head_masks[h]
        mixed = acc.astype(bf16)
        base = x[low_rows : low_rows + rows]
        out = (base + jnp.dot(mixed, wo_ref[...], preferred_element_type=f32)).astype(bf16)
        atom_ref[s] = out[:atom_dev]
        hidden = jnp.maximum(jnp.dot(out, wt_ref[...], preferred_element_type=f32), 0.0)
        top_part = hidden.astype(bf16)
        rest = hidden - top_part.astype(f32)
        mid_part = rest.astype(bf16)
        low_part = (rest - mid_part.astype(f32)).astype(bf16)
        sums = (
            jnp.dot(onehot, top_part, preferred_element_type=f32)
            + jnp.dot(onehot, mid_part, preferred_element_type=f32)
            + jnp.dot(onehot, low_part, preferred_element_type=f32)
        )
        state_ref[s] = (token_ref[s].astype(f32) + sums / counts).astype(bf16)


def token_kernel(
    every_ref,
    own_ref,
    bias_ref,
    flags_ref,
    wq_ref,
    wk_ref,
    wv_ref,
    wo_ref,
    out_ref,
    *,
    heads,
):
    f32, bf16 = jnp.float32, jnp.bfloat16
    samples, tok_dev, width = own_ref.shape
    head_dim = width // heads
    lane = lax.broadcasted_iota(jnp.int32, (1, width), 1) // head_dim
    head_masks = [(lane == h).astype(f32) for h in range(heads)]
    root = jnp.float32(math.sqrt(head_dim))
    keep = flags_ref[...] > 0
    bias = bias_ref[...]

    def normed(x):
        mean = jnp.mean(x, axis=-1, keepdims=True)
        var = jnp.mean((x - mean) ** 2, axis=-1, keepdims=True)
        return ((x - mean) / jnp.sqrt(var + 1e-05)).astype(bf16)

    for s in range(samples):
        allx = normed(every_ref[s].astype(f32))
        own = own_ref[s].astype(f32)
        q = jnp.dot(normed(own), wq_ref[...], preferred_element_type=f32).astype(bf16)
        k = jnp.dot(allx, wk_ref[...], preferred_element_type=f32).astype(bf16)
        v = jnp.dot(allx, wv_ref[...], preferred_element_type=f32).astype(bf16)
        stacked = jnp.concatenate([q * head_masks[h].astype(bf16) for h in range(heads)], axis=0)
        sc = lax.dot_general(
            stacked, k, (((1,), (1,)), ((), ())), preferred_element_type=f32
        ) / root + bias
        sc = jnp.where(keep, sc, -1e30)
        top = jnp.max(sc, axis=-1, keepdims=True)
        e = jnp.where(keep, jnp.exp(sc - top), 0.0)
        tot = jnp.sum(e, axis=-1, keepdims=True)
        o = jnp.dot(e.astype(bf16), v, preferred_element_type=f32) / tot
        mix = o[0:tok_dev] * head_masks[0]
        for h in range(1, heads):
            mix = mix + o[h * tok_dev : (h + 1) * tok_dev] * head_masks[h]
        mix = mix.astype(bf16)
        out_ref[s] = (own + jnp.dot(mix, wo_ref[...], preferred_element_type=f32)).astype(bf16)


def on_device(
    atom_feat,
    window_shift,
    atom_token,
    token_in,
    pair,
    key_mask,
    w_atom_query,
    w_atom_key,
    w_atom_value,
    w_atom_out,
    w_to_token,
    w_query,
    w_key,
    w_value,
    w_out,
    w_bias,
):
    high = lax.Precision.HIGHEST
    atom_dev, samples, width = atom_feat.shape
    tok_dev = token_in.shape[0]
    tok_width = token_in.shape[2]
    devices = lax.axis_size("row")
    rank = lax.axis_index("row")
    atom_base = rank * atom_dev
    total_atoms = atom_dev * devices
    margin = (KWIN - QBLOCK) // 2
    low_rows = margin + SHIFT
    span = KWIN + 2 * SHIFT
    high_rows = span - low_rows
    blocks = atom_dev // QBLOCK + 1

    shift_row = jnp.broadcast_to(
        window_shift[0].astype(jnp.bfloat16), (1, samples, width)
    )
    low = shifted(atom_feat[atom_dev - low_rows :], "row", 1)
    upper = shifted(
        jnp.concatenate([atom_feat[:high_rows], shift_row], axis=0), "row", -1
    )
    next_shift = upper[high_rows, 0, 0].astype(jnp.int32)
    upper = upper[:high_rows]

    head_dim = width // ATOM_HEADS
    shifts = jnp.concatenate([window_shift, next_shift[None]], axis=0)
    rows = blocks * QBLOCK
    ext_rows = low_rows + atom_dev + high_rows
    row_block = jnp.arange(rows, dtype=jnp.int32) // QBLOCK
    first = row_block * QBLOCK + SHIFT + jnp.repeat(shifts, QBLOCK)
    bounds = jnp.stack(
        [
            jnp.maximum(first, low_rows - atom_base),
            jnp.minimum(first + KWIN, total_atoms - atom_base + low_rows),
        ],
        axis=1,
    )
    own_ids = rank * tok_dev + jnp.arange(tok_dev, dtype=jnp.int32)
    row_ids = lax.dynamic_slice_in_dim(
        jnp.concatenate([atom_token, jnp.full((QBLOCK,), -1, jnp.int32)]), atom_base, rows
    )
    extended = jnp.transpose(jnp.concatenate([low, atom_feat, upper], axis=0), (1, 0, 2))
    kernel = functools.partial(
        atom_kernel, atom_dev=atom_dev, rows=rows, low_rows=low_rows, head_dim=head_dim
    )
    vmem = pl.BlockSpec(memory_space=pltpu.VMEM)
    flops = 2 * samples * (
        ext_rows * width * 3 * width
        + rows * width * (width + tok_width)
        + ATOM_HEADS * rows * ext_rows * width * 2
        + 3 * tok_dev * rows * tok_width
    )
    atom_t, state_t = pl.pallas_call(
        kernel,
        out_shape=(
            jax.ShapeDtypeStruct((samples, atom_dev, width), jnp.bfloat16),
            jax.ShapeDtypeStruct((samples, tok_dev, tok_width), jnp.bfloat16),
        ),
        in_specs=[vmem] * 10,
        out_specs=(vmem, vmem),
        cost_estimate=pl.CostEstimate(
            flops=flops,
            transcendentals=samples * ATOM_HEADS * rows * ext_rows,
            bytes_accessed=2 * (ext_rows + atom_dev) * samples * width
            + 2 * width * (3 * width + width + tok_width)
            + 4 * samples * tok_dev * tok_width,
        ),
    )(
        extended,
        bounds,
        w_atom_query,
        w_atom_key,
        w_atom_value,
        w_atom_out,
        w_to_token,
        row_ids[None, :],
        own_ids[:, None],
        jnp.transpose(token_in, (1, 0, 2)),
    )
    atom_out = jnp.transpose(atom_t, (1, 0, 2))

    bias = jnp.einsum("qkc,ch->hqk", pair, w_bias, preferred_element_type=jnp.float32)
    every = lax.all_gather(state_t, "row", axis=1, tiled=True)
    count = every.shape[1]
    token_t = pl.pallas_call(
        functools.partial(token_kernel, heads=TOKEN_HEADS),
        out_shape=jax.ShapeDtypeStruct((samples, tok_dev, tok_width), jnp.bfloat16),
        in_specs=[vmem] * 8,
        out_specs=vmem,
        cost_estimate=pl.CostEstimate(
            flops=2 * samples * tok_width * (
                2 * count * tok_width + 2 * tok_dev * tok_width + 2 * TOKEN_HEADS * tok_dev * count
            ),
            transcendentals=samples * TOKEN_HEADS * tok_dev * count,
            bytes_accessed=2 * 4 * tok_width * tok_width
            + 2 * samples * (count + 2 * tok_dev) * tok_width
            + 4 * TOKEN_HEADS * tok_dev * count,
        ),
    )(
        every,
        state_t,
        bias.reshape(TOKEN_HEADS * tok_dev, count),
        key_mask[None, :],
        w_query,
        w_key,
        w_value,
        w_out,
    )
    token_out = jnp.transpose(token_t, (1, 0, 2))
    return (atom_out, token_out)


def solution(mesh):
    return jax.shard_map(
        on_device,
        mesh=mesh,
        in_specs=(
            P(("groups", "row"), None, None),
            P(("groups", "row")),
            P("groups"),
            P(("groups", "row"), None, None),
            P(("groups", "row"), None, None),
            P("groups"),
            P(),
            P(),
            P(),
            P(),
            P(),
            P(),
            P(),
            P(),
            P(),
            P(),
        ),
        out_specs=(P(("groups", "row"), None, None), P(("groups", "row"), None, None)),
        check_vma=False,
    )
```

```python
import functools
import math

import jax
import jax.numpy as jnp
from jax import lax
from jax.experimental import pallas as pl
from jax.experimental.pallas import tpu as pltpu
from jax.sharding import PartitionSpec as P

ATOM_HEADS = 4
QBLOCK = 32
KWIN = 128
SHIFT = 16
TOKEN_HEADS = 16


def layer_norm(values):
    values = values.astype(jnp.float32)
    mean = jnp.mean(values, axis=-1, keepdims=True)
    var = jnp.mean((values - mean) ** 2, axis=-1, keepdims=True)
    return (values - mean) / jnp.sqrt(var + 1e-05)


def project(values, weight):
    return jnp.einsum("asc,cd->asd", values, weight, preferred_element_type=jnp.float32)


def shifted(block, axis, step):
    count = lax.axis_size(axis)
    route = [(i, i + step) for i in range(count) if 0 <= i + step < count]
    return lax.ppermute(block, axis, route)


def atom_kernel(
    own_ref,
    low_ref,
    upper_ref,
    bounds_ref,
    wq_ref,
    wk_ref,
    wv_ref,
    wo_ref,
    wt_ref,
    row_ids_ref,
    own_ids_ref,
    token_ref,
    atom_ref,
    state_ref,
    *,
    atom_dev,
    rows,
    low_rows,
    high_rows,
    head_dim,
):
    f32, bf16 = jnp.float32, jnp.bfloat16
    _, samples, width = own_ref.shape
    ext_rows = low_rows + atom_dev + high_rows
    lane = lax.broadcasted_iota(jnp.int32, (1, width), 1) // head_dim
    head_masks = [(lane == h).astype(f32) for h in range(ATOM_HEADS)]
    root = jnp.float32(math.sqrt(head_dim))
    column = lax.broadcasted_iota(jnp.int32, (rows, ext_rows), 1)
    keep = (column >= bounds_ref[:, 0:1]) & (column < bounds_ref[:, 1:2])
    onehot = (own_ids_ref[...] == row_ids_ref[...]).astype(f32)
    counts = jnp.sum(onehot, axis=1, keepdims=True)
    onehot = onehot.astype(bf16)
    for s in range(samples):
        x = jnp.concatenate(
            [low_ref[:, s, :], own_ref[:, s, :], upper_ref[0:high_rows, s, :]], axis=0
        ).astype(f32)
        mean = jnp.mean(x, axis=-1, keepdims=True)
        var = jnp.mean((x - mean) ** 2, axis=-1, keepdims=True)
        xn = ((x - mean) / jnp.sqrt(var + 1e-05)).astype(bf16)
        q = jnp.dot(xn[low_rows : low_rows + rows], wq_ref[...], preferred_element_type=f32)
        q = q.astype(bf16)
        k = jnp.dot(xn, wk_ref[...], preferred_element_type=f32).astype(bf16)
        v = jnp.dot(xn, wv_ref[...], preferred_element_type=f32).astype(bf16)
        acc = jnp.zeros((rows, width), f32)
        for h in range(ATOM_HEADS):
            qh = q * head_masks[h].astype(bf16)
            sc = lax.dot_general(
                qh, k, (((1,), (1,)), ((), ())), preferred_element_type=f32
            ) / root
            sc = jnp.where(keep, sc, -1e30)
            top = jnp.max(sc, axis=-1, keepdims=True)
            e = jnp.where(keep, jnp.exp(sc - top), 0.0)
            tot = jnp.sum(e, axis=-1, keepdims=True)
            o = jnp.dot(e.astype(bf16), v, preferred_element_type=f32)
            acc = acc + (o / tot) * head_masks[h]
        mixed = acc.astype(bf16)
        base = x[low_rows : low_rows + rows]
        out = (base + jnp.dot(mixed, wo_ref[...], preferred_element_type=f32)).astype(bf16)
        atom_ref[:, s, :] = out[:atom_dev]
        hidden = jnp.maximum(jnp.dot(out, wt_ref[...], preferred_element_type=f32), 0.0)
        top_part = hidden.astype(bf16)
        rest = hidden - top_part.astype(f32)
        mid_part = rest.astype(bf16)
        low_part = (rest - mid_part.astype(f32)).astype(bf16)
        sums = (
            jnp.dot(onehot, top_part, preferred_element_type=f32)
            + jnp.dot(onehot, mid_part, preferred_element_type=f32)
            + jnp.dot(onehot, low_part, preferred_element_type=f32)
        )
        state_ref[s] = (token_ref[:, s, :].astype(f32) + sums / counts).astype(bf16)


def token_kernel(
    every_ref,
    own_ref,
    bias_ref,
    flags_ref,
    wq_ref,
    wk_ref,
    wv_ref,
    wo_ref,
    out_ref,
    *,
    heads,
):
    f32, bf16 = jnp.float32, jnp.bfloat16
    samples, tok_dev, width = own_ref.shape
    head_dim = width // heads
    lane = lax.broadcasted_iota(jnp.int32, (1, width), 1) // head_dim
    head_masks = [(lane == h).astype(f32) for h in range(heads)]
    root = jnp.float32(math.sqrt(head_dim))
    keep = flags_ref[...] > 0
    bias = bias_ref[...]

    def normed(x):
        mean = jnp.mean(x, axis=-1, keepdims=True)
        var = jnp.mean((x - mean) ** 2, axis=-1, keepdims=True)
        return ((x - mean) / jnp.sqrt(var + 1e-05)).astype(bf16)

    for s in range(samples):
        allx = normed(every_ref[s].astype(f32))
        own = own_ref[s].astype(f32)
        q = jnp.dot(normed(own), wq_ref[...], preferred_element_type=f32).astype(bf16)
        k = jnp.dot(allx, wk_ref[...], preferred_element_type=f32).astype(bf16)
        v = jnp.dot(allx, wv_ref[...], preferred_element_type=f32).astype(bf16)
        stacked = jnp.concatenate([q * head_masks[h].astype(bf16) for h in range(heads)], axis=0)
        sc = lax.dot_general(
            stacked, k, (((1,), (1,)), ((), ())), preferred_element_type=f32
        ) / root + bias
        sc = jnp.where(keep, sc, -1e30)
        top = jnp.max(sc, axis=-1, keepdims=True)
        e = jnp.where(keep, jnp.exp(sc - top), 0.0)
        tot = jnp.sum(e, axis=-1, keepdims=True)
        o = jnp.dot(e.astype(bf16), v, preferred_element_type=f32) / tot
        mix = o[0:tok_dev] * head_masks[0]
        for h in range(1, heads):
            mix = mix + o[h * tok_dev : (h + 1) * tok_dev] * head_masks[h]
        mix = mix.astype(bf16)
        out_ref[:, s, :] = (own + jnp.dot(mix, wo_ref[...], preferred_element_type=f32)).astype(bf16)


def on_device(
    atom_feat,
    window_shift,
    atom_token,
    token_in,
    pair,
    key_mask,
    w_atom_query,
    w_atom_key,
    w_atom_value,
    w_atom_out,
    w_to_token,
    w_query,
    w_key,
    w_value,
    w_out,
    w_bias,
):
    high = lax.Precision.HIGHEST
    atom_dev, samples, width = atom_feat.shape
    tok_dev = token_in.shape[0]
    tok_width = token_in.shape[2]
    devices = lax.axis_size("row")
    rank = lax.axis_index("row")
    atom_base = rank * atom_dev
    total_atoms = atom_dev * devices
    margin = (KWIN - QBLOCK) // 2
    low_rows = margin + SHIFT
    span = KWIN + 2 * SHIFT
    high_rows = span - low_rows
    blocks = atom_dev // QBLOCK + 1

    shift_row = jnp.broadcast_to(
        window_shift[0].astype(jnp.bfloat16), (1, samples, width)
    )
    low = shifted(atom_feat[atom_dev - low_rows :], "row", 1)
    upper = shifted(
        jnp.concatenate([atom_feat[:high_rows], shift_row], axis=0), "row", -1
    )
    next_shift = upper[high_rows, 0, 0].astype(jnp.int32)

    head_dim = width // ATOM_HEADS
    shifts = jnp.concatenate([window_shift, next_shift[None]], axis=0)
    rows = blocks * QBLOCK
    ext_rows = low_rows + atom_dev + high_rows
    row_block = jnp.arange(rows, dtype=jnp.int32) // QBLOCK
    first = row_block * QBLOCK + SHIFT + jnp.repeat(shifts, QBLOCK)
    bounds = jnp.stack(
        [
            jnp.maximum(first, low_rows - atom_base),
            jnp.minimum(first + KWIN, total_atoms - atom_base + low_rows),
        ],
        axis=1,
    )
    own_ids = rank * tok_dev + jnp.arange(tok_dev, dtype=jnp.int32)
    row_ids = lax.dynamic_slice_in_dim(
        jnp.concatenate([atom_token, jnp.full((QBLOCK,), -1, jnp.int32)]), atom_base, rows
    )
    kernel = functools.partial(
        atom_kernel,
        atom_dev=atom_dev,
        rows=rows,
        low_rows=low_rows,
        high_rows=high_rows,
        head_dim=head_dim,
    )
    vmem = pl.BlockSpec(memory_space=pltpu.VMEM)
    flops = 2 * samples * (
        ext_rows * width * 3 * width
        + rows * width * (width + tok_width)
        + ATOM_HEADS * rows * ext_rows * width * 2
        + 3 * tok_dev * rows * tok_width
    )
    atom_out, state_t = pl.pallas_call(
        kernel,
        out_shape=(
            jax.ShapeDtypeStruct((atom_dev, samples, width), jnp.bfloat16),
            jax.ShapeDtypeStruct((samples, tok_dev, tok_width), jnp.bfloat16),
        ),
        in_specs=[vmem] * 12,
        out_specs=(vmem, vmem),
        cost_estimate=pl.CostEstimate(
            flops=flops,
            transcendentals=samples * ATOM_HEADS * rows * ext_rows,
            bytes_accessed=2 * (ext_rows + atom_dev) * samples * width
            + 2 * width * (3 * width + width + tok_width)
            + 4 * samples * tok_dev * tok_width,
        ),
    )(
        atom_feat,
        low,
        upper,
        bounds,
        w_atom_query,
        w_atom_key,
        w_atom_value,
        w_atom_out,
        w_to_token,
        row_ids[None, :],
        own_ids[:, None],
        token_in,
    )

    bias = jnp.einsum("qkc,ch->hqk", pair, w_bias, preferred_element_type=jnp.float32)
    every = lax.all_gather(state_t, "row", axis=1, tiled=True)
    count = every.shape[1]
    token_out = pl.pallas_call(
        functools.partial(token_kernel, heads=TOKEN_HEADS),
        out_shape=jax.ShapeDtypeStruct((tok_dev, samples, tok_width), jnp.bfloat16),
        in_specs=[vmem] * 8,
        out_specs=vmem,
        cost_estimate=pl.CostEstimate(
            flops=2 * samples * tok_width * (
                2 * count * tok_width + 2 * tok_dev * tok_width + 2 * TOKEN_HEADS * tok_dev * count
            ),
            transcendentals=samples * TOKEN_HEADS * tok_dev * count,
            bytes_accessed=2 * 4 * tok_width * tok_width
            + 2 * samples * (count + 2 * tok_dev) * tok_width
            + 4 * TOKEN_HEADS * tok_dev * count,
        ),
    )(
        every,
        state_t,
        bias.reshape(TOKEN_HEADS * tok_dev, count),
        key_mask[None, :],
        w_query,
        w_key,
        w_value,
        w_out,
    )
    return (atom_out, token_out)


def solution(mesh):
    return jax.shard_map(
        on_device,
        mesh=mesh,
        in_specs=(
            P(("groups", "row"), None, None),
            P(("groups", "row")),
            P("groups"),
            P(("groups", "row"), None, None),
            P(("groups", "row"), None, None),
            P("groups"),
            P(),
            P(),
            P(),
            P(),
            P(),
            P(),
            P(),
            P(),
            P(),
            P(),
        ),
        out_specs=(P(("groups", "row"), None, None), P(("groups", "row"), None, None)),
        check_vma=False,
    )
```

```python
import functools
import math

import jax
import jax.numpy as jnp
from jax import lax
from jax.experimental import pallas as pl
from jax.experimental.pallas import tpu as pltpu
from jax.sharding import PartitionSpec as P

ATOM_HEADS = 4
QBLOCK = 32
KWIN = 128
SHIFT = 16
TOKEN_HEADS = 16


def layer_norm(values):
    values = values.astype(jnp.float32)
    mean = jnp.mean(values, axis=-1, keepdims=True)
    var = jnp.mean((values - mean) ** 2, axis=-1, keepdims=True)
    return (values - mean) / jnp.sqrt(var + 1e-05)


def project(values, weight):
    return jnp.einsum("asc,cd->asd", values, weight, preferred_element_type=jnp.float32)


def shifted(block, axis, step):
    count = lax.axis_size(axis)
    route = [(i, i + step) for i in range(count) if 0 <= i + step < count]
    return lax.ppermute(block, axis, route)


def atom_kernel(
    own_ref,
    low_ref,
    upper_ref,
    shift_ref,
    wq_ref,
    wk_ref,
    wv_ref,
    wo_ref,
    wt_ref,
    ids_ref,
    token_ref,
    atom_ref,
    state_ref,
    *,
    atom_dev,
    rows,
    low_rows,
    high_rows,
    head_dim,
    devices,
):
    f32, bf16 = jnp.float32, jnp.bfloat16
    _, samples, width = own_ref.shape
    ext_rows = low_rows + atom_dev + high_rows
    lane = lax.broadcasted_iota(jnp.int32, (1, width), 1) // head_dim
    head_masks = [(lane == h).astype(f32) for h in range(ATOM_HEADS)]
    root = jnp.float32(math.sqrt(head_dim))
    rank = lax.axis_index("row")
    base = rank * atom_dev
    total = devices * atom_dev
    tok_dev = token_ref.shape[0]
    row_block = lax.broadcasted_iota(jnp.int32, (rows, 1), 0) // QBLOCK
    next_shift = upper_ref[pl.ds(high_rows, 1), 0, :].astype(f32)[:, 0:1].astype(jnp.int32)
    shift = jnp.where(row_block == rows // QBLOCK - 1, next_shift, 0)
    for j in range(rows // QBLOCK - 1):
        shift = shift + jnp.where(row_block == j, shift_ref[j], 0)
    first = row_block * QBLOCK + SHIFT + shift
    lo = jnp.maximum(first, low_rows - base)
    hi = jnp.minimum(first + KWIN, total - base + low_rows)
    column = lax.broadcasted_iota(jnp.int32, (rows, ext_rows), 1)
    keep = (column >= lo) & (column < hi)
    own_start = pl.multiple_of(base, atom_dev)
    next_start = pl.multiple_of(jnp.minimum(base + atom_dev, total - atom_dev), atom_dev)
    next_ids = ids_ref[:, pl.ds(next_start, atom_dev)][:, 0 : rows - atom_dev]
    next_ids = jnp.where(rank < devices - 1, next_ids, -1)
    row_ids = jnp.concatenate([ids_ref[:, pl.ds(own_start, atom_dev)], next_ids], axis=1)
    own_ids = rank * tok_dev + lax.broadcasted_iota(jnp.int32, (tok_dev, 1), 0)
    onehot = (own_ids == row_ids).astype(f32)
    counts = jnp.sum(onehot, axis=1, keepdims=True)
    onehot = onehot.astype(bf16)
    for s in range(samples):
        x = jnp.concatenate(
            [low_ref[:, s, :], own_ref[:, s, :], upper_ref[0:high_rows, s, :]], axis=0
        ).astype(f32)
        mean = jnp.mean(x, axis=-1, keepdims=True)
        var = jnp.mean((x - mean) ** 2, axis=-1, keepdims=True)
        xn = ((x - mean) / jnp.sqrt(var + 1e-05)).astype(bf16)
        q = jnp.dot(xn[low_rows : low_rows + rows], wq_ref[...], preferred_element_type=f32)
        q = q.astype(bf16)
        k = jnp.dot(xn, wk_ref[...], preferred_element_type=f32).astype(bf16)
        v = jnp.dot(xn, wv_ref[...], preferred_element_type=f32).astype(bf16)
        acc = jnp.zeros((rows, width), f32)
        for h in range(ATOM_HEADS):
            qh = q * head_masks[h].astype(bf16)
            sc = lax.dot_general(
                qh, k, (((1,), (1,)), ((), ())), preferred_element_type=f32
            ) / root
            sc = jnp.where(keep, sc, -1e30)
            top = jnp.max(sc, axis=-1, keepdims=True)
            e = jnp.where(keep, jnp.exp(sc - top), 0.0)
            tot = jnp.sum(e, axis=-1, keepdims=True)
            o = jnp.dot(e.astype(bf16), v, preferred_element_type=f32)
            acc = acc + (o / tot) * head_masks[h]
        mixed = acc.astype(bf16)
        base = x[low_rows : low_rows + rows]
        out = (base + jnp.dot(mixed, wo_ref[...], preferred_element_type=f32)).astype(bf16)
        atom_ref[:, s, :] = out[:atom_dev]
        hidden = jnp.maximum(jnp.dot(out, wt_ref[...], preferred_element_type=f32), 0.0)
        top_part = hidden.astype(bf16)
        rest = hidden - top_part.astype(f32)
        mid_part = rest.astype(bf16)
        low_part = (rest - mid_part.astype(f32)).astype(bf16)
        sums = (
            jnp.dot(onehot, top_part, preferred_element_type=f32)
            + jnp.dot(onehot, mid_part, preferred_element_type=f32)
            + jnp.dot(onehot, low_part, preferred_element_type=f32)
        )
        state_ref[s] = (token_ref[:, s, :].astype(f32) + sums / counts).astype(bf16)


def token_kernel(
    every_ref,
    own_ref,
    pair_ref,
    wb_ref,
    flags_ref,
    wq_ref,
    wk_ref,
    wv_ref,
    wo_ref,
    out_ref,
    *,
    heads,
):
    f32, bf16 = jnp.float32, jnp.bfloat16
    samples, tok_dev, width = own_ref.shape
    head_dim = width // heads
    lane = lax.broadcasted_iota(jnp.int32, (1, width), 1) // head_dim
    head_masks = [(lane == h).astype(f32) for h in range(heads)]
    root = jnp.float32(math.sqrt(head_dim))
    keep = flags_ref[...] > 0
    wb = wb_ref[...]
    bias = jnp.concatenate(
        [
            lax.dot_general(wb, pair_ref[t], (((1,), (1,)), ((), ())), preferred_element_type=f32)
            for t in range(tok_dev)
        ],
        axis=0,
    )
    mask_rows = jnp.concatenate(head_masks, axis=0)

    def normed(x):
        mean = jnp.mean(x, axis=-1, keepdims=True)
        var = jnp.mean((x - mean) ** 2, axis=-1, keepdims=True)
        return ((x - mean) / jnp.sqrt(var + 1e-05)).astype(bf16)

    for s in range(samples):
        allx = normed(every_ref[s].astype(f32))
        own = own_ref[s].astype(f32)
        q = jnp.dot(normed(own), wq_ref[...], preferred_element_type=f32).astype(bf16)
        k = jnp.dot(allx, wk_ref[...], preferred_element_type=f32).astype(bf16)
        v = jnp.dot(allx, wv_ref[...], preferred_element_type=f32).astype(bf16)
        stacked = jnp.concatenate(
            [q[t : t + 1].astype(f32) * mask_rows for t in range(tok_dev)], axis=0
        ).astype(bf16)
        sc = lax.dot_general(
            stacked, k, (((1,), (1,)), ((), ())), preferred_element_type=f32
        ) / root + bias
        sc = jnp.where(keep, sc, -1e30)
        top = jnp.max(sc, axis=-1, keepdims=True)
        e = jnp.where(keep, jnp.exp(sc - top), 0.0)
        tot = jnp.sum(e, axis=-1, keepdims=True)
        o = jnp.dot(e.astype(bf16), v, preferred_element_type=f32) / tot
        mix = jnp.concatenate(
            [
                jnp.sum(o[t * heads : (t + 1) * heads] * mask_rows, axis=0, keepdims=True)
                for t in range(tok_dev)
            ],
            axis=0,
        ).astype(bf16)
        out_ref[:, s, :] = (own + jnp.dot(mix, wo_ref[...], preferred_element_type=f32)).astype(bf16)


def on_device(
    atom_feat,
    window_shift,
    atom_token,
    token_in,
    pair,
    key_mask,
    w_atom_query,
    w_atom_key,
    w_atom_value,
    w_atom_out,
    w_to_token,
    w_query,
    w_key,
    w_value,
    w_out,
    w_bias,
):
    high = lax.Precision.HIGHEST
    atom_dev, samples, width = atom_feat.shape
    tok_dev = token_in.shape[0]
    tok_width = token_in.shape[2]
    devices = lax.axis_size("row")
    rank = lax.axis_index("row")
    atom_base = rank * atom_dev
    total_atoms = atom_dev * devices
    margin = (KWIN - QBLOCK) // 2
    low_rows = margin + SHIFT
    span = KWIN + 2 * SHIFT
    high_rows = span - low_rows
    blocks = atom_dev // QBLOCK + 1

    shift_row = jnp.broadcast_to(
        window_shift[0].astype(jnp.bfloat16), (1, samples, width)
    )
    low = shifted(atom_feat[atom_dev - low_rows :], "row", 1)
    upper = shifted(
        jnp.concatenate([atom_feat[:high_rows], shift_row], axis=0), "row", -1
    )

    head_dim = width // ATOM_HEADS
    rows = blocks * QBLOCK
    ext_rows = low_rows + atom_dev + high_rows
    kernel = functools.partial(
        atom_kernel,
        atom_dev=atom_dev,
        rows=rows,
        low_rows=low_rows,
        high_rows=high_rows,
        head_dim=head_dim,
        devices=devices,
    )
    vmem = pl.BlockSpec(memory_space=pltpu.VMEM)
    flops = 2 * samples * (
        ext_rows * width * 3 * width
        + rows * width * (width + tok_width)
        + ATOM_HEADS * rows * ext_rows * width * 2
        + 3 * tok_dev * rows * tok_width
    )
    atom_out, state_t = pl.pallas_call(
        kernel,
        out_shape=(
            jax.ShapeDtypeStruct((atom_dev, samples, width), jnp.bfloat16),
            jax.ShapeDtypeStruct((samples, tok_dev, tok_width), jnp.bfloat16),
        ),
        in_specs=[vmem] * 3 + [pl.BlockSpec(memory_space=pltpu.SMEM)] + [vmem] * 7,
        out_specs=(vmem, vmem),
        compiler_params=pltpu.CompilerParams(vmem_limit_bytes=8 * 1024 * 1024),
        cost_estimate=pl.CostEstimate(
            flops=flops,
            transcendentals=samples * ATOM_HEADS * rows * ext_rows,
            bytes_accessed=2 * (ext_rows + atom_dev) * samples * width
            + 2 * width * (3 * width + width + tok_width)
            + 4 * samples * tok_dev * tok_width,
        ),
    )(
        atom_feat,
        low,
        upper,
        window_shift,
        w_atom_query,
        w_atom_key,
        w_atom_value,
        w_atom_out,
        w_to_token,
        atom_token[None, :],
        token_in,
    )

    every = lax.all_gather(state_t, "row", axis=1, tiled=True)
    count = every.shape[1]
    token_out = pl.pallas_call(
        functools.partial(token_kernel, heads=TOKEN_HEADS),
        out_shape=jax.ShapeDtypeStruct((tok_dev, samples, tok_width), jnp.bfloat16),
        in_specs=[vmem] * 9,
        out_specs=vmem,
        compiler_params=pltpu.CompilerParams(vmem_limit_bytes=24 * 1024 * 1024),
        cost_estimate=pl.CostEstimate(
            flops=2 * samples * tok_width * (
                2 * count * tok_width + 2 * tok_dev * tok_width + 2 * TOKEN_HEADS * tok_dev * count
            ),
            transcendentals=samples * TOKEN_HEADS * tok_dev * count,
            bytes_accessed=2 * 4 * tok_width * tok_width
            + 2 * samples * (count + 2 * tok_dev) * tok_width
            + 4 * TOKEN_HEADS * tok_dev * count,
        ),
    )(
        every,
        state_t,
        pair,
        jnp.transpose(w_bias),
        key_mask[None, :],
        w_query,
        w_key,
        w_value,
        w_out,
    )
    return (atom_out, token_out)


def solution(mesh):
    return jax.shard_map(
        on_device,
        mesh=mesh,
        in_specs=(
            P(("groups", "row"), None, None),
            P(("groups", "row")),
            P("groups"),
            P(("groups", "row"), None, None),
            P(("groups", "row"), None, None),
            P("groups"),
            P(),
            P(),
            P(),
            P(),
            P(),
            P(),
            P(),
            P(),
            P(),
            P(),
        ),
        out_specs=(P(("groups", "row"), None, None), P(("groups", "row"), None, None)),
        check_vma=False,
    )
```

```python
import functools
import math

import jax
import jax.numpy as jnp
from jax import lax
from jax.experimental import pallas as pl
from jax.experimental.pallas import tpu as pltpu
from jax.sharding import PartitionSpec as P

ATOM_HEADS = 4
QBLOCK = 32
KWIN = 128
SHIFT = 16
TOKEN_HEADS = 16


def layer_norm(values):
    values = values.astype(jnp.float32)
    mean = jnp.mean(values, axis=-1, keepdims=True)
    var = jnp.mean((values - mean) ** 2, axis=-1, keepdims=True)
    return (values - mean) / jnp.sqrt(var + 1e-05)


def project(values, weight):
    return jnp.einsum("asc,cd->asd", values, weight, preferred_element_type=jnp.float32)


def shifted(block, axis, step):
    count = lax.axis_size(axis)
    route = [(i, i + step) for i in range(count) if 0 <= i + step < count]
    return lax.ppermute(block, axis, route)


def atom_kernel(
    own_ref,
    low_ref,
    upper_ref,
    shift_ref,
    wq_ref,
    wk_ref,
    wv_ref,
    wo_ref,
    wt_ref,
    ids_ref,
    token_ref,
    atom_ref,
    state_ref,
    *,
    atom_dev,
    rows,
    low_rows,
    high_rows,
    head_dim,
    devices,
):
    f32, bf16 = jnp.float32, jnp.bfloat16
    _, samples, width = own_ref.shape
    ext_rows = low_rows + atom_dev + high_rows
    lane = lax.broadcasted_iota(jnp.int32, (1, width), 1) // head_dim
    head_masks = [(lane == h).astype(f32) for h in range(ATOM_HEADS)]
    root = jnp.float32(math.sqrt(head_dim))
    rank = lax.axis_index("row")
    base = rank * atom_dev
    total = devices * atom_dev
    tok_dev = token_ref.shape[0]
    row_block = lax.broadcasted_iota(jnp.int32, (rows, 1), 0) // QBLOCK
    next_shift = upper_ref[pl.ds(high_rows, 1), 0, :].astype(f32)[:, 0:1].astype(jnp.int32)
    shift = jnp.where(row_block == rows // QBLOCK - 1, next_shift, 0)
    for j in range(rows // QBLOCK - 1):
        shift = shift + jnp.where(row_block == j, shift_ref[j], 0)
    first = row_block * QBLOCK + SHIFT + shift
    lo = jnp.maximum(first, low_rows - base)
    hi = jnp.minimum(first + KWIN, total - base + low_rows)
    column = lax.broadcasted_iota(jnp.int32, (rows, ext_rows), 1)
    keep = (column >= lo) & (column < hi)
    own_start = pl.multiple_of(base, atom_dev)
    next_start = pl.multiple_of(jnp.minimum(base + atom_dev, total - atom_dev), atom_dev)
    next_ids = ids_ref[:, pl.ds(next_start, atom_dev)][:, 0 : rows - atom_dev]
    next_ids = jnp.where(rank < devices - 1, next_ids, -1)
    row_ids = jnp.concatenate([ids_ref[:, pl.ds(own_start, atom_dev)], next_ids], axis=1)
    own_ids = rank * tok_dev + lax.broadcasted_iota(jnp.int32, (tok_dev, 1), 0)
    onehot = (own_ids == row_ids).astype(f32)
    counts = jnp.sum(onehot, axis=1, keepdims=True)
    onehot = onehot.astype(bf16)
    for s in range(samples):
        x = jnp.concatenate(
            [low_ref[:, s, :], own_ref[:, s, :], upper_ref[0:high_rows, s, :]], axis=0
        ).astype(f32)
        mean = jnp.mean(x, axis=-1, keepdims=True)
        var = jnp.mean((x - mean) ** 2, axis=-1, keepdims=True)
        xn = ((x - mean) / jnp.sqrt(var + 1e-05)).astype(bf16)
        q = jnp.dot(xn[low_rows : low_rows + rows], wq_ref[...], preferred_element_type=f32)
        q = q.astype(bf16)
        k = jnp.dot(xn, wk_ref[...], preferred_element_type=f32).astype(bf16)
        v = jnp.dot(xn, wv_ref[...], preferred_element_type=f32).astype(bf16)
        acc = jnp.zeros((rows, width), f32)
        for h in range(ATOM_HEADS):
            qh = q * head_masks[h].astype(bf16)
            sc = lax.dot_general(
                qh, k, (((1,), (1,)), ((), ())), preferred_element_type=f32
            ) / root
            sc = jnp.where(keep, sc, -1e30)
            top = jnp.max(sc, axis=-1, keepdims=True)
            e = jnp.where(keep, jnp.exp(sc - top), 0.0)
            tot = jnp.sum(e, axis=-1, keepdims=True)
            o = jnp.dot(e.astype(bf16), v, preferred_element_type=f32)
            acc = acc + (o / tot) * head_masks[h]
        mixed = acc.astype(bf16)
        base = x[low_rows : low_rows + rows]
        out = (base + jnp.dot(mixed, wo_ref[...], preferred_element_type=f32)).astype(bf16)
        atom_ref[:, s, :] = out[:atom_dev]
        hidden = jnp.maximum(jnp.dot(out, wt_ref[...], preferred_element_type=f32), 0.0)
        top_part = hidden.astype(bf16)
        rest = hidden - top_part.astype(f32)
        mid_part = rest.astype(bf16)
        low_part = (rest - mid_part.astype(f32)).astype(bf16)
        sums = (
            jnp.dot(onehot, top_part, preferred_element_type=f32)
            + jnp.dot(onehot, mid_part, preferred_element_type=f32)
            + jnp.dot(onehot, low_part, preferred_element_type=f32)
        )
        state_ref[s] = (token_ref[:, s, :].astype(f32) + sums / counts).astype(bf16)


def token_kernel(
    every_ref,
    own_ref,
    pair_hbm,
    wb_ref,
    flags_ref,
    wq_hbm,
    wk_hbm,
    wv_hbm,
    wo_hbm,
    out_ref,
    pair_ref,
    wq_ref,
    wk_ref,
    wv_ref,
    wo_ref,
    sems,
    *,
    heads,
):
    copies = [
        pltpu.make_async_copy(src, dst, sems.at[i])
        for i, (src, dst) in enumerate(
            [(wk_hbm, wk_ref), (wv_hbm, wv_ref), (pair_hbm, pair_ref), (wq_hbm, wq_ref), (wo_hbm, wo_ref)]
        )
    ]
    for copy in copies:
        copy.start()
    f32, bf16 = jnp.float32, jnp.bfloat16
    samples, tok_dev, width = own_ref.shape
    head_dim = width // heads
    lane = lax.broadcasted_iota(jnp.int32, (1, width), 1) // head_dim
    head_masks = [(lane == h).astype(f32) for h in range(heads)]
    root = jnp.float32(math.sqrt(head_dim))
    keep = flags_ref[...] > 0
    wb = wb_ref[...]
    mask_rows = jnp.concatenate(head_masks, axis=0)

    def normed(x):
        mean = jnp.mean(x, axis=-1, keepdims=True)
        var = jnp.mean((x - mean) ** 2, axis=-1, keepdims=True)
        return ((x - mean) / jnp.sqrt(var + 1e-05)).astype(bf16)

    allx = [normed(every_ref[s].astype(f32)) for s in range(samples)]
    copies[0].wait()
    ks = [jnp.dot(x, wk_ref[...], preferred_element_type=f32).astype(bf16) for x in allx]
    copies[1].wait()
    vs = [jnp.dot(x, wv_ref[...], preferred_element_type=f32).astype(bf16) for x in allx]
    copies[2].wait()
    bias = jnp.concatenate(
        [
            lax.dot_general(wb, pair_ref[t], (((1,), (1,)), ((), ())), preferred_element_type=f32)
            for t in range(tok_dev)
        ],
        axis=0,
    )
    copies[3].wait()
    mixes = []
    for s in range(samples):
        own = own_ref[s].astype(f32)
        q = jnp.dot(normed(own), wq_ref[...], preferred_element_type=f32).astype(bf16)
        stacked = jnp.concatenate(
            [q[t : t + 1].astype(f32) * mask_rows for t in range(tok_dev)], axis=0
        ).astype(bf16)
        sc = lax.dot_general(
            stacked, ks[s], (((1,), (1,)), ((), ())), preferred_element_type=f32
        ) / root + bias
        sc = jnp.where(keep, sc, -1e30)
        top = jnp.max(sc, axis=-1, keepdims=True)
        e = jnp.where(keep, jnp.exp(sc - top), 0.0)
        tot = jnp.sum(e, axis=-1, keepdims=True)
        o = jnp.dot(e.astype(bf16), vs[s], preferred_element_type=f32) / tot
        mixes.append(
            jnp.concatenate(
                [
                    jnp.sum(o[t * heads : (t + 1) * heads] * mask_rows, axis=0, keepdims=True)
                    for t in range(tok_dev)
                ],
                axis=0,
            ).astype(bf16)
        )
    copies[4].wait()
    for s in range(samples):
        own = own_ref[s].astype(f32)
        mix = mixes[s]
        out_ref[:, s, :] = (own + jnp.dot(mix, wo_ref[...], preferred_element_type=f32)).astype(bf16)


def on_device(
    atom_feat,
    window_shift,
    atom_token,
    token_in,
    pair,
    key_mask,
    w_atom_query,
    w_atom_key,
    w_atom_value,
    w_atom_out,
    w_to_token,
    w_query,
    w_key,
    w_value,
    w_out,
    w_bias,
):
    high = lax.Precision.HIGHEST
    atom_dev, samples, width = atom_feat.shape
    tok_dev = token_in.shape[0]
    tok_width = token_in.shape[2]
    devices = lax.axis_size("row")
    rank = lax.axis_index("row")
    atom_base = rank * atom_dev
    total_atoms = atom_dev * devices
    margin = (KWIN - QBLOCK) // 2
    low_rows = margin + SHIFT
    span = KWIN + 2 * SHIFT
    high_rows = span - low_rows
    blocks = atom_dev // QBLOCK + 1

    shift_row = jnp.broadcast_to(
        window_shift[0].astype(jnp.bfloat16), (1, samples, width)
    )
    low = shifted(atom_feat[atom_dev - low_rows :], "row", 1)
    upper = shifted(
        jnp.concatenate([atom_feat[:high_rows], shift_row], axis=0), "row", -1
    )

    head_dim = width // ATOM_HEADS
    rows = blocks * QBLOCK
    ext_rows = low_rows + atom_dev + high_rows
    kernel = functools.partial(
        atom_kernel,
        atom_dev=atom_dev,
        rows=rows,
        low_rows=low_rows,
        high_rows=high_rows,
        head_dim=head_dim,
        devices=devices,
    )
    vmem = pl.BlockSpec(memory_space=pltpu.VMEM)
    flops = 2 * samples * (
        ext_rows * width * 3 * width
        + rows * width * (width + tok_width)
        + ATOM_HEADS * rows * ext_rows * width * 2
        + 3 * tok_dev * rows * tok_width
    )
    atom_out, state_t = pl.pallas_call(
        kernel,
        out_shape=(
            jax.ShapeDtypeStruct((atom_dev, samples, width), jnp.bfloat16),
            jax.ShapeDtypeStruct((samples, tok_dev, tok_width), jnp.bfloat16),
        ),
        in_specs=[vmem] * 3 + [pl.BlockSpec(memory_space=pltpu.SMEM)] + [vmem] * 7,
        out_specs=(vmem, vmem),
        cost_estimate=pl.CostEstimate(
            flops=flops,
            transcendentals=samples * ATOM_HEADS * rows * ext_rows,
            bytes_accessed=2 * (ext_rows + atom_dev) * samples * width
            + 2 * width * (3 * width + width + tok_width)
            + 4 * samples * tok_dev * tok_width,
        ),
    )(
        atom_feat,
        low,
        upper,
        window_shift,
        w_atom_query,
        w_atom_key,
        w_atom_value,
        w_atom_out,
        w_to_token,
        atom_token[None, :],
        token_in,
    )

    every = lax.all_gather(state_t, "row", axis=1, tiled=True)
    count = every.shape[1]
    hbm = pl.BlockSpec(memory_space=pl.ANY)
    token_out = pl.pallas_call(
        functools.partial(token_kernel, heads=TOKEN_HEADS),
        out_shape=jax.ShapeDtypeStruct((tok_dev, samples, tok_width), jnp.bfloat16),
        in_specs=[vmem, vmem, hbm, vmem, vmem, hbm, hbm, hbm, hbm],
        out_specs=vmem,
        scratch_shapes=[
            pltpu.VMEM(pair.shape, pair.dtype),
            pltpu.VMEM(w_query.shape, w_query.dtype),
            pltpu.VMEM(w_key.shape, w_key.dtype),
            pltpu.VMEM(w_value.shape, w_value.dtype),
            pltpu.VMEM(w_out.shape, w_out.dtype),
            pltpu.SemaphoreType.DMA((5,)),
        ],
        cost_estimate=pl.CostEstimate(
            flops=2 * samples * tok_width * (
                2 * count * tok_width + 2 * tok_dev * tok_width + 2 * TOKEN_HEADS * tok_dev * count
            ),
            transcendentals=samples * TOKEN_HEADS * tok_dev * count,
            bytes_accessed=2 * 4 * tok_width * tok_width
            + 2 * samples * (count + 2 * tok_dev) * tok_width
            + 4 * TOKEN_HEADS * tok_dev * count,
        ),
    )(
        every,
        state_t,
        pair,
        jnp.transpose(w_bias),
        key_mask[None, :],
        w_query,
        w_key,
        w_value,
        w_out,
    )
    return (atom_out, token_out)


def solution(mesh):
    return jax.shard_map(
        on_device,
        mesh=mesh,
        in_specs=(
            P(("groups", "row"), None, None),
            P(("groups", "row")),
            P("groups"),
            P(("groups", "row"), None, None),
            P(("groups", "row"), None, None),
            P("groups"),
            P(),
            P(),
            P(),
            P(),
            P(),
            P(),
            P(),
            P(),
            P(),
            P(),
        ),
        out_specs=(P(("groups", "row"), None, None), P(("groups", "row"), None, None)),
        check_vma=False,
    )
```

```python
import functools
import math

import jax
import jax.numpy as jnp
from jax import lax
from jax.experimental import pallas as pl
from jax.experimental.pallas import tpu as pltpu
from jax.sharding import PartitionSpec as P

ATOM_HEADS = 4
QBLOCK = 32
KWIN = 128
SHIFT = 16
TOKEN_HEADS = 16


def layer_norm(values):
    values = values.astype(jnp.float32)
    mean = jnp.mean(values, axis=-1, keepdims=True)
    var = jnp.mean((values - mean) ** 2, axis=-1, keepdims=True)
    return (values - mean) / jnp.sqrt(var + 1e-05)


def project(values, weight):
    return jnp.einsum("asc,cd->asd", values, weight, preferred_element_type=jnp.float32)


def shifted(block, axis, step):
    count = lax.axis_size(axis)
    route = [(i, i + step) for i in range(count) if 0 <= i + step < count]
    return lax.ppermute(block, axis, route)


def atom_kernel(
    own_ref,
    low_ref,
    upper_ref,
    shift_ref,
    wq_ref,
    wk_ref,
    wv_ref,
    wo_ref,
    wt_ref,
    ids_ref,
    token_ref,
    wq_hbm,
    pair_hbm,
    wb_ref,
    atom_ref,
    state_ref,
    query_ref,
    bias_ref,
    wtq_ref,
    pair_ref,
    sems,
    *,
    atom_dev,
    rows,
    low_rows,
    high_rows,
    head_dim,
    devices,
):
    f32, bf16 = jnp.float32, jnp.bfloat16
    copies = [
        pltpu.make_async_copy(wq_hbm, wtq_ref, sems.at[0]),
        pltpu.make_async_copy(pair_hbm, pair_ref, sems.at[1]),
    ]
    for copy in copies:
        copy.start()
    _, samples, width = own_ref.shape
    ext_rows = low_rows + atom_dev + high_rows
    lane = lax.broadcasted_iota(jnp.int32, (1, width), 1) // head_dim
    head_masks = [(lane == h).astype(f32) for h in range(ATOM_HEADS)]
    root = jnp.float32(math.sqrt(head_dim))
    rank = lax.axis_index("row")
    base = rank * atom_dev
    total = devices * atom_dev
    tok_dev = token_ref.shape[0]
    row_block = lax.broadcasted_iota(jnp.int32, (rows, 1), 0) // QBLOCK
    next_shift = upper_ref[pl.ds(high_rows, 1), 0, :].astype(f32)[:, 0:1].astype(jnp.int32)
    shift = jnp.where(row_block == rows // QBLOCK - 1, next_shift, 0)
    for j in range(rows // QBLOCK - 1):
        shift = shift + jnp.where(row_block == j, shift_ref[j], 0)
    first = row_block * QBLOCK + SHIFT + shift
    lo = jnp.maximum(first, low_rows - base)
    hi = jnp.minimum(first + KWIN, total - base + low_rows)
    column = lax.broadcasted_iota(jnp.int32, (rows, ext_rows), 1)
    keep = (column >= lo) & (column < hi)
    own_start = pl.multiple_of(base, atom_dev)
    next_start = pl.multiple_of(jnp.minimum(base + atom_dev, total - atom_dev), atom_dev)
    next_ids = ids_ref[:, pl.ds(next_start, atom_dev)][:, 0 : rows - atom_dev]
    next_ids = jnp.where(rank < devices - 1, next_ids, -1)
    row_ids = jnp.concatenate([ids_ref[:, pl.ds(own_start, atom_dev)], next_ids], axis=1)
    own_ids = rank * tok_dev + lax.broadcasted_iota(jnp.int32, (tok_dev, 1), 0)
    onehot = (own_ids == row_ids).astype(f32)
    counts = jnp.sum(onehot, axis=1, keepdims=True)
    onehot = onehot.astype(bf16)
    for s in range(samples):
        x = jnp.concatenate(
            [low_ref[:, s, :], own_ref[:, s, :], upper_ref[0:high_rows, s, :]], axis=0
        ).astype(f32)
        mean = jnp.mean(x, axis=-1, keepdims=True)
        var = jnp.mean((x - mean) ** 2, axis=-1, keepdims=True)
        xn = ((x - mean) / jnp.sqrt(var + 1e-05)).astype(bf16)
        q = jnp.dot(xn[low_rows : low_rows + rows], wq_ref[...], preferred_element_type=f32)
        q = q.astype(bf16)
        k = jnp.dot(xn, wk_ref[...], preferred_element_type=f32).astype(bf16)
        v = jnp.dot(xn, wv_ref[...], preferred_element_type=f32).astype(bf16)
        acc = jnp.zeros((rows, width), f32)
        for h in range(ATOM_HEADS):
            qh = q * head_masks[h].astype(bf16)
            sc = lax.dot_general(
                qh, k, (((1,), (1,)), ((), ())), preferred_element_type=f32
            ) / root
            sc = jnp.where(keep, sc, -1e30)
            top = jnp.max(sc, axis=-1, keepdims=True)
            e = jnp.where(keep, jnp.exp(sc - top), 0.0)
            tot = jnp.sum(e, axis=-1, keepdims=True)
            o = jnp.dot(e.astype(bf16), v, preferred_element_type=f32)
            acc = acc + (o / tot) * head_masks[h]
        mixed = acc.astype(bf16)
        base = x[low_rows : low_rows + rows]
        out = (base + jnp.dot(mixed, wo_ref[...], preferred_element_type=f32)).astype(bf16)
        atom_ref[:, s, :] = out[:atom_dev]
        hidden = jnp.maximum(jnp.dot(out, wt_ref[...], preferred_element_type=f32), 0.0)
        top_part = hidden.astype(bf16)
        rest = hidden - top_part.astype(f32)
        mid_part = rest.astype(bf16)
        low_part = (rest - mid_part.astype(f32)).astype(bf16)
        sums = (
            jnp.dot(onehot, top_part, preferred_element_type=f32)
            + jnp.dot(onehot, mid_part, preferred_element_type=f32)
            + jnp.dot(onehot, low_part, preferred_element_type=f32)
        )
        state_ref[s] = (token_ref[:, s, :].astype(f32) + sums / counts).astype(bf16)
    copies[1].wait()
    wb = wb_ref[...]
    bias_ref[...] = jnp.concatenate(
        [
            lax.dot_general(wb, pair_ref[t], (((1,), (1,)), ((), ())), preferred_element_type=f32)
            for t in range(tok_dev)
        ],
        axis=0,
    )
    copies[0].wait()
    for s in range(samples):
        st = state_ref[s].astype(f32)
        mean = jnp.mean(st, axis=-1, keepdims=True)
        var = jnp.mean((st - mean) ** 2, axis=-1, keepdims=True)
        tn = ((st - mean) / jnp.sqrt(var + 1e-05)).astype(bf16)
        query_ref[s] = jnp.dot(tn, wtq_ref[...], preferred_element_type=f32).astype(bf16)


def token_kernel(
    every_ref,
    own_ref,
    query_ref,
    bias_ref,
    flags_ref,
    wk_hbm,
    wv_hbm,
    wo_hbm,
    out_ref,
    wk_ref,
    wv_ref,
    wo_ref,
    sems,
    *,
    heads,
):
    copies = [
        pltpu.make_async_copy(src, dst, sems.at[i])
        for i, (src, dst) in enumerate([(wk_hbm, wk_ref), (wv_hbm, wv_ref), (wo_hbm, wo_ref)])
    ]
    for copy in copies:
        copy.start()
    f32, bf16 = jnp.float32, jnp.bfloat16
    samples, tok_dev, width = own_ref.shape
    head_dim = width // heads
    lane = lax.broadcasted_iota(jnp.int32, (1, width), 1) // head_dim
    head_masks = [(lane == h).astype(f32) for h in range(heads)]
    root = jnp.float32(math.sqrt(head_dim))
    keep = flags_ref[...] > 0
    mask_rows = jnp.concatenate(head_masks, axis=0)

    def normed(x):
        mean = jnp.mean(x, axis=-1, keepdims=True)
        var = jnp.mean((x - mean) ** 2, axis=-1, keepdims=True)
        return ((x - mean) / jnp.sqrt(var + 1e-05)).astype(bf16)

    allx = [normed(every_ref[s].astype(f32)) for s in range(samples)]
    copies[0].wait()
    ks = [jnp.dot(x, wk_ref[...], preferred_element_type=f32).astype(bf16) for x in allx]
    copies[1].wait()
    vs = [jnp.dot(x, wv_ref[...], preferred_element_type=f32).astype(bf16) for x in allx]
    bias = bias_ref[...]
    mixes = []
    for s in range(samples):
        q = query_ref[s]
        stacked = jnp.concatenate(
            [q[t : t + 1].astype(f32) * mask_rows for t in range(tok_dev)], axis=0
        ).astype(bf16)
        sc = lax.dot_general(
            stacked, ks[s], (((1,), (1,)), ((), ())), preferred_element_type=f32
        ) / root + bias
        sc = jnp.where(keep, sc, -1e30)
        top = jnp.max(sc, axis=-1, keepdims=True)
        e = jnp.where(keep, jnp.exp(sc - top), 0.0)
        tot = jnp.sum(e, axis=-1, keepdims=True)
        o = jnp.dot(e.astype(bf16), vs[s], preferred_element_type=f32) / tot
        mixes.append(
            jnp.concatenate(
                [
                    jnp.sum(o[t * heads : (t + 1) * heads] * mask_rows, axis=0, keepdims=True)
                    for t in range(tok_dev)
                ],
                axis=0,
            ).astype(bf16)
        )
    copies[2].wait()
    for s in range(samples):
        own = own_ref[s].astype(f32)
        mix = mixes[s]
        out_ref[:, s, :] = (own + jnp.dot(mix, wo_ref[...], preferred_element_type=f32)).astype(bf16)


def on_device(
    atom_feat,
    window_shift,
    atom_token,
    token_in,
    pair,
    key_mask,
    w_atom_query,
    w_atom_key,
    w_atom_value,
    w_atom_out,
    w_to_token,
    w_query,
    w_key,
    w_value,
    w_out,
    w_bias,
):
    high = lax.Precision.HIGHEST
    atom_dev, samples, width = atom_feat.shape
    tok_dev = token_in.shape[0]
    tok_width = token_in.shape[2]
    devices = lax.axis_size("row")
    rank = lax.axis_index("row")
    atom_base = rank * atom_dev
    total_atoms = atom_dev * devices
    margin = (KWIN - QBLOCK) // 2
    low_rows = margin + SHIFT
    span = KWIN + 2 * SHIFT
    high_rows = span - low_rows
    blocks = atom_dev // QBLOCK + 1

    shift_row = jnp.broadcast_to(
        window_shift[0].astype(jnp.bfloat16), (1, samples, width)
    )
    low = shifted(atom_feat[atom_dev - low_rows :], "row", 1)
    upper = shifted(
        jnp.concatenate([atom_feat[:high_rows], shift_row], axis=0), "row", -1
    )

    head_dim = width // ATOM_HEADS
    rows = blocks * QBLOCK
    ext_rows = low_rows + atom_dev + high_rows
    kernel = functools.partial(
        atom_kernel,
        atom_dev=atom_dev,
        rows=rows,
        low_rows=low_rows,
        high_rows=high_rows,
        head_dim=head_dim,
        devices=devices,
    )
    vmem = pl.BlockSpec(memory_space=pltpu.VMEM)
    flops = 2 * samples * (
        ext_rows * width * 3 * width
        + rows * width * (width + tok_width)
        + ATOM_HEADS * rows * ext_rows * width * 2
        + 3 * tok_dev * rows * tok_width
    )
    hbm = pl.BlockSpec(memory_space=pl.ANY)
    count = tok_dev * devices
    atom_out, state_t, query_t, bias = pl.pallas_call(
        kernel,
        out_shape=(
            jax.ShapeDtypeStruct((atom_dev, samples, width), jnp.bfloat16),
            jax.ShapeDtypeStruct((samples, tok_dev, tok_width), jnp.bfloat16),
            jax.ShapeDtypeStruct((samples, tok_dev, tok_width), jnp.bfloat16),
            jax.ShapeDtypeStruct((TOKEN_HEADS * tok_dev, count), jnp.float32),
        ),
        in_specs=[vmem] * 3
        + [pl.BlockSpec(memory_space=pltpu.SMEM)]
        + [vmem] * 7
        + [hbm, hbm, vmem],
        out_specs=(vmem, vmem, vmem, vmem),
        scratch_shapes=[
            pltpu.VMEM(w_query.shape, w_query.dtype),
            pltpu.VMEM(pair.shape, pair.dtype),
            pltpu.SemaphoreType.DMA((2,)),
        ],
        cost_estimate=pl.CostEstimate(
            flops=flops,
            transcendentals=samples * ATOM_HEADS * rows * ext_rows,
            bytes_accessed=2 * (ext_rows + atom_dev) * samples * width
            + 2 * width * (3 * width + width + tok_width)
            + 4 * samples * tok_dev * tok_width,
        ),
    )(
        atom_feat,
        low,
        upper,
        window_shift,
        w_atom_query,
        w_atom_key,
        w_atom_value,
        w_atom_out,
        w_to_token,
        atom_token[None, :],
        token_in,
        w_query,
        pair,
        jnp.transpose(w_bias),
    )

    every = lax.all_gather(state_t, "row", axis=1, tiled=True)
    token_out = pl.pallas_call(
        functools.partial(token_kernel, heads=TOKEN_HEADS),
        out_shape=jax.ShapeDtypeStruct((tok_dev, samples, tok_width), jnp.bfloat16),
        in_specs=[vmem, vmem, vmem, vmem, vmem, hbm, hbm, hbm],
        out_specs=vmem,
        scratch_shapes=[
            pltpu.VMEM(w_key.shape, w_key.dtype),
            pltpu.VMEM(w_value.shape, w_value.dtype),
            pltpu.VMEM(w_out.shape, w_out.dtype),
            pltpu.SemaphoreType.DMA((3,)),
        ],
        cost_estimate=pl.CostEstimate(
            flops=2 * samples * tok_width * (
                2 * count * tok_width + 2 * tok_dev * tok_width + 2 * TOKEN_HEADS * tok_dev * count
            ),
            transcendentals=samples * TOKEN_HEADS * tok_dev * count,
            bytes_accessed=2 * 4 * tok_width * tok_width
            + 2 * samples * (count + 2 * tok_dev) * tok_width
            + 4 * TOKEN_HEADS * tok_dev * count,
        ),
    )(
        every,
        state_t,
        query_t,
        bias,
        key_mask[None, :],
        w_key,
        w_value,
        w_out,
    )
    return (atom_out, token_out)


def solution(mesh):
    return jax.shard_map(
        on_device,
        mesh=mesh,
        in_specs=(
            P(("groups", "row"), None, None),
            P(("groups", "row")),
            P("groups"),
            P(("groups", "row"), None, None),
            P(("groups", "row"), None, None),
            P("groups"),
            P(),
            P(),
            P(),
            P(),
            P(),
            P(),
            P(),
            P(),
            P(),
            P(),
        ),
        out_specs=(P(("groups", "row"), None, None), P(("groups", "row"), None, None)),
        check_vma=False,
    )
```

```python
import functools
import math

import jax
import jax.numpy as jnp
from jax import lax
from jax.experimental import pallas as pl
from jax.experimental.pallas import tpu as pltpu
from jax.sharding import PartitionSpec as P

ATOM_HEADS = 4
QBLOCK = 32
KWIN = 128
SHIFT = 16
TOKEN_HEADS = 16


def layer_norm(values):
    values = values.astype(jnp.float32)
    mean = jnp.mean(values, axis=-1, keepdims=True)
    var = jnp.mean((values - mean) ** 2, axis=-1, keepdims=True)
    return (values - mean) / jnp.sqrt(var + 1e-05)


def project(values, weight):
    return jnp.einsum("asc,cd->asd", values, weight, preferred_element_type=jnp.float32)


def shifted(block, axis, step):
    count = lax.axis_size(axis)
    route = [(i, i + step) for i in range(count) if 0 <= i + step < count]
    return lax.ppermute(block, axis, route)


def atom_kernel(
    own_ref,
    low_ref,
    upper_ref,
    shift_ref,
    wq_ref,
    wk_ref,
    wv_ref,
    wo_ref,
    wt_ref,
    ids_ref,
    token_ref,
    wq_hbm,
    atom_ref,
    state_ref,
    query_ref,
    wtq_ref,
    sems,
    *,
    atom_dev,
    rows,
    low_rows,
    high_rows,
    head_dim,
    devices,
):
    f32, bf16 = jnp.float32, jnp.bfloat16
    copies = [pltpu.make_async_copy(wq_hbm, wtq_ref, sems.at[0])]
    for copy in copies:
        copy.start()
    _, samples, width = own_ref.shape
    ext_rows = low_rows + atom_dev + high_rows
    lane = lax.broadcasted_iota(jnp.int32, (1, width), 1) // head_dim
    head_masks = [(lane == h).astype(f32) for h in range(ATOM_HEADS)]
    root = jnp.float32(math.sqrt(head_dim))
    rank = lax.axis_index("row")
    base = rank * atom_dev
    total = devices * atom_dev
    tok_dev = token_ref.shape[0]
    row_block = lax.broadcasted_iota(jnp.int32, (rows, 1), 0) // QBLOCK
    next_shift = upper_ref[pl.ds(high_rows, 1), 0, :].astype(f32)[:, 0:1].astype(jnp.int32)
    shift = jnp.where(row_block == rows // QBLOCK - 1, next_shift, 0)
    for j in range(rows // QBLOCK - 1):
        shift = shift + jnp.where(row_block == j, shift_ref[j], 0)
    first = row_block * QBLOCK + SHIFT + shift
    lo = jnp.maximum(first, low_rows - base)
    hi = jnp.minimum(first + KWIN, total - base + low_rows)
    column = lax.broadcasted_iota(jnp.int32, (rows, ext_rows), 1)
    keep = (column >= lo) & (column < hi)
    own_start = pl.multiple_of(base, atom_dev)
    next_start = pl.multiple_of(jnp.minimum(base + atom_dev, total - atom_dev), atom_dev)
    next_ids = ids_ref[:, pl.ds(next_start, atom_dev)][:, 0 : rows - atom_dev]
    next_ids = jnp.where(rank < devices - 1, next_ids, -1)
    row_ids = jnp.concatenate([ids_ref[:, pl.ds(own_start, atom_dev)], next_ids], axis=1)
    own_ids = rank * tok_dev + lax.broadcasted_iota(jnp.int32, (tok_dev, 1), 0)
    onehot = (own_ids == row_ids).astype(f32)
    counts = jnp.sum(onehot, axis=1, keepdims=True)
    onehot = onehot.astype(bf16)
    for s in range(samples):
        x = jnp.concatenate(
            [low_ref[:, s, :], own_ref[:, s, :], upper_ref[0:high_rows, s, :]], axis=0
        ).astype(f32)
        mean = jnp.mean(x, axis=-1, keepdims=True)
        var = jnp.mean((x - mean) ** 2, axis=-1, keepdims=True)
        xn = ((x - mean) / jnp.sqrt(var + 1e-05)).astype(bf16)
        q = jnp.dot(xn[low_rows : low_rows + rows], wq_ref[...], preferred_element_type=f32)
        q = q.astype(bf16)
        k = jnp.dot(xn, wk_ref[...], preferred_element_type=f32).astype(bf16)
        v = jnp.dot(xn, wv_ref[...], preferred_element_type=f32).astype(bf16)
        acc = jnp.zeros((rows, width), f32)
        for h in range(ATOM_HEADS):
            qh = q * head_masks[h].astype(bf16)
            sc = lax.dot_general(
                qh, k, (((1,), (1,)), ((), ())), preferred_element_type=f32
            ) / root
            sc = jnp.where(keep, sc, -1e30)
            top = jnp.max(sc, axis=-1, keepdims=True)
            e = jnp.where(keep, jnp.exp(sc - top), 0.0)
            tot = jnp.sum(e, axis=-1, keepdims=True)
            o = jnp.dot(e.astype(bf16), v, preferred_element_type=f32)
            acc = acc + (o / tot) * head_masks[h]
        mixed = acc.astype(bf16)
        base = x[low_rows : low_rows + rows]
        out = (base + jnp.dot(mixed, wo_ref[...], preferred_element_type=f32)).astype(bf16)
        atom_ref[:, s, :] = out[:atom_dev]
        hidden = jnp.maximum(jnp.dot(out, wt_ref[...], preferred_element_type=f32), 0.0)
        top_part = hidden.astype(bf16)
        rest = hidden - top_part.astype(f32)
        mid_part = rest.astype(bf16)
        low_part = (rest - mid_part.astype(f32)).astype(bf16)
        sums = (
            jnp.dot(onehot, top_part, preferred_element_type=f32)
            + jnp.dot(onehot, mid_part, preferred_element_type=f32)
            + jnp.dot(onehot, low_part, preferred_element_type=f32)
        )
        state_ref[s] = (token_ref[:, s, :].astype(f32) + sums / counts).astype(bf16)
    copies[0].wait()
    for s in range(samples):
        st = state_ref[s].astype(f32)
        mean = jnp.mean(st, axis=-1, keepdims=True)
        var = jnp.mean((st - mean) ** 2, axis=-1, keepdims=True)
        tn = ((st - mean) / jnp.sqrt(var + 1e-05)).astype(bf16)
        query_ref[s] = jnp.dot(tn, wtq_ref[...], preferred_element_type=f32).astype(bf16)


def token_kernel(
    every_ref,
    own_ref,
    query_ref,
    bias_ref,
    flags_ref,
    wk_hbm,
    wv_hbm,
    wo_hbm,
    out_ref,
    wk_ref,
    wv_ref,
    wo_ref,
    sems,
    *,
    heads,
):
    copies = [
        pltpu.make_async_copy(src, dst, sems.at[i])
        for i, (src, dst) in enumerate([(wk_hbm, wk_ref), (wv_hbm, wv_ref), (wo_hbm, wo_ref)])
    ]
    for copy in copies:
        copy.start()
    f32, bf16 = jnp.float32, jnp.bfloat16
    samples, tok_dev, width = own_ref.shape
    head_dim = width // heads
    lane = lax.broadcasted_iota(jnp.int32, (1, width), 1) // head_dim
    head_masks = [(lane == h).astype(f32) for h in range(heads)]
    root = jnp.float32(math.sqrt(head_dim))
    keep = flags_ref[...] > 0
    mask_rows = jnp.concatenate(head_masks, axis=0)

    def normed(x):
        mean = jnp.mean(x, axis=-1, keepdims=True)
        var = jnp.mean((x - mean) ** 2, axis=-1, keepdims=True)
        return ((x - mean) / jnp.sqrt(var + 1e-05)).astype(bf16)

    allx = [normed(every_ref[s].astype(f32)) for s in range(samples)]
    copies[0].wait()
    ks = [jnp.dot(x, wk_ref[...], preferred_element_type=f32).astype(bf16) for x in allx]
    copies[1].wait()
    vs = [jnp.dot(x, wv_ref[...], preferred_element_type=f32).astype(bf16) for x in allx]
    bias = bias_ref[...]
    mixes = []
    for s in range(samples):
        q = query_ref[s]
        stacked = jnp.concatenate(
            [q[t : t + 1].astype(f32) * mask_rows for t in range(tok_dev)], axis=0
        ).astype(bf16)
        sc = lax.dot_general(
            stacked, ks[s], (((1,), (1,)), ((), ())), preferred_element_type=f32
        ) / root + bias
        sc = jnp.where(keep, sc, -1e30)
        top = jnp.max(sc, axis=-1, keepdims=True)
        e = jnp.where(keep, jnp.exp(sc - top), 0.0)
        tot = jnp.sum(e, axis=-1, keepdims=True)
        o = jnp.dot(e.astype(bf16), vs[s], preferred_element_type=f32) / tot
        mixes.append(
            jnp.concatenate(
                [
                    jnp.sum(o[t * heads : (t + 1) * heads] * mask_rows, axis=0, keepdims=True)
                    for t in range(tok_dev)
                ],
                axis=0,
            ).astype(bf16)
        )
    copies[2].wait()
    for s in range(samples):
        own = own_ref[s].astype(f32)
        mix = mixes[s]
        out_ref[:, s, :] = (own + jnp.dot(mix, wo_ref[...], preferred_element_type=f32)).astype(bf16)


def on_device(
    atom_feat,
    window_shift,
    atom_token,
    token_in,
    pair,
    key_mask,
    w_atom_query,
    w_atom_key,
    w_atom_value,
    w_atom_out,
    w_to_token,
    w_query,
    w_key,
    w_value,
    w_out,
    w_bias,
):
    high = lax.Precision.HIGHEST
    atom_dev, samples, width = atom_feat.shape
    tok_dev = token_in.shape[0]
    tok_width = token_in.shape[2]
    devices = lax.axis_size("row")
    rank = lax.axis_index("row")
    atom_base = rank * atom_dev
    total_atoms = atom_dev * devices
    margin = (KWIN - QBLOCK) // 2
    low_rows = margin + SHIFT
    span = KWIN + 2 * SHIFT
    high_rows = span - low_rows
    blocks = atom_dev // QBLOCK + 1

    shift_row = jnp.broadcast_to(
        window_shift[0].astype(jnp.bfloat16), (1, samples, width)
    )
    low = shifted(atom_feat[atom_dev - low_rows :], "row", 1)
    upper = shifted(
        jnp.concatenate([atom_feat[:high_rows], shift_row], axis=0), "row", -1
    )

    head_dim = width // ATOM_HEADS
    rows = blocks * QBLOCK
    ext_rows = low_rows + atom_dev + high_rows
    kernel = functools.partial(
        atom_kernel,
        atom_dev=atom_dev,
        rows=rows,
        low_rows=low_rows,
        high_rows=high_rows,
        head_dim=head_dim,
        devices=devices,
    )
    vmem = pl.BlockSpec(memory_space=pltpu.VMEM)
    flops = 2 * samples * (
        ext_rows * width * 3 * width
        + rows * width * (width + tok_width)
        + ATOM_HEADS * rows * ext_rows * width * 2
        + 3 * tok_dev * rows * tok_width
    )
    hbm = pl.BlockSpec(memory_space=pl.ANY)
    count = tok_dev * devices
    atom_out, state_t, query_t = pl.pallas_call(
        kernel,
        out_shape=(
            jax.ShapeDtypeStruct((atom_dev, samples, width), jnp.bfloat16),
            jax.ShapeDtypeStruct((samples, tok_dev, tok_width), jnp.bfloat16),
            jax.ShapeDtypeStruct((samples, tok_dev, tok_width), jnp.bfloat16),
        ),
        in_specs=[vmem] * 3
        + [pl.BlockSpec(memory_space=pltpu.SMEM)]
        + [vmem] * 7
        + [hbm],
        out_specs=(vmem, vmem, vmem),
        scratch_shapes=[
            pltpu.VMEM(w_query.shape, w_query.dtype),
            pltpu.SemaphoreType.DMA((1,)),
        ],
        cost_estimate=pl.CostEstimate(
            flops=flops,
            transcendentals=samples * ATOM_HEADS * rows * ext_rows,
            bytes_accessed=2 * (ext_rows + atom_dev) * samples * width
            + 2 * width * (3 * width + width + tok_width)
            + 4 * samples * tok_dev * tok_width,
        ),
    )(
        atom_feat,
        low,
        upper,
        window_shift,
        w_atom_query,
        w_atom_key,
        w_atom_value,
        w_atom_out,
        w_to_token,
        atom_token[None, :],
        token_in,
        w_query,
    )
    bias = jnp.einsum("qkc,ch->qhk", pair, w_bias, preferred_element_type=jnp.float32)
    bias = bias.reshape(tok_dev * TOKEN_HEADS, count)

    every = lax.all_gather(state_t, "row", axis=1, tiled=True)
    token_out = pl.pallas_call(
        functools.partial(token_kernel, heads=TOKEN_HEADS),
        out_shape=jax.ShapeDtypeStruct((tok_dev, samples, tok_width), jnp.bfloat16),
        in_specs=[vmem, vmem, vmem, vmem, vmem, hbm, hbm, hbm],
        out_specs=vmem,
        scratch_shapes=[
            pltpu.VMEM(w_key.shape, w_key.dtype),
            pltpu.VMEM(w_value.shape, w_value.dtype),
            pltpu.VMEM(w_out.shape, w_out.dtype),
            pltpu.SemaphoreType.DMA((3,)),
        ],
        cost_estimate=pl.CostEstimate(
            flops=2 * samples * tok_width * (
                2 * count * tok_width + 2 * tok_dev * tok_width + 2 * TOKEN_HEADS * tok_dev * count
            ),
            transcendentals=samples * TOKEN_HEADS * tok_dev * count,
            bytes_accessed=2 * 4 * tok_width * tok_width
            + 2 * samples * (count + 2 * tok_dev) * tok_width
            + 4 * TOKEN_HEADS * tok_dev * count,
        ),
    )(
        every,
        state_t,
        query_t,
        bias,
        key_mask[None, :],
        w_key,
        w_value,
        w_out,
    )
    return (atom_out, token_out)


def solution(mesh):
    return jax.shard_map(
        on_device,
        mesh=mesh,
        in_specs=(
            P(("groups", "row"), None, None),
            P(("groups", "row")),
            P("groups"),
            P(("groups", "row"), None, None),
            P(("groups", "row"), None, None),
            P("groups"),
            P(),
            P(),
            P(),
            P(),
            P(),
            P(),
            P(),
            P(),
            P(),
            P(),
        ),
        out_specs=(P(("groups", "row"), None, None), P(("groups", "row"), None, None)),
        check_vma=False,
    )
```

```python
import functools
import math

import jax
import jax.numpy as jnp
from jax import lax
from jax.experimental import pallas as pl
from jax.experimental.pallas import tpu as pltpu
from jax.sharding import PartitionSpec as P

ATOM_HEADS = 4
QBLOCK = 32
KWIN = 128
SHIFT = 16
TOKEN_HEADS = 16


def layer_norm(values):
    values = values.astype(jnp.float32)
    mean = jnp.mean(values, axis=-1, keepdims=True)
    var = jnp.mean((values - mean) ** 2, axis=-1, keepdims=True)
    return (values - mean) / jnp.sqrt(var + 1e-05)


def project(values, weight):
    return jnp.einsum("asc,cd->asd", values, weight, preferred_element_type=jnp.float32)


def shifted(block, axis, step):
    count = lax.axis_size(axis)
    route = [(i, i + step) for i in range(count) if 0 <= i + step < count]
    return lax.ppermute(block, axis, route)


def atom_kernel(
    own_ref,
    low_ref,
    upper_ref,
    shift_ref,
    wq_ref,
    wk_ref,
    wv_ref,
    wo_ref,
    wt_ref,
    ids_ref,
    token_ref,
    wq_hbm,
    atom_ref,
    state_ref,
    query_ref,
    wtq_ref,
    sems,
    *,
    atom_dev,
    rows,
    low_rows,
    high_rows,
    head_dim,
    devices,
):
    f32, bf16 = jnp.float32, jnp.bfloat16
    copies = [pltpu.make_async_copy(wq_hbm, wtq_ref, sems.at[0])]
    for copy in copies:
        copy.start()
    _, samples, width = own_ref.shape
    ext_rows = low_rows + atom_dev + high_rows
    lane = lax.broadcasted_iota(jnp.int32, (1, width), 1) // head_dim
    head_masks = [(lane == h).astype(f32) for h in range(ATOM_HEADS)]
    root = jnp.float32(math.sqrt(head_dim))
    rank = lax.axis_index("row")
    base = rank * atom_dev
    total = devices * atom_dev
    tok_dev = token_ref.shape[0]
    row_block = lax.broadcasted_iota(jnp.int32, (rows, 1), 0) // QBLOCK
    next_shift = upper_ref[pl.ds(high_rows, 1), 0, :].astype(f32)[:, 0:1].astype(jnp.int32)
    shift = jnp.where(row_block == rows // QBLOCK - 1, next_shift, 0)
    for j in range(rows // QBLOCK - 1):
        shift = shift + jnp.where(row_block == j, shift_ref[j], 0)
    first = row_block * QBLOCK + SHIFT + shift
    lo = jnp.maximum(first, low_rows - base)
    hi = jnp.minimum(first + KWIN, total - base + low_rows)
    column = lax.broadcasted_iota(jnp.int32, (rows, ext_rows), 1)
    keep = (column >= lo) & (column < hi)
    own_start = pl.multiple_of(base, atom_dev)
    next_start = pl.multiple_of(jnp.minimum(base + atom_dev, total - atom_dev), atom_dev)
    next_ids = ids_ref[:, pl.ds(next_start, atom_dev)][:, 0 : rows - atom_dev]
    next_ids = jnp.where(rank < devices - 1, next_ids, -1)
    row_ids = jnp.concatenate([ids_ref[:, pl.ds(own_start, atom_dev)], next_ids], axis=1)
    own_ids = rank * tok_dev + lax.broadcasted_iota(jnp.int32, (tok_dev, 1), 0)
    onehot = (own_ids == row_ids).astype(f32)
    counts = jnp.sum(onehot, axis=1, keepdims=True)
    onehot = onehot.astype(bf16)
    for s in range(samples):
        x = jnp.concatenate(
            [low_ref[:, s, :], own_ref[:, s, :], upper_ref[0:high_rows, s, :]], axis=0
        ).astype(f32)
        mean = jnp.mean(x, axis=-1, keepdims=True)
        var = jnp.mean((x - mean) ** 2, axis=-1, keepdims=True)
        xn = ((x - mean) / jnp.sqrt(var + 1e-05)).astype(bf16)
        q = jnp.dot(xn[low_rows : low_rows + rows], wq_ref[...], preferred_element_type=f32)
        q = q.astype(bf16)
        k = jnp.dot(xn, wk_ref[...], preferred_element_type=f32).astype(bf16)
        v = jnp.dot(xn, wv_ref[...], preferred_element_type=f32).astype(bf16)
        acc = jnp.zeros((rows, width), f32)
        for h in range(ATOM_HEADS):
            qh = q * head_masks[h].astype(bf16)
            sc = lax.dot_general(
                qh, k, (((1,), (1,)), ((), ())), preferred_element_type=f32
            ) / root
            sc = jnp.where(keep, sc, -1e30)
            top = jnp.max(sc, axis=-1, keepdims=True)
            e = jnp.where(keep, jnp.exp(sc - top), 0.0)
            tot = jnp.sum(e, axis=-1, keepdims=True)
            o = jnp.dot(e.astype(bf16), v, preferred_element_type=f32)
            acc = acc + (o / tot) * head_masks[h]
        mixed = acc.astype(bf16)
        base = x[low_rows : low_rows + rows]
        out = (base + jnp.dot(mixed, wo_ref[...], preferred_element_type=f32)).astype(bf16)
        atom_ref[:, s, :] = out[:atom_dev]
        hidden = jnp.maximum(jnp.dot(out, wt_ref[...], preferred_element_type=f32), 0.0)
        top_part = hidden.astype(bf16)
        rest = hidden - top_part.astype(f32)
        mid_part = rest.astype(bf16)
        low_part = (rest - mid_part.astype(f32)).astype(bf16)
        sums = (
            jnp.dot(onehot, top_part, preferred_element_type=f32)
            + jnp.dot(onehot, mid_part, preferred_element_type=f32)
            + jnp.dot(onehot, low_part, preferred_element_type=f32)
        )
        state_ref[s] = (token_ref[:, s, :].astype(f32) + sums / counts).astype(bf16)
    copies[0].wait()
    for s in range(samples):
        st = state_ref[s].astype(f32)
        mean = jnp.mean(st, axis=-1, keepdims=True)
        var = jnp.mean((st - mean) ** 2, axis=-1, keepdims=True)
        tn = ((st - mean) / jnp.sqrt(var + 1e-05)).astype(bf16)
        query_ref[s] = jnp.dot(tn, wtq_ref[...], preferred_element_type=f32).astype(bf16)


def token_kernel(
    every_hbm,
    own_ref,
    query_ref,
    bias_ref,
    flags_ref,
    wk_hbm,
    wv_hbm,
    wo_hbm,
    out_ref,
    every_ref,
    wk_ref,
    wv_ref,
    wo_ref,
    sems,
    *,
    heads,
    chunk,
):
    f32, bf16 = jnp.float32, jnp.bfloat16
    samples = every_ref.shape[0]
    width = wk_ref.shape[0]
    chunks = width // chunk
    pairs = [(every_hbm.at[s], every_ref.at[s]) for s in range(samples)]
    for w_hbm, w_ref in ((wk_hbm, wk_ref), (wv_hbm, wv_ref)):
        pairs += [
            (w_hbm.at[pl.ds(c * chunk, chunk)], w_ref.at[pl.ds(c * chunk, chunk)])
            for c in range(chunks)
        ]
    pairs.append((wo_hbm, wo_ref))
    copies = [pltpu.make_async_copy(src, dst, sems.at[i]) for i, (src, dst) in enumerate(pairs)]
    for copy in copies:
        copy.start()
    f32, bf16 = jnp.float32, jnp.bfloat16
    samples, tok_dev, width = own_ref.shape
    head_dim = width // heads
    lane = lax.broadcasted_iota(jnp.int32, (1, width), 1) // head_dim
    head_masks = [(lane == h).astype(f32) for h in range(heads)]
    root = jnp.float32(math.sqrt(head_dim))
    keep = flags_ref[...] > 0
    mask_rows = jnp.concatenate(head_masks, axis=0)

    def normed(x):
        mean = jnp.mean(x, axis=-1, keepdims=True)
        var = jnp.mean((x - mean) ** 2, axis=-1, keepdims=True)
        return ((x - mean) / jnp.sqrt(var + 1e-05)).astype(bf16)

    allx = []
    for s in range(samples):
        copies[s].wait()
        allx.append(normed(every_ref[s].astype(f32)))

    def projected(w_ref, first):
        acc = [None] * samples
        for c in range(chunks):
            copies[first + c].wait()
            part = w_ref[c * chunk : (c + 1) * chunk, :]
            for s in range(samples):
                term = jnp.dot(
                    allx[s][:, c * chunk : (c + 1) * chunk], part, preferred_element_type=f32
                )
                acc[s] = term if acc[s] is None else acc[s] + term
        return [a.astype(bf16) for a in acc]

    ks = projected(wk_ref, samples)
    vs = projected(wv_ref, samples + chunks)
    bias = bias_ref[...]
    mixes = []
    for s in range(samples):
        q = query_ref[s]
        stacked = jnp.concatenate(
            [q[t : t + 1].astype(f32) * mask_rows for t in range(tok_dev)], axis=0
        ).astype(bf16)
        sc = lax.dot_general(
            stacked, ks[s], (((1,), (1,)), ((), ())), preferred_element_type=f32
        ) / root + bias
        sc = jnp.where(keep, sc, -1e30)
        top = jnp.max(sc, axis=-1, keepdims=True)
        e = jnp.where(keep, jnp.exp(sc - top), 0.0)
        tot = jnp.sum(e, axis=-1, keepdims=True)
        o = jnp.dot(e.astype(bf16), vs[s], preferred_element_type=f32) / tot
        mixes.append(
            jnp.concatenate(
                [
                    jnp.sum(o[t * heads : (t + 1) * heads] * mask_rows, axis=0, keepdims=True)
                    for t in range(tok_dev)
                ],
                axis=0,
            ).astype(bf16)
        )
    copies[-1].wait()
    for s in range(samples):
        own = own_ref[s].astype(f32)
        mix = mixes[s]
        out_ref[:, s, :] = (own + jnp.dot(mix, wo_ref[...], preferred_element_type=f32)).astype(bf16)


def on_device(
    atom_feat,
    window_shift,
    atom_token,
    token_in,
    pair,
    key_mask,
    w_atom_query,
    w_atom_key,
    w_atom_value,
    w_atom_out,
    w_to_token,
    w_query,
    w_key,
    w_value,
    w_out,
    w_bias,
):
    high = lax.Precision.HIGHEST
    atom_dev, samples, width = atom_feat.shape
    tok_dev = token_in.shape[0]
    tok_width = token_in.shape[2]
    devices = lax.axis_size("row")
    rank = lax.axis_index("row")
    atom_base = rank * atom_dev
    total_atoms = atom_dev * devices
    margin = (KWIN - QBLOCK) // 2
    low_rows = margin + SHIFT
    span = KWIN + 2 * SHIFT
    high_rows = span - low_rows
    blocks = atom_dev // QBLOCK + 1

    shift_row = jnp.broadcast_to(
        window_shift[0].astype(jnp.bfloat16), (1, samples, width)
    )
    low = shifted(atom_feat[atom_dev - low_rows :], "row", 1)
    upper = shifted(
        jnp.concatenate([atom_feat[:high_rows], shift_row], axis=0), "row", -1
    )

    head_dim = width // ATOM_HEADS
    rows = blocks * QBLOCK
    ext_rows = low_rows + atom_dev + high_rows
    kernel = functools.partial(
        atom_kernel,
        atom_dev=atom_dev,
        rows=rows,
        low_rows=low_rows,
        high_rows=high_rows,
        head_dim=head_dim,
        devices=devices,
    )
    vmem = pl.BlockSpec(memory_space=pltpu.VMEM)
    flops = 2 * samples * (
        ext_rows * width * 3 * width
        + rows * width * (width + tok_width)
        + ATOM_HEADS * rows * ext_rows * width * 2
        + 3 * tok_dev * rows * tok_width
    )
    hbm = pl.BlockSpec(memory_space=pl.ANY)
    count = tok_dev * devices
    atom_out, state_t, query_t = pl.pallas_call(
        kernel,
        out_shape=(
            jax.ShapeDtypeStruct((atom_dev, samples, width), jnp.bfloat16),
            jax.ShapeDtypeStruct((samples, tok_dev, tok_width), jnp.bfloat16),
            jax.ShapeDtypeStruct((samples, tok_dev, tok_width), jnp.bfloat16),
        ),
        in_specs=[vmem] * 3
        + [pl.BlockSpec(memory_space=pltpu.SMEM)]
        + [vmem] * 7
        + [hbm],
        out_specs=(vmem, vmem, vmem),
        scratch_shapes=[
            pltpu.VMEM(w_query.shape, w_query.dtype),
            pltpu.SemaphoreType.DMA((1,)),
        ],
        cost_estimate=pl.CostEstimate(
            flops=flops,
            transcendentals=samples * ATOM_HEADS * rows * ext_rows,
            bytes_accessed=2 * (ext_rows + atom_dev) * samples * width
            + 2 * width * (3 * width + width + tok_width)
            + 4 * samples * tok_dev * tok_width,
        ),
    )(
        atom_feat,
        low,
        upper,
        window_shift,
        w_atom_query,
        w_atom_key,
        w_atom_value,
        w_atom_out,
        w_to_token,
        atom_token[None, :],
        token_in,
        w_query,
    )
    bias = jnp.einsum("qkc,ch->qhk", pair, w_bias, preferred_element_type=jnp.float32)
    bias = bias.reshape(tok_dev * TOKEN_HEADS, count)

    every = lax.all_gather(state_t, "row", axis=1, tiled=True)
    token_out = pl.pallas_call(
        functools.partial(token_kernel, heads=TOKEN_HEADS, chunk=128),
        out_shape=jax.ShapeDtypeStruct((tok_dev, samples, tok_width), jnp.bfloat16),
        in_specs=[hbm, vmem, vmem, vmem, vmem, hbm, hbm, hbm],
        out_specs=vmem,
        scratch_shapes=[
            pltpu.VMEM(every.shape, every.dtype),
            pltpu.VMEM(w_key.shape, w_key.dtype),
            pltpu.VMEM(w_value.shape, w_value.dtype),
            pltpu.VMEM(w_out.shape, w_out.dtype),
            pltpu.SemaphoreType.DMA((samples + 2 * (tok_width // 128) + 1,)),
        ],
        cost_estimate=pl.CostEstimate(
            flops=2 * samples * tok_width * (
                2 * count * tok_width + 2 * tok_dev * tok_width + 2 * TOKEN_HEADS * tok_dev * count
            ),
            transcendentals=samples * TOKEN_HEADS * tok_dev * count,
            bytes_accessed=2 * 4 * tok_width * tok_width
            + 2 * samples * (count + 2 * tok_dev) * tok_width
            + 4 * TOKEN_HEADS * tok_dev * count,
        ),
    )(
        every,
        state_t,
        query_t,
        bias,
        key_mask[None, :],
        w_key,
        w_value,
        w_out,
    )
    return (atom_out, token_out)


def solution(mesh):
    return jax.shard_map(
        on_device,
        mesh=mesh,
        in_specs=(
            P(("groups", "row"), None, None),
            P(("groups", "row")),
            P("groups"),
            P(("groups", "row"), None, None),
            P(("groups", "row"), None, None),
            P("groups"),
            P(),
            P(),
            P(),
            P(),
            P(),
            P(),
            P(),
            P(),
            P(),
            P(),
        ),
        out_specs=(P(("groups", "row"), None, None), P(("groups", "row"), None, None)),
        check_vma=False,
    )
```

```python
import functools
import math

import jax
import jax.numpy as jnp
from jax import lax
from jax.experimental import pallas as pl
from jax.experimental.pallas import tpu as pltpu
from jax.sharding import PartitionSpec as P

ATOM_HEADS = 4
QBLOCK = 32
KWIN = 128
SHIFT = 16
TOKEN_HEADS = 16


def layer_norm(values):
    values = values.astype(jnp.float32)
    mean = jnp.mean(values, axis=-1, keepdims=True)
    var = jnp.mean((values - mean) ** 2, axis=-1, keepdims=True)
    return (values - mean) / jnp.sqrt(var + 1e-05)


def project(values, weight):
    return jnp.einsum("asc,cd->asd", values, weight, preferred_element_type=jnp.float32)


def shifted(block, axis, step):
    count = lax.axis_size(axis)
    route = [(i, i + step) for i in range(count) if 0 <= i + step < count]
    return lax.ppermute(block, axis, route)


def atom_kernel(
    own_ref,
    low_ref,
    upper_ref,
    shift_ref,
    wq_ref,
    wk_ref,
    wv_ref,
    wo_ref,
    wt_ref,
    ids_ref,
    token_ref,
    wq_hbm,
    atom_ref,
    state_ref,
    query_ref,
    wtq_ref,
    sems,
    *,
    atom_dev,
    rows,
    low_rows,
    high_rows,
    head_dim,
    devices,
):
    f32, bf16 = jnp.float32, jnp.bfloat16
    copies = [pltpu.make_async_copy(wq_hbm, wtq_ref, sems.at[0])]
    for copy in copies:
        copy.start()
    _, samples, width = own_ref.shape
    ext_rows = low_rows + atom_dev + high_rows
    lane = lax.broadcasted_iota(jnp.int32, (1, width), 1) // head_dim
    head_masks = [(lane == h).astype(f32) for h in range(ATOM_HEADS)]
    root = jnp.float32(math.sqrt(head_dim))
    rank = lax.axis_index("row")
    base = rank * atom_dev
    total = devices * atom_dev
    tok_dev = token_ref.shape[0]
    row_block = lax.broadcasted_iota(jnp.int32, (rows, 1), 0) // QBLOCK
    next_shift = upper_ref[pl.ds(high_rows, 1), 0, :].astype(f32)[:, 0:1].astype(jnp.int32)
    shift = jnp.where(row_block == rows // QBLOCK - 1, next_shift, 0)
    for j in range(rows // QBLOCK - 1):
        shift = shift + jnp.where(row_block == j, shift_ref[j], 0)
    first = row_block * QBLOCK + SHIFT + shift
    lo = jnp.maximum(first, low_rows - base)
    hi = jnp.minimum(first + KWIN, total - base + low_rows)
    column = lax.broadcasted_iota(jnp.int32, (rows, ext_rows), 1)
    keep = (column >= lo) & (column < hi)
    own_start = pl.multiple_of(base, atom_dev)
    next_start = pl.multiple_of(jnp.minimum(base + atom_dev, total - atom_dev), atom_dev)
    next_ids = ids_ref[:, pl.ds(next_start, atom_dev)][:, 0 : rows - atom_dev]
    next_ids = jnp.where(rank < devices - 1, next_ids, -1)
    row_ids = jnp.concatenate([ids_ref[:, pl.ds(own_start, atom_dev)], next_ids], axis=1)
    own_ids = rank * tok_dev + lax.broadcasted_iota(jnp.int32, (tok_dev, 1), 0)
    onehot = (own_ids == row_ids).astype(f32)
    counts = jnp.sum(onehot, axis=1, keepdims=True)
    onehot = onehot.astype(bf16)
    xs, xns = [], []
    for s in range(samples):
        x = jnp.concatenate(
            [low_ref[:, s, :], own_ref[:, s, :], upper_ref[0:high_rows, s, :]], axis=0
        ).astype(f32)
        mean = jnp.mean(x, axis=-1, keepdims=True)
        var = jnp.mean((x - mean) ** 2, axis=-1, keepdims=True)
        xs.append(x)
        xns.append(((x - mean) / jnp.sqrt(var + 1e-05)).astype(bf16))
    xn_all = jnp.concatenate(xns, axis=0)
    q_all = jnp.dot(
        jnp.concatenate([xn[low_rows : low_rows + rows] for xn in xns], axis=0),
        wq_ref[...],
        preferred_element_type=f32,
    ).astype(bf16)
    k_all = jnp.dot(xn_all, wk_ref[...], preferred_element_type=f32).astype(bf16)
    v_all = jnp.dot(xn_all, wv_ref[...], preferred_element_type=f32).astype(bf16)
    mixed = []
    for s in range(samples):
        q = q_all[s * rows : (s + 1) * rows]
        k = k_all[s * ext_rows : (s + 1) * ext_rows]
        v = v_all[s * ext_rows : (s + 1) * ext_rows]
        acc = jnp.zeros((rows, width), f32)
        for h in range(ATOM_HEADS):
            qh = q * head_masks[h].astype(bf16)
            sc = lax.dot_general(
                qh, k, (((1,), (1,)), ((), ())), preferred_element_type=f32
            ) / root
            sc = jnp.where(keep, sc, -1e30)
            top = jnp.max(sc, axis=-1, keepdims=True)
            e = jnp.where(keep, jnp.exp(sc - top), 0.0)
            tot = jnp.sum(e, axis=-1, keepdims=True)
            o = jnp.dot(e.astype(bf16), v, preferred_element_type=f32)
            acc = acc + (o / tot) * head_masks[h]
        mixed.append(acc.astype(bf16))
    base = jnp.concatenate([x[low_rows : low_rows + rows] for x in xs], axis=0)
    out = (
        base + jnp.dot(jnp.concatenate(mixed, axis=0), wo_ref[...], preferred_element_type=f32)
    ).astype(bf16)
    for s in range(samples):
        atom_ref[:, s, :] = out[s * rows : s * rows + atom_dev]
    hidden = jnp.maximum(jnp.dot(out, wt_ref[...], preferred_element_type=f32), 0.0)
    top_part = hidden.astype(bf16)
    rest = hidden - top_part.astype(f32)
    mid_part = rest.astype(bf16)
    low_part = (rest - mid_part.astype(f32)).astype(bf16)
    zero = jnp.zeros_like(onehot)
    diagonal = jnp.concatenate(
        [
            jnp.concatenate([onehot if c == r else zero for c in range(samples)], axis=1)
            for r in range(samples)
        ],
        axis=0,
    )
    sums = (
        jnp.dot(diagonal, top_part, preferred_element_type=f32)
        + jnp.dot(diagonal, mid_part, preferred_element_type=f32)
        + jnp.dot(diagonal, low_part, preferred_element_type=f32)
    )
    tns = []
    for s in range(samples):
        st = (token_ref[:, s, :].astype(f32) + sums[s * tok_dev : (s + 1) * tok_dev] / counts)
        st = st.astype(bf16)
        state_ref[s] = st
        st = st.astype(f32)
        mean = jnp.mean(st, axis=-1, keepdims=True)
        var = jnp.mean((st - mean) ** 2, axis=-1, keepdims=True)
        tns.append(((st - mean) / jnp.sqrt(var + 1e-05)).astype(bf16))
    copies[0].wait()
    query = jnp.dot(jnp.concatenate(tns, axis=0), wtq_ref[...], preferred_element_type=f32)
    query = query.astype(bf16)
    for s in range(samples):
        query_ref[s] = query[s * tok_dev : (s + 1) * tok_dev]


def token_kernel(
    every_ref,
    own_ref,
    query_ref,
    bias_ref,
    flags_ref,
    wk_hbm,
    wv_hbm,
    wo_hbm,
    out_ref,
    wk_ref,
    wv_ref,
    wo_ref,
    sems,
    *,
    heads,
):
    copies = [
        pltpu.make_async_copy(src, dst, sems.at[i])
        for i, (src, dst) in enumerate([(wk_hbm, wk_ref), (wv_hbm, wv_ref), (wo_hbm, wo_ref)])
    ]
    for copy in copies:
        copy.start()
    f32, bf16 = jnp.float32, jnp.bfloat16
    samples, tok_dev, width = own_ref.shape
    head_dim = width // heads
    lane = lax.broadcasted_iota(jnp.int32, (1, width), 1) // head_dim
    head_masks = [(lane == h).astype(f32) for h in range(heads)]
    root = jnp.float32(math.sqrt(head_dim))
    keep = flags_ref[...] > 0
    mask_rows = jnp.concatenate(head_masks, axis=0)

    def normed(x):
        mean = jnp.mean(x, axis=-1, keepdims=True)
        var = jnp.mean((x - mean) ** 2, axis=-1, keepdims=True)
        return ((x - mean) / jnp.sqrt(var + 1e-05)).astype(bf16)

    allx = jnp.concatenate([normed(every_ref[s].astype(f32)) for s in range(samples)], axis=0)
    count = every_ref.shape[1]
    copies[0].wait()
    k_all = jnp.dot(allx, wk_ref[...], preferred_element_type=f32).astype(bf16)
    copies[1].wait()
    v_all = jnp.dot(allx, wv_ref[...], preferred_element_type=f32).astype(bf16)
    ks = [k_all[s * count : (s + 1) * count] for s in range(samples)]
    vs = [v_all[s * count : (s + 1) * count] for s in range(samples)]
    bias = bias_ref[...]
    mixes = []
    for s in range(samples):
        q = query_ref[s]
        stacked = jnp.concatenate(
            [q[t : t + 1].astype(f32) * mask_rows for t in range(tok_dev)], axis=0
        ).astype(bf16)
        sc = lax.dot_general(
            stacked, ks[s], (((1,), (1,)), ((), ())), preferred_element_type=f32
        ) / root + bias
        sc = jnp.where(keep, sc, -1e30)
        top = jnp.max(sc, axis=-1, keepdims=True)
        e = jnp.where(keep, jnp.exp(sc - top), 0.0)
        tot = jnp.sum(e, axis=-1, keepdims=True)
        o = jnp.dot(e.astype(bf16), vs[s], preferred_element_type=f32) / tot
        mixes.append(
            jnp.concatenate(
                [
                    jnp.sum(o[t * heads : (t + 1) * heads] * mask_rows, axis=0, keepdims=True)
                    for t in range(tok_dev)
                ],
                axis=0,
            ).astype(bf16)
        )
    copies[2].wait()
    projected = jnp.dot(jnp.concatenate(mixes, axis=0), wo_ref[...], preferred_element_type=f32)
    for s in range(samples):
        own = own_ref[s].astype(f32)
        out_ref[:, s, :] = (own + projected[s * tok_dev : (s + 1) * tok_dev]).astype(bf16)


def on_device(
    atom_feat,
    window_shift,
    atom_token,
    token_in,
    pair,
    key_mask,
    w_atom_query,
    w_atom_key,
    w_atom_value,
    w_atom_out,
    w_to_token,
    w_query,
    w_key,
    w_value,
    w_out,
    w_bias,
):
    high = lax.Precision.HIGHEST
    atom_dev, samples, width = atom_feat.shape
    tok_dev = token_in.shape[0]
    tok_width = token_in.shape[2]
    devices = lax.axis_size("row")
    rank = lax.axis_index("row")
    atom_base = rank * atom_dev
    total_atoms = atom_dev * devices
    margin = (KWIN - QBLOCK) // 2
    low_rows = margin + SHIFT
    span = KWIN + 2 * SHIFT
    high_rows = span - low_rows
    blocks = atom_dev // QBLOCK + 1

    shift_row = jnp.broadcast_to(
        window_shift[0].astype(jnp.bfloat16), (1, samples, width)
    )
    low = shifted(atom_feat[atom_dev - low_rows :], "row", 1)
    upper = shifted(
        jnp.concatenate([atom_feat[:high_rows], shift_row], axis=0), "row", -1
    )

    head_dim = width // ATOM_HEADS
    rows = blocks * QBLOCK
    ext_rows = low_rows + atom_dev + high_rows
    kernel = functools.partial(
        atom_kernel,
        atom_dev=atom_dev,
        rows=rows,
        low_rows=low_rows,
        high_rows=high_rows,
        head_dim=head_dim,
        devices=devices,
    )
    vmem = pl.BlockSpec(memory_space=pltpu.VMEM)
    flops = 2 * samples * (
        ext_rows * width * 3 * width
        + rows * width * (width + tok_width)
        + ATOM_HEADS * rows * ext_rows * width * 2
        + 3 * tok_dev * rows * tok_width
    )
    hbm = pl.BlockSpec(memory_space=pl.ANY)
    count = tok_dev * devices
    atom_out, state_t, query_t = pl.pallas_call(
        kernel,
        out_shape=(
            jax.ShapeDtypeStruct((atom_dev, samples, width), jnp.bfloat16),
            jax.ShapeDtypeStruct((samples, tok_dev, tok_width), jnp.bfloat16),
            jax.ShapeDtypeStruct((samples, tok_dev, tok_width), jnp.bfloat16),
        ),
        in_specs=[vmem] * 3
        + [pl.BlockSpec(memory_space=pltpu.SMEM)]
        + [vmem] * 7
        + [hbm],
        out_specs=(vmem, vmem, vmem),
        scratch_shapes=[
            pltpu.VMEM(w_query.shape, w_query.dtype),
            pltpu.SemaphoreType.DMA((1,)),
        ],
        cost_estimate=pl.CostEstimate(
            flops=flops,
            transcendentals=samples * ATOM_HEADS * rows * ext_rows,
            bytes_accessed=2 * (ext_rows + atom_dev) * samples * width
            + 2 * width * (3 * width + width + tok_width)
            + 4 * samples * tok_dev * tok_width,
        ),
    )(
        atom_feat,
        low,
        upper,
        window_shift,
        w_atom_query,
        w_atom_key,
        w_atom_value,
        w_atom_out,
        w_to_token,
        atom_token[None, :],
        token_in,
        w_query,
    )
    bias = jnp.einsum("qkc,ch->qhk", pair, w_bias, preferred_element_type=jnp.float32)
    bias = bias.reshape(tok_dev * TOKEN_HEADS, count)

    every = lax.all_gather(state_t, "row", axis=1, tiled=True)
    token_out = pl.pallas_call(
        functools.partial(token_kernel, heads=TOKEN_HEADS),
        out_shape=jax.ShapeDtypeStruct((tok_dev, samples, tok_width), jnp.bfloat16),
        in_specs=[vmem, vmem, vmem, vmem, vmem, hbm, hbm, hbm],
        out_specs=vmem,
        scratch_shapes=[
            pltpu.VMEM(w_key.shape, w_key.dtype),
            pltpu.VMEM(w_value.shape, w_value.dtype),
            pltpu.VMEM(w_out.shape, w_out.dtype),
            pltpu.SemaphoreType.DMA((3,)),
        ],
        cost_estimate=pl.CostEstimate(
            flops=2 * samples * tok_width * (
                2 * count * tok_width + 2 * tok_dev * tok_width + 2 * TOKEN_HEADS * tok_dev * count
            ),
            transcendentals=samples * TOKEN_HEADS * tok_dev * count,
            bytes_accessed=2 * 4 * tok_width * tok_width
            + 2 * samples * (count + 2 * tok_dev) * tok_width
            + 4 * TOKEN_HEADS * tok_dev * count,
        ),
    )(
        every,
        state_t,
        query_t,
        bias,
        key_mask[None, :],
        w_key,
        w_value,
        w_out,
    )
    return (atom_out, token_out)


def solution(mesh):
    return jax.shard_map(
        on_device,
        mesh=mesh,
        in_specs=(
            P(("groups", "row"), None, None),
            P(("groups", "row")),
            P("groups"),
            P(("groups", "row"), None, None),
            P(("groups", "row"), None, None),
            P("groups"),
            P(),
            P(),
            P(),
            P(),
            P(),
            P(),
            P(),
            P(),
            P(),
            P(),
        ),
        out_specs=(P(("groups", "row"), None, None), P(("groups", "row"), None, None)),
        check_vma=False,
    )
```

```python
import functools
import math

import jax
import jax.numpy as jnp
from jax import lax
from jax.experimental import pallas as pl
from jax.experimental.pallas import tpu as pltpu
from jax.sharding import PartitionSpec as P

ATOM_HEADS = 4
QBLOCK = 32
KWIN = 128
SHIFT = 16
TOKEN_HEADS = 16


def layer_norm(values):
    values = values.astype(jnp.float32)
    mean = jnp.mean(values, axis=-1, keepdims=True)
    var = jnp.mean((values - mean) ** 2, axis=-1, keepdims=True)
    return (values - mean) / jnp.sqrt(var + 1e-05)


def project(values, weight):
    return jnp.einsum("asc,cd->asd", values, weight, preferred_element_type=jnp.float32)


def shifted(block, axis, step):
    count = lax.axis_size(axis)
    route = [(i, i + step) for i in range(count) if 0 <= i + step < count]
    return lax.ppermute(block, axis, route)


def atom_kernel(
    own_ref,
    low_ref,
    upper_ref,
    shift_ref,
    next_ref,
    wq_ref,
    wk_ref,
    wv_ref,
    wo_ref,
    wt_ref,
    ids_ref,
    token_ref,
    wq_hbm,
    atom_ref,
    state_ref,
    query_ref,
    wtq_ref,
    sems,
    *,
    atom_dev,
    rows,
    low_rows,
    high_rows,
    head_dim,
    devices,
):
    f32, bf16 = jnp.float32, jnp.bfloat16
    copies = [pltpu.make_async_copy(wq_hbm, wtq_ref, sems.at[0])]
    for copy in copies:
        copy.start()
    _, samples, width = own_ref.shape
    ext_rows = low_rows + atom_dev + high_rows
    lane = lax.broadcasted_iota(jnp.int32, (1, width), 1) // head_dim
    head_masks = [(lane == h).astype(f32) for h in range(ATOM_HEADS)]
    root = jnp.float32(math.sqrt(head_dim))
    rank = lax.axis_index("row")
    base = rank * atom_dev
    total = devices * atom_dev
    tok_dev = token_ref.shape[0]
    row_block = lax.broadcasted_iota(jnp.int32, (rows, 1), 0) // QBLOCK
    shift = jnp.where(row_block == rows // QBLOCK - 1, next_ref[0], 0)
    for j in range(rows // QBLOCK - 1):
        shift = shift + jnp.where(row_block == j, shift_ref[j], 0)
    first = row_block * QBLOCK + SHIFT + shift
    lo = jnp.maximum(first, low_rows - base)
    hi = jnp.minimum(first + KWIN, total - base + low_rows)
    column = lax.broadcasted_iota(jnp.int32, (rows, ext_rows), 1)
    keep = (column >= lo) & (column < hi)
    own_start = pl.multiple_of(base, atom_dev)
    next_start = pl.multiple_of(jnp.minimum(base + atom_dev, total - atom_dev), atom_dev)
    next_ids = ids_ref[:, pl.ds(next_start, atom_dev)][:, 0 : rows - atom_dev]
    next_ids = jnp.where(rank < devices - 1, next_ids, -1)
    row_ids = jnp.concatenate([ids_ref[:, pl.ds(own_start, atom_dev)], next_ids], axis=1)
    own_ids = rank * tok_dev + lax.broadcasted_iota(jnp.int32, (tok_dev, 1), 0)
    onehot = (own_ids == row_ids).astype(f32)
    counts = jnp.sum(onehot, axis=1, keepdims=True)
    onehot = onehot.astype(bf16)
    xs, xns = [], []
    for s in range(samples):
        x = jnp.concatenate(
            [
                low_ref[atom_dev - low_rows : atom_dev, s, :],
                own_ref[:, s, :],
                upper_ref[0:high_rows, s, :],
            ],
            axis=0,
        ).astype(f32)
        mean = jnp.mean(x, axis=-1, keepdims=True)
        var = jnp.mean((x - mean) ** 2, axis=-1, keepdims=True)
        xs.append(x)
        xns.append(((x - mean) / jnp.sqrt(var + 1e-05)).astype(bf16))
    xn_all = jnp.concatenate(xns, axis=0)
    q_all = jnp.dot(
        jnp.concatenate([xn[low_rows : low_rows + rows] for xn in xns], axis=0),
        wq_ref[...],
        preferred_element_type=f32,
    ).astype(bf16)
    k_all = jnp.dot(xn_all, wk_ref[...], preferred_element_type=f32).astype(bf16)
    v_all = jnp.dot(xn_all, wv_ref[...], preferred_element_type=f32).astype(bf16)
    mixed = []
    for s in range(samples):
        q = q_all[s * rows : (s + 1) * rows]
        k = k_all[s * ext_rows : (s + 1) * ext_rows]
        v = v_all[s * ext_rows : (s + 1) * ext_rows]
        acc = jnp.zeros((rows, width), f32)
        for h in range(ATOM_HEADS):
            qh = q * head_masks[h].astype(bf16)
            sc = lax.dot_general(
                qh, k, (((1,), (1,)), ((), ())), preferred_element_type=f32
            ) / root
            sc = jnp.where(keep, sc, -1e30)
            top = jnp.max(sc, axis=-1, keepdims=True)
            e = jnp.where(keep, jnp.exp(sc - top), 0.0)
            tot = jnp.sum(e, axis=-1, keepdims=True)
            o = jnp.dot(e.astype(bf16), v, preferred_element_type=f32)
            acc = acc + (o / tot) * head_masks[h]
        mixed.append(acc.astype(bf16))
    base = jnp.concatenate([x[low_rows : low_rows + rows] for x in xs], axis=0)
    out = (
        base + jnp.dot(jnp.concatenate(mixed, axis=0), wo_ref[...], preferred_element_type=f32)
    ).astype(bf16)
    for s in range(samples):
        atom_ref[:, s, :] = out[s * rows : s * rows + atom_dev]
    hidden = jnp.maximum(jnp.dot(out, wt_ref[...], preferred_element_type=f32), 0.0)
    top_part = hidden.astype(bf16)
    rest = hidden - top_part.astype(f32)
    mid_part = rest.astype(bf16)
    low_part = (rest - mid_part.astype(f32)).astype(bf16)
    zero = jnp.zeros_like(onehot)
    diagonal = jnp.concatenate(
        [
            jnp.concatenate([onehot if c == r else zero for c in range(samples)], axis=1)
            for r in range(samples)
        ],
        axis=0,
    )
    sums = (
        jnp.dot(diagonal, top_part, preferred_element_type=f32)
        + jnp.dot(diagonal, mid_part, preferred_element_type=f32)
        + jnp.dot(diagonal, low_part, preferred_element_type=f32)
    )
    tns = []
    for s in range(samples):
        st = (token_ref[:, s, :].astype(f32) + sums[s * tok_dev : (s + 1) * tok_dev] / counts)
        st = st.astype(bf16)
        state_ref[s] = st
        st = st.astype(f32)
        mean = jnp.mean(st, axis=-1, keepdims=True)
        var = jnp.mean((st - mean) ** 2, axis=-1, keepdims=True)
        tns.append(((st - mean) / jnp.sqrt(var + 1e-05)).astype(bf16))
    copies[0].wait()
    query = jnp.dot(jnp.concatenate(tns, axis=0), wtq_ref[...], preferred_element_type=f32)
    query = query.astype(bf16)
    for s in range(samples):
        query_ref[s] = query[s * tok_dev : (s + 1) * tok_dev]


def token_kernel(
    every_ref,
    own_ref,
    query_ref,
    bias_ref,
    flags_ref,
    wk_hbm,
    wv_hbm,
    wo_hbm,
    out_ref,
    wk_ref,
    wv_ref,
    wo_ref,
    sems,
    *,
    heads,
):
    copies = [
        pltpu.make_async_copy(src, dst, sems.at[i])
        for i, (src, dst) in enumerate([(wk_hbm, wk_ref), (wv_hbm, wv_ref), (wo_hbm, wo_ref)])
    ]
    for copy in copies:
        copy.start()
    f32, bf16 = jnp.float32, jnp.bfloat16
    samples, tok_dev, width = own_ref.shape
    head_dim = width // heads
    lane = lax.broadcasted_iota(jnp.int32, (1, width), 1) // head_dim
    head_masks = [(lane == h).astype(f32) for h in range(heads)]
    root = jnp.float32(math.sqrt(head_dim))
    keep = flags_ref[...] > 0
    mask_rows = jnp.concatenate(head_masks, axis=0)

    def normed(x):
        mean = jnp.mean(x, axis=-1, keepdims=True)
        var = jnp.mean((x - mean) ** 2, axis=-1, keepdims=True)
        return ((x - mean) / jnp.sqrt(var + 1e-05)).astype(bf16)

    allx = jnp.concatenate([normed(every_ref[s].astype(f32)) for s in range(samples)], axis=0)
    count = every_ref.shape[1]
    copies[0].wait()
    k_all = jnp.dot(allx, wk_ref[...], preferred_element_type=f32).astype(bf16)
    copies[1].wait()
    v_all = jnp.dot(allx, wv_ref[...], preferred_element_type=f32).astype(bf16)
    ks = [k_all[s * count : (s + 1) * count] for s in range(samples)]
    vs = [v_all[s * count : (s + 1) * count] for s in range(samples)]
    bias = bias_ref[...]
    mixes = []
    for s in range(samples):
        q = query_ref[s]
        stacked = jnp.concatenate(
            [q[t : t + 1].astype(f32) * mask_rows for t in range(tok_dev)], axis=0
        ).astype(bf16)
        sc = lax.dot_general(
            stacked, ks[s], (((1,), (1,)), ((), ())), preferred_element_type=f32
        ) / root + bias
        sc = jnp.where(keep, sc, -1e30)
        top = jnp.max(sc, axis=-1, keepdims=True)
        e = jnp.where(keep, jnp.exp(sc - top), 0.0)
        tot = jnp.sum(e, axis=-1, keepdims=True)
        o = jnp.dot(e.astype(bf16), vs[s], preferred_element_type=f32) / tot
        mixes.append(
            jnp.concatenate(
                [
                    jnp.sum(o[t * heads : (t + 1) * heads] * mask_rows, axis=0, keepdims=True)
                    for t in range(tok_dev)
                ],
                axis=0,
            ).astype(bf16)
        )
    copies[2].wait()
    projected = jnp.dot(jnp.concatenate(mixes, axis=0), wo_ref[...], preferred_element_type=f32)
    for s in range(samples):
        own = own_ref[s].astype(f32)
        out_ref[:, s, :] = (own + projected[s * tok_dev : (s + 1) * tok_dev]).astype(bf16)


def on_device(
    atom_feat,
    window_shift,
    atom_token,
    token_in,
    pair,
    key_mask,
    w_atom_query,
    w_atom_key,
    w_atom_value,
    w_atom_out,
    w_to_token,
    w_query,
    w_key,
    w_value,
    w_out,
    w_bias,
):
    high = lax.Precision.HIGHEST
    atom_dev, samples, width = atom_feat.shape
    tok_dev = token_in.shape[0]
    tok_width = token_in.shape[2]
    devices = lax.axis_size("row")
    rank = lax.axis_index("row")
    atom_base = rank * atom_dev
    total_atoms = atom_dev * devices
    margin = (KWIN - QBLOCK) // 2
    low_rows = margin + SHIFT
    span = KWIN + 2 * SHIFT
    high_rows = span - low_rows
    blocks = atom_dev // QBLOCK + 1

    low = shifted(atom_feat, "row", 1)
    upper, next_shifts = shifted((atom_feat, window_shift), "row", -1)

    head_dim = width // ATOM_HEADS
    rows = blocks * QBLOCK
    ext_rows = low_rows + atom_dev + high_rows
    kernel = functools.partial(
        atom_kernel,
        atom_dev=atom_dev,
        rows=rows,
        low_rows=low_rows,
        high_rows=high_rows,
        head_dim=head_dim,
        devices=devices,
    )
    vmem = pl.BlockSpec(memory_space=pltpu.VMEM)
    flops = 2 * samples * (
        ext_rows * width * 3 * width
        + rows * width * (width + tok_width)
        + ATOM_HEADS * rows * ext_rows * width * 2
        + 3 * tok_dev * rows * tok_width
    )
    hbm = pl.BlockSpec(memory_space=pl.ANY)
    count = tok_dev * devices
    atom_out, state_t, query_t = pl.pallas_call(
        kernel,
        out_shape=(
            jax.ShapeDtypeStruct((atom_dev, samples, width), jnp.bfloat16),
            jax.ShapeDtypeStruct((samples, tok_dev, tok_width), jnp.bfloat16),
            jax.ShapeDtypeStruct((samples, tok_dev, tok_width), jnp.bfloat16),
        ),
        in_specs=[vmem] * 3
        + [pl.BlockSpec(memory_space=pltpu.SMEM)] * 2
        + [vmem] * 7
        + [hbm],
        out_specs=(vmem, vmem, vmem),
        scratch_shapes=[
            pltpu.VMEM(w_query.shape, w_query.dtype),
            pltpu.SemaphoreType.DMA((1,)),
        ],
        cost_estimate=pl.CostEstimate(
            flops=flops,
            transcendentals=samples * ATOM_HEADS * rows * ext_rows,
            bytes_accessed=2 * (ext_rows + atom_dev) * samples * width
            + 2 * width * (3 * width + width + tok_width)
            + 4 * samples * tok_dev * tok_width,
        ),
    )(
        atom_feat,
        low,
        upper,
        window_shift,
        next_shifts,
        w_atom_query,
        w_atom_key,
        w_atom_value,
        w_atom_out,
        w_to_token,
        atom_token[None, :],
        token_in,
        w_query,
    )
    bias = jnp.einsum("qkc,ch->qhk", pair, w_bias, preferred_element_type=jnp.float32)
    bias = bias.reshape(tok_dev * TOKEN_HEADS, count)

    every = lax.all_gather(state_t, "row", axis=1, tiled=True)
    token_out = pl.pallas_call(
        functools.partial(token_kernel, heads=TOKEN_HEADS),
        out_shape=jax.ShapeDtypeStruct((tok_dev, samples, tok_width), jnp.bfloat16),
        in_specs=[vmem, vmem, vmem, vmem, vmem, hbm, hbm, hbm],
        out_specs=vmem,
        scratch_shapes=[
            pltpu.VMEM(w_key.shape, w_key.dtype),
            pltpu.VMEM(w_value.shape, w_value.dtype),
            pltpu.VMEM(w_out.shape, w_out.dtype),
            pltpu.SemaphoreType.DMA((3,)),
        ],
        cost_estimate=pl.CostEstimate(
            flops=2 * samples * tok_width * (
                2 * count * tok_width + 2 * tok_dev * tok_width + 2 * TOKEN_HEADS * tok_dev * count
            ),
            transcendentals=samples * TOKEN_HEADS * tok_dev * count,
            bytes_accessed=2 * 4 * tok_width * tok_width
            + 2 * samples * (count + 2 * tok_dev) * tok_width
            + 4 * TOKEN_HEADS * tok_dev * count,
        ),
    )(
        every,
        state_t,
        query_t,
        bias,
        key_mask[None, :],
        w_key,
        w_value,
        w_out,
    )
    return (atom_out, token_out)


def solution(mesh):
    return jax.shard_map(
        on_device,
        mesh=mesh,
        in_specs=(
            P(("groups", "row"), None, None),
            P(("groups", "row")),
            P("groups"),
            P(("groups", "row"), None, None),
            P(("groups", "row"), None, None),
            P("groups"),
            P(),
            P(),
            P(),
            P(),
            P(),
            P(),
            P(),
            P(),
            P(),
            P(),
        ),
        out_specs=(P(("groups", "row"), None, None), P(("groups", "row"), None, None)),
        check_vma=False,
    )
```

```python
import functools
import math

import jax
import jax.numpy as jnp
from jax import lax
from jax.experimental import pallas as pl
from jax.experimental.pallas import tpu as pltpu
from jax.sharding import PartitionSpec as P

ATOM_HEADS = 4
QBLOCK = 32
KWIN = 128
SHIFT = 16
TOKEN_HEADS = 16


def layer_norm(values):
    values = values.astype(jnp.float32)
    mean = jnp.mean(values, axis=-1, keepdims=True)
    var = jnp.mean((values - mean) ** 2, axis=-1, keepdims=True)
    return (values - mean) / jnp.sqrt(var + 1e-05)


def project(values, weight):
    return jnp.einsum("asc,cd->asd", values, weight, preferred_element_type=jnp.float32)


def shifted(block, axis, step):
    count = lax.axis_size(axis)
    route = [(i, i + step) for i in range(count) if 0 <= i + step < count]
    return lax.ppermute(block, axis, route)


def atom_kernel(
    own_ref,
    low_ref,
    upper_ref,
    shift_ref,
    wq_ref,
    wk_ref,
    wv_ref,
    wo_ref,
    wt_ref,
    ids_ref,
    token_ref,
    wq_hbm,
    atom_ref,
    state_ref,
    query_ref,
    wtq_ref,
    sems,
    *,
    atom_dev,
    rows,
    low_rows,
    high_rows,
    head_dim,
    devices,
):
    f32, bf16 = jnp.float32, jnp.bfloat16
    copies = [pltpu.make_async_copy(wq_hbm, wtq_ref, sems.at[0])]
    for copy in copies:
        copy.start()
    _, samples, width = own_ref.shape
    ext_rows = low_rows + atom_dev + high_rows
    lane = lax.broadcasted_iota(jnp.int32, (1, width), 1) // head_dim
    head_masks = [(lane == h).astype(f32) for h in range(ATOM_HEADS)]
    root = jnp.float32(math.sqrt(head_dim))
    rank = lax.axis_index("row")
    base = rank * atom_dev
    total = devices * atom_dev
    tok_dev = token_ref.shape[0]
    row_block = lax.broadcasted_iota(jnp.int32, (rows, 1), 0) // QBLOCK
    next_shift = upper_ref[pl.ds(atom_dev, 1), 0, :].astype(f32)[:, 0:1].astype(jnp.int32)
    shift = jnp.where(row_block == rows // QBLOCK - 1, next_shift, 0)
    for j in range(rows // QBLOCK - 1):
        shift = shift + jnp.where(row_block == j, shift_ref[j], 0)
    first = row_block * QBLOCK + SHIFT + shift
    lo = jnp.maximum(first, low_rows - base)
    hi = jnp.minimum(first + KWIN, total - base + low_rows)
    column = lax.broadcasted_iota(jnp.int32, (rows, ext_rows), 1)
    keep = (column >= lo) & (column < hi)
    own_start = pl.multiple_of(base, atom_dev)
    next_start = pl.multiple_of(jnp.minimum(base + atom_dev, total - atom_dev), atom_dev)
    next_ids = ids_ref[:, pl.ds(next_start, atom_dev)][:, 0 : rows - atom_dev]
    next_ids = jnp.where(rank < devices - 1, next_ids, -1)
    row_ids = jnp.concatenate([ids_ref[:, pl.ds(own_start, atom_dev)], next_ids], axis=1)
    own_ids = rank * tok_dev + lax.broadcasted_iota(jnp.int32, (tok_dev, 1), 0)
    onehot = (own_ids == row_ids).astype(f32)
    counts = jnp.sum(onehot, axis=1, keepdims=True)
    onehot = onehot.astype(bf16)
    xs, xns = [], []
    for s in range(samples):
        x = jnp.concatenate(
            [
                low_ref[atom_dev - low_rows : atom_dev, s, :],
                own_ref[:, s, :],
                upper_ref[0:high_rows, s, :],
            ],
            axis=0,
        ).astype(f32)
        mean = jnp.mean(x, axis=-1, keepdims=True)
        var = jnp.mean((x - mean) ** 2, axis=-1, keepdims=True)
        xs.append(x)
        xns.append(((x - mean) / jnp.sqrt(var + 1e-05)).astype(bf16))
    xn_all = jnp.concatenate(xns, axis=0)
    q_all = jnp.dot(
        jnp.concatenate([xn[low_rows : low_rows + rows] for xn in xns], axis=0),
        wq_ref[...],
        preferred_element_type=f32,
    ).astype(bf16)
    k_all = jnp.dot(xn_all, wk_ref[...], preferred_element_type=f32).astype(bf16)
    v_all = jnp.dot(xn_all, wv_ref[...], preferred_element_type=f32).astype(bf16)
    mixed = []
    for s in range(samples):
        q = q_all[s * rows : (s + 1) * rows]
        k = k_all[s * ext_rows : (s + 1) * ext_rows]
        v = v_all[s * ext_rows : (s + 1) * ext_rows]
        acc = jnp.zeros((rows, width), f32)
        for h in range(ATOM_HEADS):
            qh = q * head_masks[h].astype(bf16)
            sc = lax.dot_general(
                qh, k, (((1,), (1,)), ((), ())), preferred_element_type=f32
            ) / root
            sc = jnp.where(keep, sc, -1e30)
            top = jnp.max(sc, axis=-1, keepdims=True)
            e = jnp.where(keep, jnp.exp(sc - top), 0.0)
            tot = jnp.sum(e, axis=-1, keepdims=True)
            o = jnp.dot(e.astype(bf16), v, preferred_element_type=f32)
            acc = acc + (o / tot) * head_masks[h]
        mixed.append(acc.astype(bf16))
    base = jnp.concatenate([x[low_rows : low_rows + rows] for x in xs], axis=0)
    out = (
        base + jnp.dot(jnp.concatenate(mixed, axis=0), wo_ref[...], preferred_element_type=f32)
    ).astype(bf16)
    for s in range(samples):
        atom_ref[:, s, :] = out[s * rows : s * rows + atom_dev]
    hidden = jnp.maximum(jnp.dot(out, wt_ref[...], preferred_element_type=f32), 0.0)
    top_part = hidden.astype(bf16)
    rest = hidden - top_part.astype(f32)
    mid_part = rest.astype(bf16)
    low_part = (rest - mid_part.astype(f32)).astype(bf16)
    zero = jnp.zeros_like(onehot)
    diagonal = jnp.concatenate(
        [
            jnp.concatenate([onehot if c == r else zero for c in range(samples)], axis=1)
            for r in range(samples)
        ],
        axis=0,
    )
    sums = (
        jnp.dot(diagonal, top_part, preferred_element_type=f32)
        + jnp.dot(diagonal, mid_part, preferred_element_type=f32)
        + jnp.dot(diagonal, low_part, preferred_element_type=f32)
    )
    tns = []
    for s in range(samples):
        st = (token_ref[:, s, :].astype(f32) + sums[s * tok_dev : (s + 1) * tok_dev] / counts)
        st = st.astype(bf16)
        state_ref[s] = st
        st = st.astype(f32)
        mean = jnp.mean(st, axis=-1, keepdims=True)
        var = jnp.mean((st - mean) ** 2, axis=-1, keepdims=True)
        tns.append(((st - mean) / jnp.sqrt(var + 1e-05)).astype(bf16))
    copies[0].wait()
    query = jnp.dot(jnp.concatenate(tns, axis=0), wtq_ref[...], preferred_element_type=f32)
    query = query.astype(bf16)
    for s in range(samples):
        query_ref[s] = query[s * tok_dev : (s + 1) * tok_dev]


def token_kernel(
    every_ref,
    own_ref,
    query_ref,
    bias_ref,
    flags_ref,
    wk_hbm,
    wv_hbm,
    wo_hbm,
    out_ref,
    wk_ref,
    wv_ref,
    wo_ref,
    sems,
    *,
    heads,
):
    copies = [
        pltpu.make_async_copy(src, dst, sems.at[i])
        for i, (src, dst) in enumerate([(wk_hbm, wk_ref), (wv_hbm, wv_ref), (wo_hbm, wo_ref)])
    ]
    for copy in copies:
        copy.start()
    f32, bf16 = jnp.float32, jnp.bfloat16
    samples, tok_dev, width = own_ref.shape
    head_dim = width // heads
    lane = lax.broadcasted_iota(jnp.int32, (1, width), 1) // head_dim
    head_masks = [(lane == h).astype(f32) for h in range(heads)]
    root = jnp.float32(math.sqrt(head_dim))
    keep = flags_ref[...] > 0
    mask_rows = jnp.concatenate(head_masks, axis=0)

    def normed(x):
        mean = jnp.mean(x, axis=-1, keepdims=True)
        var = jnp.mean((x - mean) ** 2, axis=-1, keepdims=True)
        return ((x - mean) / jnp.sqrt(var + 1e-05)).astype(bf16)

    allx = jnp.concatenate([normed(every_ref[s].astype(f32)) for s in range(samples)], axis=0)
    count = every_ref.shape[1]
    copies[0].wait()
    k_all = jnp.dot(allx, wk_ref[...], preferred_element_type=f32).astype(bf16)
    copies[1].wait()
    v_all = jnp.dot(allx, wv_ref[...], preferred_element_type=f32).astype(bf16)
    ks = [k_all[s * count : (s + 1) * count] for s in range(samples)]
    vs = [v_all[s * count : (s + 1) * count] for s in range(samples)]
    bias = bias_ref[...]
    mixes = []
    for s in range(samples):
        q = query_ref[s]
        stacked = jnp.concatenate(
            [q[t : t + 1].astype(f32) * mask_rows for t in range(tok_dev)], axis=0
        ).astype(bf16)
        sc = lax.dot_general(
            stacked, ks[s], (((1,), (1,)), ((), ())), preferred_element_type=f32
        ) / root + bias
        sc = jnp.where(keep, sc, -1e30)
        top = jnp.max(sc, axis=-1, keepdims=True)
        e = jnp.where(keep, jnp.exp(sc - top), 0.0)
        tot = jnp.sum(e, axis=-1, keepdims=True)
        o = jnp.dot(e.astype(bf16), vs[s], preferred_element_type=f32) / tot
        mixes.append(
            jnp.concatenate(
                [
                    jnp.sum(o[t * heads : (t + 1) * heads] * mask_rows, axis=0, keepdims=True)
                    for t in range(tok_dev)
                ],
                axis=0,
            ).astype(bf16)
        )
    copies[2].wait()
    projected = jnp.dot(jnp.concatenate(mixes, axis=0), wo_ref[...], preferred_element_type=f32)
    for s in range(samples):
        own = own_ref[s].astype(f32)
        out_ref[:, s, :] = (own + projected[s * tok_dev : (s + 1) * tok_dev]).astype(bf16)


def on_device(
    atom_feat,
    window_shift,
    atom_token,
    token_in,
    pair,
    key_mask,
    w_atom_query,
    w_atom_key,
    w_atom_value,
    w_atom_out,
    w_to_token,
    w_query,
    w_key,
    w_value,
    w_out,
    w_bias,
):
    high = lax.Precision.HIGHEST
    atom_dev, samples, width = atom_feat.shape
    tok_dev = token_in.shape[0]
    tok_width = token_in.shape[2]
    devices = lax.axis_size("row")
    rank = lax.axis_index("row")
    atom_base = rank * atom_dev
    total_atoms = atom_dev * devices
    margin = (KWIN - QBLOCK) // 2
    low_rows = margin + SHIFT
    span = KWIN + 2 * SHIFT
    high_rows = span - low_rows
    blocks = atom_dev // QBLOCK + 1

    low = shifted(atom_feat, "row", 1)
    shift_row = jnp.broadcast_to(window_shift[0], (1, samples, width)).astype(jnp.bfloat16)
    upper = shifted(jnp.concatenate([atom_feat, shift_row], axis=0), "row", -1)

    head_dim = width // ATOM_HEADS
    rows = blocks * QBLOCK
    ext_rows = low_rows + atom_dev + high_rows
    kernel = functools.partial(
        atom_kernel,
        atom_dev=atom_dev,
        rows=rows,
        low_rows=low_rows,
        high_rows=high_rows,
        head_dim=head_dim,
        devices=devices,
    )
    vmem = pl.BlockSpec(memory_space=pltpu.VMEM)
    flops = 2 * samples * (
        ext_rows * width * 3 * width
        + rows * width * (width + tok_width)
        + ATOM_HEADS * rows * ext_rows * width * 2
        + 3 * tok_dev * rows * tok_width
    )
    hbm = pl.BlockSpec(memory_space=pl.ANY)
    count = tok_dev * devices
    atom_out, state_t, query_t = pl.pallas_call(
        kernel,
        out_shape=(
            jax.ShapeDtypeStruct((atom_dev, samples, width), jnp.bfloat16),
            jax.ShapeDtypeStruct((samples, tok_dev, tok_width), jnp.bfloat16),
            jax.ShapeDtypeStruct((samples, tok_dev, tok_width), jnp.bfloat16),
        ),
        in_specs=[vmem] * 3
        + [pl.BlockSpec(memory_space=pltpu.SMEM)]
        + [vmem] * 7
        + [hbm],
        out_specs=(vmem, vmem, vmem),
        scratch_shapes=[
            pltpu.VMEM(w_query.shape, w_query.dtype),
            pltpu.SemaphoreType.DMA((1,)),
        ],
        cost_estimate=pl.CostEstimate(
            flops=flops,
            transcendentals=samples * ATOM_HEADS * rows * ext_rows,
            bytes_accessed=2 * (ext_rows + atom_dev) * samples * width
            + 2 * width * (3 * width + width + tok_width)
            + 4 * samples * tok_dev * tok_width,
        ),
    )(
        atom_feat,
        low,
        upper,
        window_shift,
        w_atom_query,
        w_atom_key,
        w_atom_value,
        w_atom_out,
        w_to_token,
        atom_token[None, :],
        token_in,
        w_query,
    )
    bias = jnp.einsum("qkc,ch->qhk", pair, w_bias, preferred_element_type=jnp.float32)
    bias = bias.reshape(tok_dev * TOKEN_HEADS, count)

    every = lax.all_gather(state_t, "row", axis=1, tiled=True)
    token_out = pl.pallas_call(
        functools.partial(token_kernel, heads=TOKEN_HEADS),
        out_shape=jax.ShapeDtypeStruct((tok_dev, samples, tok_width), jnp.bfloat16),
        in_specs=[vmem, vmem, vmem, vmem, vmem, hbm, hbm, hbm],
        out_specs=vmem,
        scratch_shapes=[
            pltpu.VMEM(w_key.shape, w_key.dtype),
            pltpu.VMEM(w_value.shape, w_value.dtype),
            pltpu.VMEM(w_out.shape, w_out.dtype),
            pltpu.SemaphoreType.DMA((3,)),
        ],
        cost_estimate=pl.CostEstimate(
            flops=2 * samples * tok_width * (
                2 * count * tok_width + 2 * tok_dev * tok_width + 2 * TOKEN_HEADS * tok_dev * count
            ),
            transcendentals=samples * TOKEN_HEADS * tok_dev * count,
            bytes_accessed=2 * 4 * tok_width * tok_width
            + 2 * samples * (count + 2 * tok_dev) * tok_width
            + 4 * TOKEN_HEADS * tok_dev * count,
        ),
    )(
        every,
        state_t,
        query_t,
        bias,
        key_mask[None, :],
        w_key,
        w_value,
        w_out,
    )
    return (atom_out, token_out)


def solution(mesh):
    return jax.shard_map(
        on_device,
        mesh=mesh,
        in_specs=(
            P(("groups", "row"), None, None),
            P(("groups", "row")),
            P("groups"),
            P(("groups", "row"), None, None),
            P(("groups", "row"), None, None),
            P("groups"),
            P(),
            P(),
            P(),
            P(),
            P(),
            P(),
            P(),
            P(),
            P(),
            P(),
        ),
        out_specs=(P(("groups", "row"), None, None), P(("groups", "row"), None, None)),
        check_vma=False,
    )
```

```python
import functools
import math

import jax
import jax.numpy as jnp
from jax import lax
from jax.experimental import pallas as pl
from jax.experimental.pallas import tpu as pltpu
from jax.sharding import PartitionSpec as P

ATOM_HEADS = 4
QBLOCK = 32
KWIN = 128
SHIFT = 16
TOKEN_HEADS = 16


def layer_norm(values):
    values = values.astype(jnp.float32)
    mean = jnp.mean(values, axis=-1, keepdims=True)
    var = jnp.mean((values - mean) ** 2, axis=-1, keepdims=True)
    return (values - mean) / jnp.sqrt(var + 1e-05)


def project(values, weight):
    return jnp.einsum("asc,cd->asd", values, weight, preferred_element_type=jnp.float32)


def shifted(block, axis, step):
    count = lax.axis_size(axis)
    route = [(i, i + step) for i in range(count) if 0 <= i + step < count]
    return lax.ppermute(block, axis, route)


def atom_kernel(
    own_ref,
    low_ref,
    upper_ref,
    shift_ref,
    wq_ref,
    wk_ref,
    wv_ref,
    wo_ref,
    wt_ref,
    ids_ref,
    token_ref,
    wq_hbm,
    atom_ref,
    state_ref,
    query_ref,
    wtq_ref,
    sems,
    *,
    atom_dev,
    rows,
    low_rows,
    high_rows,
    head_dim,
    devices,
):
    f32, bf16 = jnp.float32, jnp.bfloat16
    copies = [pltpu.make_async_copy(wq_hbm, wtq_ref, sems.at[0])]
    for copy in copies:
        copy.start()
    _, samples, width = own_ref.shape
    ext_rows = low_rows + atom_dev + high_rows
    lane = lax.broadcasted_iota(jnp.int32, (1, width), 1) // head_dim
    head_masks = [(lane == h).astype(f32) for h in range(ATOM_HEADS)]
    root = jnp.float32(math.sqrt(head_dim))
    rank = lax.axis_index("row")
    base = rank * atom_dev
    total = devices * atom_dev
    tok_dev = token_ref.shape[0]
    row_block = lax.broadcasted_iota(jnp.int32, (rows, 1), 0) // QBLOCK
    next_shift = upper_ref[pl.ds(atom_dev, 1), 0, :].astype(f32)[:, 0:1].astype(jnp.int32)
    shift = jnp.where(row_block == rows // QBLOCK - 1, next_shift, 0)
    for j in range(rows // QBLOCK - 1):
        shift = shift + jnp.where(row_block == j, shift_ref[j], 0)
    first = row_block * QBLOCK + SHIFT + shift
    lo = jnp.maximum(first, low_rows - base)
    hi = jnp.minimum(first + KWIN, total - base + low_rows)
    column = lax.broadcasted_iota(jnp.int32, (rows, ext_rows), 1)
    keep = (column >= lo) & (column < hi)
    own_start = pl.multiple_of(base, atom_dev)
    next_start = pl.multiple_of(jnp.minimum(base + atom_dev, total - atom_dev), atom_dev)
    next_ids = ids_ref[:, pl.ds(next_start, atom_dev)][:, 0 : rows - atom_dev]
    next_ids = jnp.where(rank < devices - 1, next_ids, -1)
    row_ids = jnp.concatenate([ids_ref[:, pl.ds(own_start, atom_dev)], next_ids], axis=1)
    own_ids = rank * tok_dev + lax.broadcasted_iota(jnp.int32, (tok_dev, 1), 0)
    onehot = (own_ids == row_ids).astype(f32)
    counts = jnp.sum(onehot, axis=1, keepdims=True)
    onehot = onehot.astype(bf16)
    xs, xns = [], []
    for s in range(samples):
        x = jnp.concatenate(
            [
                low_ref[atom_dev - low_rows : atom_dev, s, :],
                own_ref[:, s, :],
                upper_ref[0:high_rows, s, :],
            ],
            axis=0,
        ).astype(f32)
        mean = jnp.mean(x, axis=-1, keepdims=True)
        var = jnp.mean((x - mean) ** 2, axis=-1, keepdims=True)
        xs.append(x)
        xns.append(((x - mean) / jnp.sqrt(var + 1e-05)).astype(bf16))
    xn_all = jnp.concatenate(xns, axis=0)
    q_all = jnp.dot(
        jnp.concatenate([xn[low_rows : low_rows + rows] for xn in xns], axis=0),
        wq_ref[...],
        preferred_element_type=f32,
    ).astype(bf16)
    k_all = jnp.dot(xn_all, wk_ref[...], preferred_element_type=f32).astype(bf16)
    v_all = jnp.dot(xn_all, wv_ref[...], preferred_element_type=f32).astype(bf16)
    mixed = []
    for s in range(samples):
        q = q_all[s * rows : (s + 1) * rows]
        k = k_all[s * ext_rows : (s + 1) * ext_rows]
        v = v_all[s * ext_rows : (s + 1) * ext_rows]
        acc = jnp.zeros((rows, width), f32)
        for h in range(ATOM_HEADS):
            qh = q * head_masks[h].astype(bf16)
            sc = lax.dot_general(
                qh, k, (((1,), (1,)), ((), ())), preferred_element_type=f32
            ) / root
            sc = jnp.where(keep, sc, -1e30)
            top = jnp.max(sc, axis=-1, keepdims=True)
            e = jnp.where(keep, jnp.exp(sc - top), 0.0)
            tot = jnp.sum(e, axis=-1, keepdims=True)
            o = jnp.dot(e.astype(bf16), v, preferred_element_type=f32)
            acc = acc + (o / tot) * head_masks[h]
        mixed.append(acc.astype(bf16))
    base = jnp.concatenate([x[low_rows : low_rows + rows] for x in xs], axis=0)
    out = (
        base + jnp.dot(jnp.concatenate(mixed, axis=0), wo_ref[...], preferred_element_type=f32)
    ).astype(bf16)
    for s in range(samples):
        atom_ref[:, s, :] = out[s * rows : s * rows + atom_dev]
    hidden = jnp.maximum(jnp.dot(out, wt_ref[...], preferred_element_type=f32), 0.0)
    top_part = hidden.astype(bf16)
    rest = hidden - top_part.astype(f32)
    mid_part = rest.astype(bf16)
    low_part = (rest - mid_part.astype(f32)).astype(bf16)
    zero = jnp.zeros_like(onehot)
    diagonal = jnp.concatenate(
        [
            jnp.concatenate([onehot if c == r else zero for c in range(samples)], axis=1)
            for r in range(samples)
        ],
        axis=0,
    )
    sums = (
        jnp.dot(diagonal, top_part, preferred_element_type=f32)
        + jnp.dot(diagonal, mid_part, preferred_element_type=f32)
        + jnp.dot(diagonal, low_part, preferred_element_type=f32)
    )
    tns = []
    for s in range(samples):
        st = (token_ref[:, s, :].astype(f32) + sums[s * tok_dev : (s + 1) * tok_dev] / counts)
        st = st.astype(bf16)
        state_ref[s] = st
        st = st.astype(f32)
        mean = jnp.mean(st, axis=-1, keepdims=True)
        var = jnp.mean((st - mean) ** 2, axis=-1, keepdims=True)
        tns.append(((st - mean) / jnp.sqrt(var + 1e-05)).astype(bf16))
    copies[0].wait()
    query = jnp.dot(jnp.concatenate(tns, axis=0), wtq_ref[...], preferred_element_type=f32)
    query = query.astype(bf16)
    for s in range(samples):
        query_ref[s] = query[s * tok_dev : (s + 1) * tok_dev]


def token_kernel(
    every_ref,
    own_ref,
    query_ref,
    bias_ref,
    flags_ref,
    wk_hbm,
    wv_hbm,
    wo_hbm,
    out_ref,
    wk_ref,
    wv_ref,
    wo_ref,
    sems,
    *,
    heads,
):
    copies = [
        pltpu.make_async_copy(src, dst, sems.at[i])
        for i, (src, dst) in enumerate([(wk_hbm, wk_ref), (wv_hbm, wv_ref), (wo_hbm, wo_ref)])
    ]
    copies[0].start()
    f32, bf16 = jnp.float32, jnp.bfloat16
    samples, tok_dev, width = own_ref.shape
    head_dim = width // heads
    lane = lax.broadcasted_iota(jnp.int32, (1, width), 1) // head_dim
    head_masks = [(lane == h).astype(f32) for h in range(heads)]
    root = jnp.float32(math.sqrt(head_dim))
    keep = flags_ref[...] > 0
    mask_rows = jnp.concatenate(head_masks, axis=0)

    def normed(x):
        mean = jnp.mean(x, axis=-1, keepdims=True)
        var = jnp.mean((x - mean) ** 2, axis=-1, keepdims=True)
        return ((x - mean) / jnp.sqrt(var + 1e-05)).astype(bf16)

    allx = jnp.concatenate([normed(every_ref[s].astype(f32)) for s in range(samples)], axis=0)
    count = every_ref.shape[1]
    copies[0].wait()
    copies[1].start()
    k_all = jnp.dot(allx, wk_ref[...], preferred_element_type=f32).astype(bf16)
    copies[1].wait()
    copies[2].start()
    v_all = jnp.dot(allx, wv_ref[...], preferred_element_type=f32).astype(bf16)
    ks = [k_all[s * count : (s + 1) * count] for s in range(samples)]
    vs = [v_all[s * count : (s + 1) * count] for s in range(samples)]
    bias = bias_ref[...]
    mixes = []
    for s in range(samples):
        q = query_ref[s]
        stacked = jnp.concatenate(
            [q[t : t + 1].astype(f32) * mask_rows for t in range(tok_dev)], axis=0
        ).astype(bf16)
        sc = lax.dot_general(
            stacked, ks[s], (((1,), (1,)), ((), ())), preferred_element_type=f32
        ) / root + bias
        sc = jnp.where(keep, sc, -1e30)
        top = jnp.max(sc, axis=-1, keepdims=True)
        e = jnp.where(keep, jnp.exp(sc - top), 0.0)
        tot = jnp.sum(e, axis=-1, keepdims=True)
        o = jnp.dot(e.astype(bf16), vs[s], preferred_element_type=f32) / tot
        mixes.append(
            jnp.concatenate(
                [
                    jnp.sum(o[t * heads : (t + 1) * heads] * mask_rows, axis=0, keepdims=True)
                    for t in range(tok_dev)
                ],
                axis=0,
            ).astype(bf16)
        )
    copies[2].wait()
    projected = jnp.dot(jnp.concatenate(mixes, axis=0), wo_ref[...], preferred_element_type=f32)
    for s in range(samples):
        own = own_ref[s].astype(f32)
        out_ref[:, s, :] = (own + projected[s * tok_dev : (s + 1) * tok_dev]).astype(bf16)


def on_device(
    atom_feat,
    window_shift,
    atom_token,
    token_in,
    pair,
    key_mask,
    w_atom_query,
    w_atom_key,
    w_atom_value,
    w_atom_out,
    w_to_token,
    w_query,
    w_key,
    w_value,
    w_out,
    w_bias,
):
    high = lax.Precision.HIGHEST
    atom_dev, samples, width = atom_feat.shape
    tok_dev = token_in.shape[0]
    tok_width = token_in.shape[2]
    devices = lax.axis_size("row")
    rank = lax.axis_index("row")
    atom_base = rank * atom_dev
    total_atoms = atom_dev * devices
    margin = (KWIN - QBLOCK) // 2
    low_rows = margin + SHIFT
    span = KWIN + 2 * SHIFT
    high_rows = span - low_rows
    blocks = atom_dev // QBLOCK + 1

    low = shifted(atom_feat, "row", 1)
    shift_row = jnp.broadcast_to(window_shift[0], (1, samples, width)).astype(jnp.bfloat16)
    upper = shifted(jnp.concatenate([atom_feat, shift_row], axis=0), "row", -1)

    head_dim = width // ATOM_HEADS
    rows = blocks * QBLOCK
    ext_rows = low_rows + atom_dev + high_rows
    kernel = functools.partial(
        atom_kernel,
        atom_dev=atom_dev,
        rows=rows,
        low_rows=low_rows,
        high_rows=high_rows,
        head_dim=head_dim,
        devices=devices,
    )
    vmem = pl.BlockSpec(memory_space=pltpu.VMEM)
    flops = 2 * samples * (
        ext_rows * width * 3 * width
        + rows * width * (width + tok_width)
        + ATOM_HEADS * rows * ext_rows * width * 2
        + 3 * tok_dev * rows * tok_width
    )
    hbm = pl.BlockSpec(memory_space=pl.ANY)
    count = tok_dev * devices
    atom_out, state_t, query_t = pl.pallas_call(
        kernel,
        out_shape=(
            jax.ShapeDtypeStruct((atom_dev, samples, width), jnp.bfloat16),
            jax.ShapeDtypeStruct((samples, tok_dev, tok_width), jnp.bfloat16),
            jax.ShapeDtypeStruct((samples, tok_dev, tok_width), jnp.bfloat16),
        ),
        in_specs=[vmem] * 3
        + [pl.BlockSpec(memory_space=pltpu.SMEM)]
        + [vmem] * 7
        + [hbm],
        out_specs=(vmem, vmem, vmem),
        scratch_shapes=[
            pltpu.VMEM(w_query.shape, w_query.dtype),
            pltpu.SemaphoreType.DMA((1,)),
        ],
        cost_estimate=pl.CostEstimate(
            flops=flops,
            transcendentals=samples * ATOM_HEADS * rows * ext_rows,
            bytes_accessed=2 * (ext_rows + atom_dev) * samples * width
            + 2 * width * (3 * width + width + tok_width)
            + 4 * samples * tok_dev * tok_width,
        ),
    )(
        atom_feat,
        low,
        upper,
        window_shift,
        w_atom_query,
        w_atom_key,
        w_atom_value,
        w_atom_out,
        w_to_token,
        atom_token[None, :],
        token_in,
        w_query,
    )
    bias = jnp.einsum("qkc,ch->qhk", pair, w_bias, preferred_element_type=jnp.float32)
    bias = bias.reshape(tok_dev * TOKEN_HEADS, count)

    every = lax.all_gather(state_t, "row", axis=1, tiled=True)
    token_out = pl.pallas_call(
        functools.partial(token_kernel, heads=TOKEN_HEADS),
        out_shape=jax.ShapeDtypeStruct((tok_dev, samples, tok_width), jnp.bfloat16),
        in_specs=[vmem, vmem, vmem, vmem, vmem, hbm, hbm, hbm],
        out_specs=vmem,
        scratch_shapes=[
            pltpu.VMEM(w_key.shape, w_key.dtype),
            pltpu.VMEM(w_value.shape, w_value.dtype),
            pltpu.VMEM(w_out.shape, w_out.dtype),
            pltpu.SemaphoreType.DMA((3,)),
        ],
        cost_estimate=pl.CostEstimate(
            flops=2 * samples * tok_width * (
                2 * count * tok_width + 2 * tok_dev * tok_width + 2 * TOKEN_HEADS * tok_dev * count
            ),
            transcendentals=samples * TOKEN_HEADS * tok_dev * count,
            bytes_accessed=2 * 4 * tok_width * tok_width
            + 2 * samples * (count + 2 * tok_dev) * tok_width
            + 4 * TOKEN_HEADS * tok_dev * count,
        ),
    )(
        every,
        state_t,
        query_t,
        bias,
        key_mask[None, :],
        w_key,
        w_value,
        w_out,
    )
    return (atom_out, token_out)


def solution(mesh):
    return jax.shard_map(
        on_device,
        mesh=mesh,
        in_specs=(
            P(("groups", "row"), None, None),
            P(("groups", "row")),
            P("groups"),
            P(("groups", "row"), None, None),
            P(("groups", "row"), None, None),
            P("groups"),
            P(),
            P(),
            P(),
            P(),
            P(),
            P(),
            P(),
            P(),
            P(),
            P(),
        ),
        out_specs=(P(("groups", "row"), None, None), P(("groups", "row"), None, None)),
        check_vma=False,
    )
```

```python
import functools
import math

import jax
import jax.numpy as jnp
from jax import lax
from jax.experimental import pallas as pl
from jax.experimental.pallas import tpu as pltpu
from jax.sharding import PartitionSpec as P

ATOM_HEADS = 4
QBLOCK = 32
KWIN = 128
SHIFT = 16
TOKEN_HEADS = 16


def layer_norm(values):
    values = values.astype(jnp.float32)
    mean = jnp.mean(values, axis=-1, keepdims=True)
    var = jnp.mean((values - mean) ** 2, axis=-1, keepdims=True)
    return (values - mean) / jnp.sqrt(var + 1e-05)


def project(values, weight):
    return jnp.einsum("asc,cd->asd", values, weight, preferred_element_type=jnp.float32)


def shifted(block, axis, step):
    count = lax.axis_size(axis)
    route = [(i, i + step) for i in range(count) if 0 <= i + step < count]
    return lax.ppermute(block, axis, route)


def atom_kernel(
    own_ref,
    low_ref,
    upper_ref,
    shift_ref,
    wq_ref,
    wk_ref,
    wv_ref,
    wo_ref,
    wt_ref,
    ids_ref,
    token_ref,
    wq_hbm,
    atom_ref,
    state_ref,
    query_ref,
    wtq_ref,
    sems,
    *,
    atom_dev,
    rows,
    low_rows,
    high_rows,
    head_dim,
    devices,
):
    f32, bf16 = jnp.float32, jnp.bfloat16
    copies = [pltpu.make_async_copy(wq_hbm, wtq_ref, sems.at[0])]
    for copy in copies:
        copy.start()
    _, samples, width = own_ref.shape
    ext_rows = low_rows + atom_dev + high_rows
    lane = lax.broadcasted_iota(jnp.int32, (1, width), 1) // head_dim
    head_masks = [(lane == h).astype(f32) for h in range(ATOM_HEADS)]
    root = jnp.float32(math.sqrt(head_dim))
    rank = lax.axis_index("row")
    base = rank * atom_dev
    total = devices * atom_dev
    tok_dev = token_ref.shape[0]
    row_block = lax.broadcasted_iota(jnp.int32, (rows, 1), 0) // QBLOCK
    next_shift = upper_ref[pl.ds(atom_dev, 1), 0, :].astype(f32)[:, 0:1].astype(jnp.int32)
    shift = jnp.where(row_block == rows // QBLOCK - 1, next_shift, 0)
    for j in range(rows // QBLOCK - 1):
        shift = shift + jnp.where(row_block == j, shift_ref[j], 0)
    first = row_block * QBLOCK + SHIFT + shift
    lo = jnp.maximum(first, low_rows - base)
    hi = jnp.minimum(first + KWIN, total - base + low_rows)
    column = lax.broadcasted_iota(jnp.int32, (rows, ext_rows), 1)
    keep = (column >= lo) & (column < hi)
    own_start = pl.multiple_of(base, atom_dev)
    next_start = pl.multiple_of(jnp.minimum(base + atom_dev, total - atom_dev), atom_dev)
    next_ids = ids_ref[:, pl.ds(next_start, atom_dev)][:, 0 : rows - atom_dev]
    next_ids = jnp.where(rank < devices - 1, next_ids, -1)
    row_ids = jnp.concatenate([ids_ref[:, pl.ds(own_start, atom_dev)], next_ids], axis=1)
    own_ids = rank * tok_dev + lax.broadcasted_iota(jnp.int32, (tok_dev, 1), 0)
    onehot = (own_ids == row_ids).astype(f32)
    counts = jnp.sum(onehot, axis=1, keepdims=True)
    onehot = onehot.astype(bf16)
    xs, xns = [], []
    for s in range(samples):
        x = jnp.concatenate(
            [
                low_ref[atom_dev - low_rows : atom_dev, s, :],
                own_ref[:, s, :],
                upper_ref[0:high_rows, s, :],
            ],
            axis=0,
        ).astype(f32)
        mean = jnp.mean(x, axis=-1, keepdims=True)
        var = jnp.mean((x - mean) ** 2, axis=-1, keepdims=True)
        xs.append(x)
        xns.append(((x - mean) / jnp.sqrt(var + 1e-05)).astype(bf16))
    xn_all = jnp.concatenate(xns, axis=0)
    q_all = jnp.dot(
        jnp.concatenate([xn[low_rows : low_rows + rows] for xn in xns], axis=0),
        wq_ref[...],
        preferred_element_type=f32,
    ).astype(bf16)
    k_all = jnp.dot(xn_all, wk_ref[...], preferred_element_type=f32).astype(bf16)
    v_all = jnp.dot(xn_all, wv_ref[...], preferred_element_type=f32).astype(bf16)
    mixed = []
    for s in range(samples):
        q = q_all[s * rows : (s + 1) * rows]
        k = k_all[s * ext_rows : (s + 1) * ext_rows]
        v = v_all[s * ext_rows : (s + 1) * ext_rows]
        acc = jnp.zeros((rows, width), f32)
        for h in range(ATOM_HEADS):
            qh = q * head_masks[h].astype(bf16)
            sc = lax.dot_general(
                qh, k, (((1,), (1,)), ((), ())), preferred_element_type=f32
            ) / root
            sc = jnp.where(keep, sc, -1e30)
            top = jnp.max(sc, axis=-1, keepdims=True)
            e = jnp.where(keep, jnp.exp(sc - top), 0.0)
            tot = jnp.sum(e, axis=-1, keepdims=True)
            o = jnp.dot(e.astype(bf16), v, preferred_element_type=f32)
            acc = acc + (o / tot) * head_masks[h]
        mixed.append(acc.astype(bf16))
    base = jnp.concatenate([x[low_rows : low_rows + rows] for x in xs], axis=0)
    out = (
        base + jnp.dot(jnp.concatenate(mixed, axis=0), wo_ref[...], preferred_element_type=f32)
    ).astype(bf16)
    for s in range(samples):
        atom_ref[:, s, :] = out[s * rows : s * rows + atom_dev]
    hidden = jnp.maximum(jnp.dot(out, wt_ref[...], preferred_element_type=f32), 0.0)
    top_part = hidden.astype(bf16)
    rest = hidden - top_part.astype(f32)
    mid_part = rest.astype(bf16)
    low_part = (rest - mid_part.astype(f32)).astype(bf16)
    zero = jnp.zeros_like(onehot)
    diagonal = jnp.concatenate(
        [
            jnp.concatenate([onehot if c == r else zero for c in range(samples)], axis=1)
            for r in range(samples)
        ],
        axis=0,
    )
    sums = (
        jnp.dot(diagonal, top_part, preferred_element_type=f32)
        + jnp.dot(diagonal, mid_part, preferred_element_type=f32)
        + jnp.dot(diagonal, low_part, preferred_element_type=f32)
    )
    tns = []
    for s in range(samples):
        st = (token_ref[:, s, :].astype(f32) + sums[s * tok_dev : (s + 1) * tok_dev] / counts)
        st = st.astype(bf16)
        state_ref[s] = st
        st = st.astype(f32)
        mean = jnp.mean(st, axis=-1, keepdims=True)
        var = jnp.mean((st - mean) ** 2, axis=-1, keepdims=True)
        tns.append(((st - mean) / jnp.sqrt(var + 1e-05)).astype(bf16))
    copies[0].wait()
    query = jnp.dot(jnp.concatenate(tns, axis=0), wtq_ref[...], preferred_element_type=f32)
    query = query.astype(bf16)
    for s in range(samples):
        query_ref[s] = query[s * tok_dev : (s + 1) * tok_dev]


def token_kernel(
    every_hbm,
    own_ref,
    query_ref,
    bias_ref,
    flags_ref,
    wk_hbm,
    wv_hbm,
    wo_hbm,
    out_ref,
    every_ref,
    wk_ref,
    wv_ref,
    wo_ref,
    sems,
    *,
    heads,
    pieces,
):
    samples = every_ref.shape[0]
    step = wk_ref.shape[0] // pieces
    groups = [[(every_hbm.at[s], every_ref.at[s])] for s in range(samples)]
    for w_hbm, w_ref in ((wk_hbm, wk_ref), (wv_hbm, wv_ref), (wo_hbm, wo_ref)):
        groups.append(
            [(w_hbm.at[pl.ds(c * step, step)], w_ref.at[pl.ds(c * step, step)]) for c in range(pieces)]
        )
    copies, index = [], 0
    for group in groups:
        made = []
        for src, dst in group:
            made.append(pltpu.make_async_copy(src, dst, sems.at[index]))
            index += 1
        copies.append(made)
    for group in copies:
        for copy in group:
            copy.start()

    def arrived(group):
        for copy in copies[group]:
            copy.wait()

    f32, bf16 = jnp.float32, jnp.bfloat16
    samples, tok_dev, width = own_ref.shape
    head_dim = width // heads
    lane = lax.broadcasted_iota(jnp.int32, (1, width), 1) // head_dim
    head_masks = [(lane == h).astype(f32) for h in range(heads)]
    root = jnp.float32(math.sqrt(head_dim))
    keep = flags_ref[...] > 0
    mask_rows = jnp.concatenate(head_masks, axis=0)

    def normed(x):
        mean = jnp.mean(x, axis=-1, keepdims=True)
        var = jnp.mean((x - mean) ** 2, axis=-1, keepdims=True)
        return ((x - mean) / jnp.sqrt(var + 1e-05)).astype(bf16)

    normal = []
    for s in range(samples):
        arrived(s)
        normal.append(normed(every_ref[s].astype(f32)))
    allx = jnp.concatenate(normal, axis=0)
    count = every_ref.shape[1]
    arrived(samples)
    k_all = jnp.dot(allx, wk_ref[...], preferred_element_type=f32).astype(bf16)
    arrived(samples + 1)
    v_all = jnp.dot(allx, wv_ref[...], preferred_element_type=f32).astype(bf16)
    ks = [k_all[s * count : (s + 1) * count] for s in range(samples)]
    vs = [v_all[s * count : (s + 1) * count] for s in range(samples)]
    bias = bias_ref[...]
    mixes = []
    for s in range(samples):
        q = query_ref[s]
        stacked = jnp.concatenate(
            [q[t : t + 1].astype(f32) * mask_rows for t in range(tok_dev)], axis=0
        ).astype(bf16)
        sc = lax.dot_general(
            stacked, ks[s], (((1,), (1,)), ((), ())), preferred_element_type=f32
        ) / root + bias
        sc = jnp.where(keep, sc, -1e30)
        top = jnp.max(sc, axis=-1, keepdims=True)
        e = jnp.where(keep, jnp.exp(sc - top), 0.0)
        tot = jnp.sum(e, axis=-1, keepdims=True)
        o = jnp.dot(e.astype(bf16), vs[s], preferred_element_type=f32) / tot
        mixes.append(
            jnp.concatenate(
                [
                    jnp.sum(o[t * heads : (t + 1) * heads] * mask_rows, axis=0, keepdims=True)
                    for t in range(tok_dev)
                ],
                axis=0,
            ).astype(bf16)
        )
    arrived(samples + 2)
    projected = jnp.dot(jnp.concatenate(mixes, axis=0), wo_ref[...], preferred_element_type=f32)
    for s in range(samples):
        own = own_ref[s].astype(f32)
        out_ref[:, s, :] = (own + projected[s * tok_dev : (s + 1) * tok_dev]).astype(bf16)


def on_device(
    atom_feat,
    window_shift,
    atom_token,
    token_in,
    pair,
    key_mask,
    w_atom_query,
    w_atom_key,
    w_atom_value,
    w_atom_out,
    w_to_token,
    w_query,
    w_key,
    w_value,
    w_out,
    w_bias,
):
    high = lax.Precision.HIGHEST
    atom_dev, samples, width = atom_feat.shape
    tok_dev = token_in.shape[0]
    tok_width = token_in.shape[2]
    devices = lax.axis_size("row")
    rank = lax.axis_index("row")
    atom_base = rank * atom_dev
    total_atoms = atom_dev * devices
    margin = (KWIN - QBLOCK) // 2
    low_rows = margin + SHIFT
    span = KWIN + 2 * SHIFT
    high_rows = span - low_rows
    blocks = atom_dev // QBLOCK + 1

    low = shifted(atom_feat, "row", 1)
    shift_row = jnp.broadcast_to(window_shift[0], (1, samples, width)).astype(jnp.bfloat16)
    upper = shifted(jnp.concatenate([atom_feat, shift_row], axis=0), "row", -1)

    head_dim = width // ATOM_HEADS
    rows = blocks * QBLOCK
    ext_rows = low_rows + atom_dev + high_rows
    kernel = functools.partial(
        atom_kernel,
        atom_dev=atom_dev,
        rows=rows,
        low_rows=low_rows,
        high_rows=high_rows,
        head_dim=head_dim,
        devices=devices,
    )
    vmem = pl.BlockSpec(memory_space=pltpu.VMEM)
    flops = 2 * samples * (
        ext_rows * width * 3 * width
        + rows * width * (width + tok_width)
        + ATOM_HEADS * rows * ext_rows * width * 2
        + 3 * tok_dev * rows * tok_width
    )
    hbm = pl.BlockSpec(memory_space=pl.ANY)
    count = tok_dev * devices
    atom_out, state_t, query_t = pl.pallas_call(
        kernel,
        out_shape=(
            jax.ShapeDtypeStruct((atom_dev, samples, width), jnp.bfloat16),
            jax.ShapeDtypeStruct((samples, tok_dev, tok_width), jnp.bfloat16),
            jax.ShapeDtypeStruct((samples, tok_dev, tok_width), jnp.bfloat16),
        ),
        in_specs=[vmem] * 3
        + [pl.BlockSpec(memory_space=pltpu.SMEM)]
        + [vmem] * 7
        + [hbm],
        out_specs=(vmem, vmem, vmem),
        scratch_shapes=[
            pltpu.VMEM(w_query.shape, w_query.dtype),
            pltpu.SemaphoreType.DMA((1,)),
        ],
        cost_estimate=pl.CostEstimate(
            flops=flops,
            transcendentals=samples * ATOM_HEADS * rows * ext_rows,
            bytes_accessed=2 * (ext_rows + atom_dev) * samples * width
            + 2 * width * (3 * width + width + tok_width)
            + 4 * samples * tok_dev * tok_width,
        ),
    )(
        atom_feat,
        low,
        upper,
        window_shift,
        w_atom_query,
        w_atom_key,
        w_atom_value,
        w_atom_out,
        w_to_token,
        atom_token[None, :],
        token_in,
        w_query,
    )
    bias = jnp.einsum("qkc,ch->qhk", pair, w_bias, preferred_element_type=jnp.float32)
    bias = bias.reshape(tok_dev * TOKEN_HEADS, count)

    every = lax.all_gather(state_t, "row", axis=1, tiled=True)
    token_out = pl.pallas_call(
        functools.partial(token_kernel, heads=TOKEN_HEADS, pieces=4),
        out_shape=jax.ShapeDtypeStruct((tok_dev, samples, tok_width), jnp.bfloat16),
        in_specs=[hbm, vmem, vmem, vmem, vmem, hbm, hbm, hbm],
        out_specs=vmem,
        scratch_shapes=[
            pltpu.VMEM(every.shape, every.dtype),
            pltpu.VMEM(w_key.shape, w_key.dtype),
            pltpu.VMEM(w_value.shape, w_value.dtype),
            pltpu.VMEM(w_out.shape, w_out.dtype),
            pltpu.SemaphoreType.DMA((samples + 3 * 4,)),
        ],
        cost_estimate=pl.CostEstimate(
            flops=2 * samples * tok_width * (
                2 * count * tok_width + 2 * tok_dev * tok_width + 2 * TOKEN_HEADS * tok_dev * count
            ),
            transcendentals=samples * TOKEN_HEADS * tok_dev * count,
            bytes_accessed=2 * 4 * tok_width * tok_width
            + 2 * samples * (count + 2 * tok_dev) * tok_width
            + 4 * TOKEN_HEADS * tok_dev * count,
        ),
    )(
        every,
        state_t,
        query_t,
        bias,
        key_mask[None, :],
        w_key,
        w_value,
        w_out,
    )
    return (atom_out, token_out)


def solution(mesh):
    return jax.shard_map(
        on_device,
        mesh=mesh,
        in_specs=(
            P(("groups", "row"), None, None),
            P(("groups", "row")),
            P("groups"),
            P(("groups", "row"), None, None),
            P(("groups", "row"), None, None),
            P("groups"),
            P(),
            P(),
            P(),
            P(),
            P(),
            P(),
            P(),
            P(),
            P(),
            P(),
        ),
        out_specs=(P(("groups", "row"), None, None), P(("groups", "row"), None, None)),
        check_vma=False,
    )
```

```python
import functools
import math

import jax
import jax.numpy as jnp
from jax import lax
from jax.experimental import pallas as pl
from jax.experimental.pallas import tpu as pltpu
from jax.sharding import PartitionSpec as P

ATOM_HEADS = 4
QBLOCK = 32
KWIN = 128
SHIFT = 16
TOKEN_HEADS = 16


def layer_norm(values):
    values = values.astype(jnp.float32)
    mean = jnp.mean(values, axis=-1, keepdims=True)
    var = jnp.mean((values - mean) ** 2, axis=-1, keepdims=True)
    return (values - mean) / jnp.sqrt(var + 1e-05)


def project(values, weight):
    return jnp.einsum("asc,cd->asd", values, weight, preferred_element_type=jnp.float32)


def shifted(block, axis, step):
    count = lax.axis_size(axis)
    route = [(i, i + step) for i in range(count) if 0 <= i + step < count]
    return lax.ppermute(block, axis, route)


def own_kernel(own_ref, wq_ref, wk_ref, wv_ref, q_ref, k_ref, v_ref):
    f32, bf16 = jnp.float32, jnp.bfloat16
    rows, samples, _ = own_ref.shape
    normal = []
    for s in range(samples):
        x = own_ref[:, s, :].astype(f32)
        mean = jnp.mean(x, axis=-1, keepdims=True)
        var = jnp.mean((x - mean) ** 2, axis=-1, keepdims=True)
        normal.append(((x - mean) / jnp.sqrt(var + 1e-05)).astype(bf16))
    xn = jnp.concatenate(normal, axis=0)
    for w_ref, o_ref in ((wq_ref, q_ref), (wk_ref, k_ref), (wv_ref, v_ref)):
        y = jnp.dot(xn, w_ref[...], preferred_element_type=f32).astype(bf16)
        for s in range(samples):
            o_ref[s] = y[s * rows : (s + 1) * rows]


def atom_kernel(
    own_ref,
    low_ref,
    upper_ref,
    shift_ref,
    wq_ref,
    wk_ref,
    wv_ref,
    wo_ref,
    wt_ref,
    ids_ref,
    token_ref,
    wq_hbm,
    q_own_ref,
    k_own_ref,
    v_own_ref,
    atom_ref,
    state_ref,
    query_ref,
    wtq_ref,
    sems,
    *,
    atom_dev,
    rows,
    low_rows,
    high_rows,
    head_dim,
    devices,
):
    f32, bf16 = jnp.float32, jnp.bfloat16
    copies = [pltpu.make_async_copy(wq_hbm, wtq_ref, sems.at[0])]
    for copy in copies:
        copy.start()
    _, samples, width = own_ref.shape
    ext_rows = low_rows + atom_dev + high_rows
    lane = lax.broadcasted_iota(jnp.int32, (1, width), 1) // head_dim
    head_masks = [(lane == h).astype(f32) for h in range(ATOM_HEADS)]
    root = jnp.float32(math.sqrt(head_dim))
    rank = lax.axis_index("row")
    base = rank * atom_dev
    total = devices * atom_dev
    tok_dev = token_ref.shape[0]
    row_block = lax.broadcasted_iota(jnp.int32, (rows, 1), 0) // QBLOCK
    next_shift = upper_ref[pl.ds(atom_dev, 1), 0, :].astype(f32)[:, 0:1].astype(jnp.int32)
    shift = jnp.where(row_block == rows // QBLOCK - 1, next_shift, 0)
    for j in range(rows // QBLOCK - 1):
        shift = shift + jnp.where(row_block == j, shift_ref[j], 0)
    first = row_block * QBLOCK + SHIFT + shift
    lo = jnp.maximum(first, low_rows - base)
    hi = jnp.minimum(first + KWIN, total - base + low_rows)
    column = lax.broadcasted_iota(jnp.int32, (rows, ext_rows), 1)
    keep = (column >= lo) & (column < hi)
    own_start = pl.multiple_of(base, atom_dev)
    next_start = pl.multiple_of(jnp.minimum(base + atom_dev, total - atom_dev), atom_dev)
    next_ids = ids_ref[:, pl.ds(next_start, atom_dev)][:, 0 : rows - atom_dev]
    next_ids = jnp.where(rank < devices - 1, next_ids, -1)
    row_ids = jnp.concatenate([ids_ref[:, pl.ds(own_start, atom_dev)], next_ids], axis=1)
    own_ids = rank * tok_dev + lax.broadcasted_iota(jnp.int32, (tok_dev, 1), 0)
    onehot = (own_ids == row_ids).astype(f32)
    counts = jnp.sum(onehot, axis=1, keepdims=True)
    onehot = onehot.astype(bf16)
    xs, halo = [], []
    for s in range(samples):
        x = jnp.concatenate(
            [
                low_ref[atom_dev - low_rows : atom_dev, s, :],
                own_ref[:, s, :],
                upper_ref[0:high_rows, s, :],
            ],
            axis=0,
        ).astype(f32)
        xs.append(x)
        for part in (x[0:low_rows], x[low_rows + atom_dev :]):
            mean = jnp.mean(part, axis=-1, keepdims=True)
            var = jnp.mean((part - mean) ** 2, axis=-1, keepdims=True)
            halo.append(((part - mean) / jnp.sqrt(var + 1e-05)).astype(bf16))
    halo_rows = low_rows + high_rows
    halo_all = jnp.concatenate(halo, axis=0)
    kh = jnp.dot(halo_all, wk_ref[...], preferred_element_type=f32).astype(bf16)
    vh = jnp.dot(halo_all, wv_ref[...], preferred_element_type=f32).astype(bf16)
    extra = rows - atom_dev
    qh = jnp.dot(
        jnp.concatenate([halo[2 * s + 1][0:extra] for s in range(samples)], axis=0),
        wq_ref[...],
        preferred_element_type=f32,
    ).astype(bf16)

    def assembled(h, own, s):
        start = s * halo_rows
        return jnp.concatenate(
            [h[start : start + low_rows], own[s], h[start + low_rows : start + halo_rows]], axis=0
        )

    q_all = jnp.concatenate(
        [jnp.concatenate([q_own_ref[s], qh[s * extra : (s + 1) * extra]], axis=0) for s in range(samples)],
        axis=0,
    )
    k_all = jnp.concatenate([assembled(kh, k_own_ref, s) for s in range(samples)], axis=0)
    v_all = jnp.concatenate([assembled(vh, v_own_ref, s) for s in range(samples)], axis=0)
    mixed = []
    for s in range(samples):
        q = q_all[s * rows : (s + 1) * rows]
        k = k_all[s * ext_rows : (s + 1) * ext_rows]
        v = v_all[s * ext_rows : (s + 1) * ext_rows]
        acc = jnp.zeros((rows, width), f32)
        for h in range(ATOM_HEADS):
            qh = q * head_masks[h].astype(bf16)
            sc = lax.dot_general(
                qh, k, (((1,), (1,)), ((), ())), preferred_element_type=f32
            ) / root
            sc = jnp.where(keep, sc, -1e30)
            top = jnp.max(sc, axis=-1, keepdims=True)
            e = jnp.where(keep, jnp.exp(sc - top), 0.0)
            tot = jnp.sum(e, axis=-1, keepdims=True)
            o = jnp.dot(e.astype(bf16), v, preferred_element_type=f32)
            acc = acc + (o / tot) * head_masks[h]
        mixed.append(acc.astype(bf16))
    base = jnp.concatenate([x[low_rows : low_rows + rows] for x in xs], axis=0)
    out = (
        base + jnp.dot(jnp.concatenate(mixed, axis=0), wo_ref[...], preferred_element_type=f32)
    ).astype(bf16)
    for s in range(samples):
        atom_ref[:, s, :] = out[s * rows : s * rows + atom_dev]
    hidden = jnp.maximum(jnp.dot(out, wt_ref[...], preferred_element_type=f32), 0.0)
    top_part = hidden.astype(bf16)
    rest = hidden - top_part.astype(f32)
    mid_part = rest.astype(bf16)
    low_part = (rest - mid_part.astype(f32)).astype(bf16)
    zero = jnp.zeros_like(onehot)
    diagonal = jnp.concatenate(
        [
            jnp.concatenate([onehot if c == r else zero for c in range(samples)], axis=1)
            for r in range(samples)
        ],
        axis=0,
    )
    sums = (
        jnp.dot(diagonal, top_part, preferred_element_type=f32)
        + jnp.dot(diagonal, mid_part, preferred_element_type=f32)
        + jnp.dot(diagonal, low_part, preferred_element_type=f32)
    )
    tns = []
    for s in range(samples):
        st = (token_ref[:, s, :].astype(f32) + sums[s * tok_dev : (s + 1) * tok_dev] / counts)
        st = st.astype(bf16)
        state_ref[s] = st
        st = st.astype(f32)
        mean = jnp.mean(st, axis=-1, keepdims=True)
        var = jnp.mean((st - mean) ** 2, axis=-1, keepdims=True)
        tns.append(((st - mean) / jnp.sqrt(var + 1e-05)).astype(bf16))
    copies[0].wait()
    query = jnp.dot(jnp.concatenate(tns, axis=0), wtq_ref[...], preferred_element_type=f32)
    query = query.astype(bf16)
    for s in range(samples):
        query_ref[s] = query[s * tok_dev : (s + 1) * tok_dev]


def token_kernel(
    every_ref,
    own_ref,
    query_ref,
    bias_ref,
    flags_ref,
    wk_hbm,
    wv_hbm,
    wo_hbm,
    out_ref,
    wk_ref,
    wv_ref,
    wo_ref,
    sems,
    *,
    heads,
):
    copies = [
        pltpu.make_async_copy(src, dst, sems.at[i])
        for i, (src, dst) in enumerate([(wk_hbm, wk_ref), (wv_hbm, wv_ref), (wo_hbm, wo_ref)])
    ]
    for copy in copies:
        copy.start()
    f32, bf16 = jnp.float32, jnp.bfloat16
    samples, tok_dev, width = own_ref.shape
    head_dim = width // heads
    lane = lax.broadcasted_iota(jnp.int32, (1, width), 1) // head_dim
    head_masks = [(lane == h).astype(f32) for h in range(heads)]
    root = jnp.float32(math.sqrt(head_dim))
    keep = flags_ref[...] > 0
    mask_rows = jnp.concatenate(head_masks, axis=0)

    def normed(x):
        mean = jnp.mean(x, axis=-1, keepdims=True)
        var = jnp.mean((x - mean) ** 2, axis=-1, keepdims=True)
        return ((x - mean) / jnp.sqrt(var + 1e-05)).astype(bf16)

    allx = jnp.concatenate([normed(every_ref[s].astype(f32)) for s in range(samples)], axis=0)
    count = every_ref.shape[1]
    copies[0].wait()
    k_all = jnp.dot(allx, wk_ref[...], preferred_element_type=f32).astype(bf16)
    copies[1].wait()
    v_all = jnp.dot(allx, wv_ref[...], preferred_element_type=f32).astype(bf16)
    ks = [k_all[s * count : (s + 1) * count] for s in range(samples)]
    vs = [v_all[s * count : (s + 1) * count] for s in range(samples)]
    bias = bias_ref[...]
    mixes = []
    for s in range(samples):
        q = query_ref[s]
        stacked = jnp.concatenate(
            [q[t : t + 1].astype(f32) * mask_rows for t in range(tok_dev)], axis=0
        ).astype(bf16)
        sc = lax.dot_general(
            stacked, ks[s], (((1,), (1,)), ((), ())), preferred_element_type=f32
        ) / root + bias
        sc = jnp.where(keep, sc, -1e30)
        top = jnp.max(sc, axis=-1, keepdims=True)
        e = jnp.where(keep, jnp.exp(sc - top), 0.0)
        tot = jnp.sum(e, axis=-1, keepdims=True)
        o = jnp.dot(e.astype(bf16), vs[s], preferred_element_type=f32) / tot
        mixes.append(
            jnp.concatenate(
                [
                    jnp.sum(o[t * heads : (t + 1) * heads] * mask_rows, axis=0, keepdims=True)
                    for t in range(tok_dev)
                ],
                axis=0,
            ).astype(bf16)
        )
    copies[2].wait()
    projected = jnp.dot(jnp.concatenate(mixes, axis=0), wo_ref[...], preferred_element_type=f32)
    for s in range(samples):
        own = own_ref[s].astype(f32)
        out_ref[:, s, :] = (own + projected[s * tok_dev : (s + 1) * tok_dev]).astype(bf16)


def on_device(
    atom_feat,
    window_shift,
    atom_token,
    token_in,
    pair,
    key_mask,
    w_atom_query,
    w_atom_key,
    w_atom_value,
    w_atom_out,
    w_to_token,
    w_query,
    w_key,
    w_value,
    w_out,
    w_bias,
):
    high = lax.Precision.HIGHEST
    atom_dev, samples, width = atom_feat.shape
    tok_dev = token_in.shape[0]
    tok_width = token_in.shape[2]
    devices = lax.axis_size("row")
    rank = lax.axis_index("row")
    atom_base = rank * atom_dev
    total_atoms = atom_dev * devices
    margin = (KWIN - QBLOCK) // 2
    low_rows = margin + SHIFT
    span = KWIN + 2 * SHIFT
    high_rows = span - low_rows
    blocks = atom_dev // QBLOCK + 1

    low = shifted(atom_feat, "row", 1)
    shift_row = jnp.broadcast_to(window_shift[0], (1, samples, width)).astype(jnp.bfloat16)
    upper = shifted(jnp.concatenate([atom_feat, shift_row], axis=0), "row", -1)

    head_dim = width // ATOM_HEADS
    rows = blocks * QBLOCK
    ext_rows = low_rows + atom_dev + high_rows
    kernel = functools.partial(
        atom_kernel,
        atom_dev=atom_dev,
        rows=rows,
        low_rows=low_rows,
        high_rows=high_rows,
        head_dim=head_dim,
        devices=devices,
    )
    vmem = pl.BlockSpec(memory_space=pltpu.VMEM)
    flops = 2 * samples * (
        ext_rows * width * 3 * width
        + rows * width * (width + tok_width)
        + ATOM_HEADS * rows * ext_rows * width * 2
        + 3 * tok_dev * rows * tok_width
    )
    hbm = pl.BlockSpec(memory_space=pl.ANY)
    count = tok_dev * devices
    own_shape = jax.ShapeDtypeStruct((samples, atom_dev, width), jnp.bfloat16)
    q_own, k_own, v_own = pl.pallas_call(
        own_kernel,
        out_shape=(own_shape, own_shape, own_shape),
        in_specs=[vmem] * 4,
        out_specs=(vmem, vmem, vmem),
        cost_estimate=pl.CostEstimate(
            flops=2 * samples * atom_dev * width * 3 * width,
            transcendentals=0,
            bytes_accessed=2 * 4 * samples * atom_dev * width + 2 * 3 * width * width,
        ),
    )(atom_feat, w_atom_query, w_atom_key, w_atom_value)
    atom_out, state_t, query_t = pl.pallas_call(
        kernel,
        out_shape=(
            jax.ShapeDtypeStruct((atom_dev, samples, width), jnp.bfloat16),
            jax.ShapeDtypeStruct((samples, tok_dev, tok_width), jnp.bfloat16),
            jax.ShapeDtypeStruct((samples, tok_dev, tok_width), jnp.bfloat16),
        ),
        in_specs=[vmem] * 3
        + [pl.BlockSpec(memory_space=pltpu.SMEM)]
        + [vmem] * 7
        + [hbm, vmem, vmem, vmem],
        out_specs=(vmem, vmem, vmem),
        scratch_shapes=[
            pltpu.VMEM(w_query.shape, w_query.dtype),
            pltpu.SemaphoreType.DMA((1,)),
        ],
        cost_estimate=pl.CostEstimate(
            flops=flops,
            transcendentals=samples * ATOM_HEADS * rows * ext_rows,
            bytes_accessed=2 * (ext_rows + atom_dev) * samples * width
            + 2 * width * (3 * width + width + tok_width)
            + 4 * samples * tok_dev * tok_width,
        ),
    )(
        atom_feat,
        low,
        upper,
        window_shift,
        w_atom_query,
        w_atom_key,
        w_atom_value,
        w_atom_out,
        w_to_token,
        atom_token[None, :],
        token_in,
        w_query,
        q_own,
        k_own,
        v_own,
    )
    bias = jnp.einsum("qkc,ch->qhk", pair, w_bias, preferred_element_type=jnp.float32)
    bias = bias.reshape(tok_dev * TOKEN_HEADS, count)

    every = lax.all_gather(state_t, "row", axis=1, tiled=True)
    token_out = pl.pallas_call(
        functools.partial(token_kernel, heads=TOKEN_HEADS),
        out_shape=jax.ShapeDtypeStruct((tok_dev, samples, tok_width), jnp.bfloat16),
        in_specs=[vmem, vmem, vmem, vmem, vmem, hbm, hbm, hbm],
        out_specs=vmem,
        scratch_shapes=[
            pltpu.VMEM(w_key.shape, w_key.dtype),
            pltpu.VMEM(w_value.shape, w_value.dtype),
            pltpu.VMEM(w_out.shape, w_out.dtype),
            pltpu.SemaphoreType.DMA((3,)),
        ],
        cost_estimate=pl.CostEstimate(
            flops=2 * samples * tok_width * (
                2 * count * tok_width + 2 * tok_dev * tok_width + 2 * TOKEN_HEADS * tok_dev * count
            ),
            transcendentals=samples * TOKEN_HEADS * tok_dev * count,
            bytes_accessed=2 * 4 * tok_width * tok_width
            + 2 * samples * (count + 2 * tok_dev) * tok_width
            + 4 * TOKEN_HEADS * tok_dev * count,
        ),
    )(
        every,
        state_t,
        query_t,
        bias,
        key_mask[None, :],
        w_key,
        w_value,
        w_out,
    )
    return (atom_out, token_out)


def solution(mesh):
    return jax.shard_map(
        on_device,
        mesh=mesh,
        in_specs=(
            P(("groups", "row"), None, None),
            P(("groups", "row")),
            P("groups"),
            P(("groups", "row"), None, None),
            P(("groups", "row"), None, None),
            P("groups"),
            P(),
            P(),
            P(),
            P(),
            P(),
            P(),
            P(),
            P(),
            P(),
            P(),
        ),
        out_specs=(P(("groups", "row"), None, None), P(("groups", "row"), None, None)),
        check_vma=False,
    )
```

```python
import functools
import math

import jax
import jax.numpy as jnp
from jax import lax
from jax.experimental import pallas as pl
from jax.experimental.pallas import tpu as pltpu
from jax.sharding import PartitionSpec as P

ATOM_HEADS = 4
QBLOCK = 32
KWIN = 128
SHIFT = 16
TOKEN_HEADS = 16


def layer_norm(values):
    values = values.astype(jnp.float32)
    mean = jnp.mean(values, axis=-1, keepdims=True)
    var = jnp.mean((values - mean) ** 2, axis=-1, keepdims=True)
    return (values - mean) / jnp.sqrt(var + 1e-05)


def project(values, weight):
    return jnp.einsum("asc,cd->asd", values, weight, preferred_element_type=jnp.float32)


def shifted(block, axis, step):
    count = lax.axis_size(axis)
    route = [(i, i + step) for i in range(count) if 0 <= i + step < count]
    return lax.ppermute(block, axis, route)


def atom_kernel(
    own_ref,
    low_ref,
    upper_ref,
    shift_ref,
    wq_ref,
    wk_ref,
    wv_ref,
    wo_ref,
    wt_ref,
    ids_ref,
    token_ref,
    wq_hbm,
    atom_ref,
    state_ref,
    query_ref,
    wtq_ref,
    sems,
    *,
    atom_dev,
    rows,
    low_rows,
    high_rows,
    head_dim,
    devices,
):
    f32, bf16 = jnp.float32, jnp.bfloat16
    copies = [pltpu.make_async_copy(wq_hbm, wtq_ref, sems.at[0])]
    for copy in copies:
        copy.start()
    _, samples, width = own_ref.shape
    ext_rows = low_rows + atom_dev + high_rows
    lane = lax.broadcasted_iota(jnp.int32, (1, width), 1) // head_dim
    head_masks = [(lane == h).astype(f32) for h in range(ATOM_HEADS)]
    root = jnp.float32(math.sqrt(head_dim))
    rank = lax.axis_index("row")
    base = rank * atom_dev
    total = devices * atom_dev
    tok_dev = token_ref.shape[0]
    row_block = lax.broadcasted_iota(jnp.int32, (rows, 1), 0) // QBLOCK
    next_shift = upper_ref[pl.ds(atom_dev, 1), 0, :].astype(f32)[:, 0:1].astype(jnp.int32)
    shift = jnp.where(row_block == rows // QBLOCK - 1, next_shift, 0)
    for j in range(rows // QBLOCK - 1):
        shift = shift + jnp.where(row_block == j, shift_ref[j], 0)
    first = row_block * QBLOCK + SHIFT + shift
    lo = jnp.maximum(first, low_rows - base)
    hi = jnp.minimum(first + KWIN, total - base + low_rows)
    column = lax.broadcasted_iota(jnp.int32, (rows, ext_rows), 1)
    keep = (column >= lo) & (column < hi)
    keep_all = jnp.concatenate([keep] * ATOM_HEADS, axis=0)
    own_start = pl.multiple_of(base, atom_dev)
    next_start = pl.multiple_of(jnp.minimum(base + atom_dev, total - atom_dev), atom_dev)
    next_ids = ids_ref[:, pl.ds(next_start, atom_dev)][:, 0 : rows - atom_dev]
    next_ids = jnp.where(rank < devices - 1, next_ids, -1)
    row_ids = jnp.concatenate([ids_ref[:, pl.ds(own_start, atom_dev)], next_ids], axis=1)
    own_ids = rank * tok_dev + lax.broadcasted_iota(jnp.int32, (tok_dev, 1), 0)
    onehot = (own_ids == row_ids).astype(f32)
    counts = jnp.sum(onehot, axis=1, keepdims=True)
    onehot = onehot.astype(bf16)
    xs, xns = [], []
    for s in range(samples):
        x = jnp.concatenate(
            [
                low_ref[atom_dev - low_rows : atom_dev, s, :],
                own_ref[:, s, :],
                upper_ref[0:high_rows, s, :],
            ],
            axis=0,
        ).astype(f32)
        mean = jnp.mean(x, axis=-1, keepdims=True)
        var = jnp.mean((x - mean) ** 2, axis=-1, keepdims=True)
        xs.append(x)
        xns.append(((x - mean) / jnp.sqrt(var + 1e-05)).astype(bf16))
    xn_all = jnp.concatenate(xns, axis=0)
    q_all = jnp.dot(
        jnp.concatenate([xn[low_rows : low_rows + rows] for xn in xns], axis=0),
        wq_ref[...],
        preferred_element_type=f32,
    ).astype(bf16)
    k_all = jnp.dot(xn_all, wk_ref[...], preferred_element_type=f32).astype(bf16)
    v_all = jnp.dot(xn_all, wv_ref[...], preferred_element_type=f32).astype(bf16)
    mixed = []
    for s in range(samples):
        q = q_all[s * rows : (s + 1) * rows]
        k = k_all[s * ext_rows : (s + 1) * ext_rows]
        v = v_all[s * ext_rows : (s + 1) * ext_rows]
        stacked = jnp.concatenate(
            [q * head_masks[h].astype(bf16) for h in range(ATOM_HEADS)], axis=0
        )
        sc = lax.dot_general(
            stacked, k, (((1,), (1,)), ((), ())), preferred_element_type=f32
        ) / root
        sc = jnp.where(keep_all, sc, -1e30)
        top = jnp.max(sc, axis=-1, keepdims=True)
        e = jnp.where(keep_all, jnp.exp(sc - top), 0.0)
        tot = jnp.sum(e, axis=-1, keepdims=True)
        o = jnp.dot(e.astype(bf16), v, preferred_element_type=f32) / tot
        acc = o[0:rows] * head_masks[0]
        for h in range(1, ATOM_HEADS):
            acc = acc + o[h * rows : (h + 1) * rows] * head_masks[h]
        mixed.append(acc.astype(bf16))
    base = jnp.concatenate([x[low_rows : low_rows + rows] for x in xs], axis=0)
    out = (
        base + jnp.dot(jnp.concatenate(mixed, axis=0), wo_ref[...], preferred_element_type=f32)
    ).astype(bf16)
    for s in range(samples):
        atom_ref[:, s, :] = out[s * rows : s * rows + atom_dev]
    hidden = jnp.maximum(jnp.dot(out, wt_ref[...], preferred_element_type=f32), 0.0)
    top_part = hidden.astype(bf16)
    rest = hidden - top_part.astype(f32)
    mid_part = rest.astype(bf16)
    low_part = (rest - mid_part.astype(f32)).astype(bf16)
    zero = jnp.zeros_like(onehot)
    diagonal = jnp.concatenate(
        [
            jnp.concatenate([onehot if c == r else zero for c in range(samples)], axis=1)
            for r in range(samples)
        ],
        axis=0,
    )
    sums = (
        jnp.dot(diagonal, top_part, preferred_element_type=f32)
        + jnp.dot(diagonal, mid_part, preferred_element_type=f32)
        + jnp.dot(diagonal, low_part, preferred_element_type=f32)
    )
    tns = []
    for s in range(samples):
        st = (token_ref[:, s, :].astype(f32) + sums[s * tok_dev : (s + 1) * tok_dev] / counts)
        st = st.astype(bf16)
        state_ref[s] = st
        st = st.astype(f32)
        mean = jnp.mean(st, axis=-1, keepdims=True)
        var = jnp.mean((st - mean) ** 2, axis=-1, keepdims=True)
        tns.append(((st - mean) / jnp.sqrt(var + 1e-05)).astype(bf16))
    copies[0].wait()
    query = jnp.dot(jnp.concatenate(tns, axis=0), wtq_ref[...], preferred_element_type=f32)
    query = query.astype(bf16)
    for s in range(samples):
        query_ref[s] = query[s * tok_dev : (s + 1) * tok_dev]


def token_kernel(
    every_ref,
    own_ref,
    query_ref,
    bias_ref,
    flags_ref,
    wk_hbm,
    wv_hbm,
    wo_hbm,
    out_ref,
    wk_ref,
    wv_ref,
    wo_ref,
    sems,
    *,
    heads,
):
    copies = [
        pltpu.make_async_copy(src, dst, sems.at[i])
        for i, (src, dst) in enumerate([(wk_hbm, wk_ref), (wv_hbm, wv_ref), (wo_hbm, wo_ref)])
    ]
    for copy in copies:
        copy.start()
    f32, bf16 = jnp.float32, jnp.bfloat16
    samples, tok_dev, width = own_ref.shape
    head_dim = width // heads
    lane = lax.broadcasted_iota(jnp.int32, (1, width), 1) // head_dim
    head_masks = [(lane == h).astype(f32) for h in range(heads)]
    root = jnp.float32(math.sqrt(head_dim))
    keep = flags_ref[...] > 0
    mask_rows = jnp.concatenate(head_masks, axis=0)

    def normed(x):
        mean = jnp.mean(x, axis=-1, keepdims=True)
        var = jnp.mean((x - mean) ** 2, axis=-1, keepdims=True)
        return ((x - mean) / jnp.sqrt(var + 1e-05)).astype(bf16)

    allx = jnp.concatenate([normed(every_ref[s].astype(f32)) for s in range(samples)], axis=0)
    count = every_ref.shape[1]
    copies[0].wait()
    k_all = jnp.dot(allx, wk_ref[...], preferred_element_type=f32).astype(bf16)
    copies[1].wait()
    v_all = jnp.dot(allx, wv_ref[...], preferred_element_type=f32).astype(bf16)
    ks = [k_all[s * count : (s + 1) * count] for s in range(samples)]
    vs = [v_all[s * count : (s + 1) * count] for s in range(samples)]
    bias = bias_ref[...]
    mixes = []
    for s in range(samples):
        q = query_ref[s]
        stacked = jnp.concatenate(
            [q[t : t + 1].astype(f32) * mask_rows for t in range(tok_dev)], axis=0
        ).astype(bf16)
        sc = lax.dot_general(
            stacked, ks[s], (((1,), (1,)), ((), ())), preferred_element_type=f32
        ) / root + bias
        sc = jnp.where(keep, sc, -1e30)
        top = jnp.max(sc, axis=-1, keepdims=True)
        e = jnp.where(keep, jnp.exp(sc - top), 0.0)
        tot = jnp.sum(e, axis=-1, keepdims=True)
        o = jnp.dot(e.astype(bf16), vs[s], preferred_element_type=f32) / tot
        mixes.append(
            jnp.concatenate(
                [
                    jnp.sum(o[t * heads : (t + 1) * heads] * mask_rows, axis=0, keepdims=True)
                    for t in range(tok_dev)
                ],
                axis=0,
            ).astype(bf16)
        )
    copies[2].wait()
    projected = jnp.dot(jnp.concatenate(mixes, axis=0), wo_ref[...], preferred_element_type=f32)
    for s in range(samples):
        own = own_ref[s].astype(f32)
        out_ref[:, s, :] = (own + projected[s * tok_dev : (s + 1) * tok_dev]).astype(bf16)


def on_device(
    atom_feat,
    window_shift,
    atom_token,
    token_in,
    pair,
    key_mask,
    w_atom_query,
    w_atom_key,
    w_atom_value,
    w_atom_out,
    w_to_token,
    w_query,
    w_key,
    w_value,
    w_out,
    w_bias,
):
    high = lax.Precision.HIGHEST
    atom_dev, samples, width = atom_feat.shape
    tok_dev = token_in.shape[0]
    tok_width = token_in.shape[2]
    devices = lax.axis_size("row")
    rank = lax.axis_index("row")
    atom_base = rank * atom_dev
    total_atoms = atom_dev * devices
    margin = (KWIN - QBLOCK) // 2
    low_rows = margin + SHIFT
    span = KWIN + 2 * SHIFT
    high_rows = span - low_rows
    blocks = atom_dev // QBLOCK + 1

    low = shifted(atom_feat, "row", 1)
    shift_row = jnp.broadcast_to(window_shift[0], (1, samples, width)).astype(jnp.bfloat16)
    upper = shifted(jnp.concatenate([atom_feat, shift_row], axis=0), "row", -1)

    head_dim = width // ATOM_HEADS
    rows = blocks * QBLOCK
    ext_rows = low_rows + atom_dev + high_rows
    kernel = functools.partial(
        atom_kernel,
        atom_dev=atom_dev,
        rows=rows,
        low_rows=low_rows,
        high_rows=high_rows,
        head_dim=head_dim,
        devices=devices,
    )
    vmem = pl.BlockSpec(memory_space=pltpu.VMEM)
    flops = 2 * samples * (
        ext_rows * width * 3 * width
        + rows * width * (width + tok_width)
        + ATOM_HEADS * rows * ext_rows * width * 2
        + 3 * tok_dev * rows * tok_width
    )
    hbm = pl.BlockSpec(memory_space=pl.ANY)
    count = tok_dev * devices
    atom_out, state_t, query_t = pl.pallas_call(
        kernel,
        out_shape=(
            jax.ShapeDtypeStruct((atom_dev, samples, width), jnp.bfloat16),
            jax.ShapeDtypeStruct((samples, tok_dev, tok_width), jnp.bfloat16),
            jax.ShapeDtypeStruct((samples, tok_dev, tok_width), jnp.bfloat16),
        ),
        in_specs=[vmem] * 3
        + [pl.BlockSpec(memory_space=pltpu.SMEM)]
        + [vmem] * 7
        + [hbm],
        out_specs=(vmem, vmem, vmem),
        scratch_shapes=[
            pltpu.VMEM(w_query.shape, w_query.dtype),
            pltpu.SemaphoreType.DMA((1,)),
        ],
        cost_estimate=pl.CostEstimate(
            flops=flops,
            transcendentals=samples * ATOM_HEADS * rows * ext_rows,
            bytes_accessed=2 * (ext_rows + atom_dev) * samples * width
            + 2 * width * (3 * width + width + tok_width)
            + 4 * samples * tok_dev * tok_width,
        ),
    )(
        atom_feat,
        low,
        upper,
        window_shift,
        w_atom_query,
        w_atom_key,
        w_atom_value,
        w_atom_out,
        w_to_token,
        atom_token[None, :],
        token_in,
        w_query,
    )
    bias = jnp.einsum("qkc,ch->qhk", pair, w_bias, preferred_element_type=jnp.float32)
    bias = bias.reshape(tok_dev * TOKEN_HEADS, count)

    every = lax.all_gather(state_t, "row", axis=1, tiled=True)
    token_out = pl.pallas_call(
        functools.partial(token_kernel, heads=TOKEN_HEADS),
        out_shape=jax.ShapeDtypeStruct((tok_dev, samples, tok_width), jnp.bfloat16),
        in_specs=[vmem, vmem, vmem, vmem, vmem, hbm, hbm, hbm],
        out_specs=vmem,
        scratch_shapes=[
            pltpu.VMEM(w_key.shape, w_key.dtype),
            pltpu.VMEM(w_value.shape, w_value.dtype),
            pltpu.VMEM(w_out.shape, w_out.dtype),
            pltpu.SemaphoreType.DMA((3,)),
        ],
        cost_estimate=pl.CostEstimate(
            flops=2 * samples * tok_width * (
                2 * count * tok_width + 2 * tok_dev * tok_width + 2 * TOKEN_HEADS * tok_dev * count
            ),
            transcendentals=samples * TOKEN_HEADS * tok_dev * count,
            bytes_accessed=2 * 4 * tok_width * tok_width
            + 2 * samples * (count + 2 * tok_dev) * tok_width
            + 4 * TOKEN_HEADS * tok_dev * count,
        ),
    )(
        every,
        state_t,
        query_t,
        bias,
        key_mask[None, :],
        w_key,
        w_value,
        w_out,
    )
    return (atom_out, token_out)


def solution(mesh):
    return jax.shard_map(
        on_device,
        mesh=mesh,
        in_specs=(
            P(("groups", "row"), None, None),
            P(("groups", "row")),
            P("groups"),
            P(("groups", "row"), None, None),
            P(("groups", "row"), None, None),
            P("groups"),
            P(),
            P(),
            P(),
            P(),
            P(),
            P(),
            P(),
            P(),
            P(),
            P(),
        ),
        out_specs=(P(("groups", "row"), None, None), P(("groups", "row"), None, None)),
        check_vma=False,
    )
```

```python
import functools
import math

import jax
import jax.numpy as jnp
from jax import lax
from jax.experimental import pallas as pl
from jax.experimental.pallas import tpu as pltpu
from jax.sharding import PartitionSpec as P

ATOM_HEADS = 4
QBLOCK = 32
KWIN = 128
SHIFT = 16
TOKEN_HEADS = 16


def layer_norm(values):
    values = values.astype(jnp.float32)
    mean = jnp.mean(values, axis=-1, keepdims=True)
    var = jnp.mean((values - mean) ** 2, axis=-1, keepdims=True)
    return (values - mean) / jnp.sqrt(var + 1e-05)


def project(values, weight):
    return jnp.einsum("asc,cd->asd", values, weight, preferred_element_type=jnp.float32)


def shifted(block, axis, step):
    count = lax.axis_size(axis)
    route = [(i, i + step) for i in range(count) if 0 <= i + step < count]
    return lax.ppermute(block, axis, route)


def atom_kernel(
    own_ref,
    low_ref,
    upper_ref,
    shift_ref,
    wq_ref,
    wk_ref,
    wv_ref,
    wo_ref,
    wt_ref,
    ids_ref,
    token_ref,
    wq_hbm,
    atom_ref,
    state_ref,
    query_ref,
    wtq_ref,
    sems,
    *,
    atom_dev,
    rows,
    low_rows,
    high_rows,
    head_dim,
    devices,
):
    f32, bf16 = jnp.float32, jnp.bfloat16
    copies = [pltpu.make_async_copy(wq_hbm, wtq_ref, sems.at[0])]
    for copy in copies:
        copy.start()
    _, samples, width = own_ref.shape
    ext_rows = low_rows + atom_dev + high_rows
    lane = lax.broadcasted_iota(jnp.int32, (1, width), 1) // head_dim
    head_masks = [(lane == h).astype(f32) for h in range(ATOM_HEADS)]
    root = jnp.float32(math.sqrt(head_dim))
    rank = lax.axis_index("row")
    base = rank * atom_dev
    total = devices * atom_dev
    tok_dev = token_ref.shape[0]
    row_block = lax.broadcasted_iota(jnp.int32, (rows, 1), 0) // QBLOCK
    next_shift = upper_ref[pl.ds(atom_dev, 1), 0, :].astype(f32)[:, 0:1].astype(jnp.int32)
    shift = jnp.where(row_block == rows // QBLOCK - 1, next_shift, 0)
    for j in range(rows // QBLOCK - 1):
        shift = shift + jnp.where(row_block == j, shift_ref[j], 0)
    first = row_block * QBLOCK + SHIFT + shift
    lo = jnp.maximum(first, low_rows - base)
    hi = jnp.minimum(first + KWIN, total - base + low_rows)
    column = lax.broadcasted_iota(jnp.int32, (rows, ext_rows), 1)
    keep = (column >= lo) & (column < hi)
    keep_all = jnp.concatenate([keep] * ATOM_HEADS, axis=0)
    own_start = pl.multiple_of(base, atom_dev)
    next_start = pl.multiple_of(jnp.minimum(base + atom_dev, total - atom_dev), atom_dev)
    next_ids = ids_ref[:, pl.ds(next_start, atom_dev)][:, 0 : rows - atom_dev]
    next_ids = jnp.where(rank < devices - 1, next_ids, -1)
    row_ids = jnp.concatenate([ids_ref[:, pl.ds(own_start, atom_dev)], next_ids], axis=1)
    own_ids = rank * tok_dev + lax.broadcasted_iota(jnp.int32, (tok_dev, 1), 0)
    onehot = (own_ids == row_ids).astype(f32)
    counts = jnp.sum(onehot, axis=1, keepdims=True)
    onehot = onehot.astype(bf16)
    xs, xns = [], []
    for s in range(samples):
        x = jnp.concatenate(
            [
                low_ref[atom_dev - low_rows : atom_dev, s, :],
                own_ref[:, s, :],
                upper_ref[0:high_rows, s, :],
            ],
            axis=0,
        ).astype(f32)
        mean = jnp.mean(x, axis=-1, keepdims=True)
        var = jnp.mean((x - mean) ** 2, axis=-1, keepdims=True)
        xs.append(x)
        xns.append(((x - mean) / jnp.sqrt(var + 1e-05)).astype(bf16))
    xn_all = jnp.concatenate(xns, axis=0)
    q_all = jnp.dot(
        jnp.concatenate([xn[low_rows : low_rows + rows] for xn in xns], axis=0),
        wq_ref[...],
        preferred_element_type=f32,
    ).astype(bf16)
    kv_all = jnp.dot(
        xn_all,
        jnp.concatenate([wk_ref[...], wv_ref[...]], axis=1),
        preferred_element_type=f32,
    ).astype(bf16)
    k_all = kv_all[:, 0:width]
    v_all = kv_all[:, width:]
    mixed = []
    for s in range(samples):
        q = q_all[s * rows : (s + 1) * rows]
        k = k_all[s * ext_rows : (s + 1) * ext_rows]
        v = v_all[s * ext_rows : (s + 1) * ext_rows]
        stacked = jnp.concatenate(
            [q * head_masks[h].astype(bf16) for h in range(ATOM_HEADS)], axis=0
        )
        sc = lax.dot_general(
            stacked, k, (((1,), (1,)), ((), ())), preferred_element_type=f32
        ) / root
        sc = jnp.where(keep_all, sc, -1e30)
        top = jnp.max(sc, axis=-1, keepdims=True)
        e = jnp.where(keep_all, jnp.exp(sc - top), 0.0)
        tot = jnp.sum(e, axis=-1, keepdims=True)
        o = jnp.dot(e.astype(bf16), v, preferred_element_type=f32) / tot
        acc = o[0:rows] * head_masks[0]
        for h in range(1, ATOM_HEADS):
            acc = acc + o[h * rows : (h + 1) * rows] * head_masks[h]
        mixed.append(acc.astype(bf16))
    base = jnp.concatenate([x[low_rows : low_rows + rows] for x in xs], axis=0)
    out = (
        base + jnp.dot(jnp.concatenate(mixed, axis=0), wo_ref[...], preferred_element_type=f32)
    ).astype(bf16)
    for s in range(samples):
        atom_ref[:, s, :] = out[s * rows : s * rows + atom_dev]
    hidden = jnp.maximum(jnp.dot(out, wt_ref[...], preferred_element_type=f32), 0.0)
    top_part = hidden.astype(bf16)
    rest = hidden - top_part.astype(f32)
    mid_part = rest.astype(bf16)
    low_part = (rest - mid_part.astype(f32)).astype(bf16)
    zero = jnp.zeros_like(onehot)
    diagonal = jnp.concatenate(
        [
            jnp.concatenate([onehot if c == r else zero for c in range(samples)], axis=1)
            for r in range(samples)
        ],
        axis=0,
    )
    sums = jnp.dot(
        jnp.concatenate([diagonal] * 3, axis=1),
        jnp.concatenate([top_part, mid_part, low_part], axis=0),
        preferred_element_type=f32,
    )
    tns = []
    for s in range(samples):
        st = (token_ref[:, s, :].astype(f32) + sums[s * tok_dev : (s + 1) * tok_dev] / counts)
        st = st.astype(bf16)
        state_ref[s] = st
        st = st.astype(f32)
        mean = jnp.mean(st, axis=-1, keepdims=True)
        var = jnp.mean((st - mean) ** 2, axis=-1, keepdims=True)
        tns.append(((st - mean) / jnp.sqrt(var + 1e-05)).astype(bf16))
    copies[0].wait()
    query = jnp.dot(jnp.concatenate(tns, axis=0), wtq_ref[...], preferred_element_type=f32)
    query = query.astype(bf16)
    for s in range(samples):
        query_ref[s] = query[s * tok_dev : (s + 1) * tok_dev]


def token_kernel(
    every_ref,
    own_ref,
    query_ref,
    bias_ref,
    flags_ref,
    wk_hbm,
    wv_hbm,
    wo_hbm,
    out_ref,
    wk_ref,
    wv_ref,
    wo_ref,
    sems,
    *,
    heads,
):
    copies = [
        pltpu.make_async_copy(src, dst, sems.at[i])
        for i, (src, dst) in enumerate([(wk_hbm, wk_ref), (wv_hbm, wv_ref), (wo_hbm, wo_ref)])
    ]
    for copy in copies:
        copy.start()
    f32, bf16 = jnp.float32, jnp.bfloat16
    samples, tok_dev, width = own_ref.shape
    head_dim = width // heads
    lane = lax.broadcasted_iota(jnp.int32, (1, width), 1) // head_dim
    head_masks = [(lane == h).astype(f32) for h in range(heads)]
    root = jnp.float32(math.sqrt(head_dim))
    keep = flags_ref[...] > 0
    mask_rows = jnp.concatenate(head_masks, axis=0)

    def normed(x):
        mean = jnp.mean(x, axis=-1, keepdims=True)
        var = jnp.mean((x - mean) ** 2, axis=-1, keepdims=True)
        return ((x - mean) / jnp.sqrt(var + 1e-05)).astype(bf16)

    allx = jnp.concatenate([normed(every_ref[s].astype(f32)) for s in range(samples)], axis=0)
    count = every_ref.shape[1]
    copies[0].wait()
    k_all = jnp.dot(allx, wk_ref[...], preferred_element_type=f32).astype(bf16)
    copies[1].wait()
    v_all = jnp.dot(allx, wv_ref[...], preferred_element_type=f32).astype(bf16)
    ks = [k_all[s * count : (s + 1) * count] for s in range(samples)]
    vs = [v_all[s * count : (s + 1) * count] for s in range(samples)]
    bias = bias_ref[...]
    mixes = []
    for s in range(samples):
        q = query_ref[s]
        stacked = jnp.concatenate(
            [q[t : t + 1].astype(f32) * mask_rows for t in range(tok_dev)], axis=0
        ).astype(bf16)
        sc = lax.dot_general(
            stacked, ks[s], (((1,), (1,)), ((), ())), preferred_element_type=f32
        ) / root + bias
        sc = jnp.where(keep, sc, -1e30)
        top = jnp.max(sc, axis=-1, keepdims=True)
        e = jnp.where(keep, jnp.exp(sc - top), 0.0)
        tot = jnp.sum(e, axis=-1, keepdims=True)
        o = jnp.dot(e.astype(bf16), vs[s], preferred_element_type=f32) / tot
        mixes.append(
            jnp.concatenate(
                [
                    jnp.sum(o[t * heads : (t + 1) * heads] * mask_rows, axis=0, keepdims=True)
                    for t in range(tok_dev)
                ],
                axis=0,
            ).astype(bf16)
        )
    copies[2].wait()
    projected = jnp.dot(jnp.concatenate(mixes, axis=0), wo_ref[...], preferred_element_type=f32)
    for s in range(samples):
        own = own_ref[s].astype(f32)
        out_ref[:, s, :] = (own + projected[s * tok_dev : (s + 1) * tok_dev]).astype(bf16)


def on_device(
    atom_feat,
    window_shift,
    atom_token,
    token_in,
    pair,
    key_mask,
    w_atom_query,
    w_atom_key,
    w_atom_value,
    w_atom_out,
    w_to_token,
    w_query,
    w_key,
    w_value,
    w_out,
    w_bias,
):
    high = lax.Precision.HIGHEST
    atom_dev, samples, width = atom_feat.shape
    tok_dev = token_in.shape[0]
    tok_width = token_in.shape[2]
    devices = lax.axis_size("row")
    rank = lax.axis_index("row")
    atom_base = rank * atom_dev
    total_atoms = atom_dev * devices
    margin = (KWIN - QBLOCK) // 2
    low_rows = margin + SHIFT
    span = KWIN + 2 * SHIFT
    high_rows = span - low_rows
    blocks = atom_dev // QBLOCK + 1

    low = shifted(atom_feat, "row", 1)
    shift_row = jnp.broadcast_to(window_shift[0], (1, samples, width)).astype(jnp.bfloat16)
    upper = shifted(jnp.concatenate([atom_feat, shift_row], axis=0), "row", -1)

    head_dim = width // ATOM_HEADS
    rows = blocks * QBLOCK
    ext_rows = low_rows + atom_dev + high_rows
    kernel = functools.partial(
        atom_kernel,
        atom_dev=atom_dev,
        rows=rows,
        low_rows=low_rows,
        high_rows=high_rows,
        head_dim=head_dim,
        devices=devices,
    )
    vmem = pl.BlockSpec(memory_space=pltpu.VMEM)
    flops = 2 * samples * (
        ext_rows * width * 3 * width
        + rows * width * (width + tok_width)
        + ATOM_HEADS * rows * ext_rows * width * 2
        + 3 * tok_dev * rows * tok_width
    )
    hbm = pl.BlockSpec(memory_space=pl.ANY)
    count = tok_dev * devices
    atom_out, state_t, query_t = pl.pallas_call(
        kernel,
        out_shape=(
            jax.ShapeDtypeStruct((atom_dev, samples, width), jnp.bfloat16),
            jax.ShapeDtypeStruct((samples, tok_dev, tok_width), jnp.bfloat16),
            jax.ShapeDtypeStruct((samples, tok_dev, tok_width), jnp.bfloat16),
        ),
        in_specs=[vmem] * 3
        + [pl.BlockSpec(memory_space=pltpu.SMEM)]
        + [vmem] * 7
        + [hbm],
        out_specs=(vmem, vmem, vmem),
        scratch_shapes=[
            pltpu.VMEM(w_query.shape, w_query.dtype),
            pltpu.SemaphoreType.DMA((1,)),
        ],
        cost_estimate=pl.CostEstimate(
            flops=flops,
            transcendentals=samples * ATOM_HEADS * rows * ext_rows,
            bytes_accessed=2 * (ext_rows + atom_dev) * samples * width
            + 2 * width * (3 * width + width + tok_width)
            + 4 * samples * tok_dev * tok_width,
        ),
    )(
        atom_feat,
        low,
        upper,
        window_shift,
        w_atom_query,
        w_atom_key,
        w_atom_value,
        w_atom_out,
        w_to_token,
        atom_token[None, :],
        token_in,
        w_query,
    )
    bias = jnp.einsum("qkc,ch->qhk", pair, w_bias, preferred_element_type=jnp.float32)
    bias = bias.reshape(tok_dev * TOKEN_HEADS, count)

    every = lax.all_gather(state_t, "row", axis=1, tiled=True)
    token_out = pl.pallas_call(
        functools.partial(token_kernel, heads=TOKEN_HEADS),
        out_shape=jax.ShapeDtypeStruct((tok_dev, samples, tok_width), jnp.bfloat16),
        in_specs=[vmem, vmem, vmem, vmem, vmem, hbm, hbm, hbm],
        out_specs=vmem,
        scratch_shapes=[
            pltpu.VMEM(w_key.shape, w_key.dtype),
            pltpu.VMEM(w_value.shape, w_value.dtype),
            pltpu.VMEM(w_out.shape, w_out.dtype),
            pltpu.SemaphoreType.DMA((3,)),
        ],
        cost_estimate=pl.CostEstimate(
            flops=2 * samples * tok_width * (
                2 * count * tok_width + 2 * tok_dev * tok_width + 2 * TOKEN_HEADS * tok_dev * count
            ),
            transcendentals=samples * TOKEN_HEADS * tok_dev * count,
            bytes_accessed=2 * 4 * tok_width * tok_width
            + 2 * samples * (count + 2 * tok_dev) * tok_width
            + 4 * TOKEN_HEADS * tok_dev * count,
        ),
    )(
        every,
        state_t,
        query_t,
        bias,
        key_mask[None, :],
        w_key,
        w_value,
        w_out,
    )
    return (atom_out, token_out)


def solution(mesh):
    return jax.shard_map(
        on_device,
        mesh=mesh,
        in_specs=(
            P(("groups", "row"), None, None),
            P(("groups", "row")),
            P("groups"),
            P(("groups", "row"), None, None),
            P(("groups", "row"), None, None),
            P("groups"),
            P(),
            P(),
            P(),
            P(),
            P(),
            P(),
            P(),
            P(),
            P(),
            P(),
        ),
        out_specs=(P(("groups", "row"), None, None), P(("groups", "row"), None, None)),
        check_vma=False,
    )
```

```python
import functools
import math

import jax
import jax.numpy as jnp
from jax import lax
from jax.experimental import pallas as pl
from jax.experimental.pallas import tpu as pltpu
from jax.sharding import PartitionSpec as P

ATOM_HEADS = 4
QBLOCK = 32
KWIN = 128
SHIFT = 16
TOKEN_HEADS = 16


def layer_norm(values):
    values = values.astype(jnp.float32)
    mean = jnp.mean(values, axis=-1, keepdims=True)
    var = jnp.mean((values - mean) ** 2, axis=-1, keepdims=True)
    return (values - mean) / jnp.sqrt(var + 1e-05)


def project(values, weight):
    return jnp.einsum("asc,cd->asd", values, weight, preferred_element_type=jnp.float32)


def shifted(block, axis, step):
    count = lax.axis_size(axis)
    route = [(i, i + step) for i in range(count) if 0 <= i + step < count]
    return lax.ppermute(block, axis, route)


def atom_kernel(
    own_ref,
    low_ref,
    upper_ref,
    shift_ref,
    wq_ref,
    wk_ref,
    wv_ref,
    wo_ref,
    wt_ref,
    ids_ref,
    token_ref,
    wq_hbm,
    atom_ref,
    state_ref,
    query_ref,
    wtq_ref,
    sems,
    *,
    atom_dev,
    rows,
    low_rows,
    high_rows,
    head_dim,
    devices,
):
    f32, bf16 = jnp.float32, jnp.bfloat16
    copies = [pltpu.make_async_copy(wq_hbm, wtq_ref, sems.at[0])]
    for copy in copies:
        copy.start()
    _, samples, width = own_ref.shape
    ext_rows = low_rows + atom_dev + high_rows
    lane = lax.broadcasted_iota(jnp.int32, (1, width), 1) // head_dim
    head_masks = [(lane == h).astype(f32) for h in range(ATOM_HEADS)]
    root = jnp.float32(math.sqrt(head_dim))
    rank = lax.axis_index("row")
    base = rank * atom_dev
    total = devices * atom_dev
    tok_dev = token_ref.shape[0]
    row_block = lax.broadcasted_iota(jnp.int32, (rows, 1), 0) // QBLOCK
    next_shift = upper_ref[pl.ds(atom_dev, 1), 0, :].astype(f32)[:, 0:1].astype(jnp.int32)
    shift = jnp.where(row_block == rows // QBLOCK - 1, next_shift, 0)
    for j in range(rows // QBLOCK - 1):
        shift = shift + jnp.where(row_block == j, shift_ref[j], 0)
    first = row_block * QBLOCK + SHIFT + shift
    lo = jnp.maximum(first, low_rows - base)
    hi = jnp.minimum(first + KWIN, total - base + low_rows)
    column = lax.broadcasted_iota(jnp.int32, (rows, ext_rows), 1)
    keep = (column >= lo) & (column < hi)
    keep_all = jnp.concatenate([keep] * ATOM_HEADS, axis=0)
    own_start = pl.multiple_of(base, atom_dev)
    next_start = pl.multiple_of(jnp.minimum(base + atom_dev, total - atom_dev), atom_dev)
    next_ids = ids_ref[:, pl.ds(next_start, atom_dev)][:, 0 : rows - atom_dev]
    next_ids = jnp.where(rank < devices - 1, next_ids, -1)
    row_ids = jnp.concatenate([ids_ref[:, pl.ds(own_start, atom_dev)], next_ids], axis=1)
    own_ids = rank * tok_dev + lax.broadcasted_iota(jnp.int32, (tok_dev, 1), 0)
    onehot = (own_ids == row_ids).astype(f32)
    counts = jnp.sum(onehot, axis=1, keepdims=True)
    onehot = onehot.astype(bf16)
    xs, xns = [], []
    for s in range(samples):
        x = jnp.concatenate(
            [
                low_ref[atom_dev - low_rows : atom_dev, s, :],
                own_ref[:, s, :],
                upper_ref[0:high_rows, s, :],
            ],
            axis=0,
        ).astype(f32)
        mean = jnp.mean(x, axis=-1, keepdims=True)
        var = jnp.mean((x - mean) ** 2, axis=-1, keepdims=True)
        xs.append(x)
        xns.append(((x - mean) / jnp.sqrt(var + 1e-05)).astype(bf16))
    xn_all = jnp.concatenate(xns, axis=0)
    q_all = jnp.dot(
        jnp.concatenate([xn[low_rows : low_rows + rows] for xn in xns], axis=0),
        wq_ref[...],
        preferred_element_type=f32,
    ).astype(bf16)
    k_all = jnp.dot(xn_all, wk_ref[...], preferred_element_type=f32).astype(bf16)
    v_all = jnp.dot(xn_all, wv_ref[...], preferred_element_type=f32).astype(bf16)
    mixed = []
    for s in range(samples):
        q = q_all[s * rows : (s + 1) * rows]
        k = k_all[s * ext_rows : (s + 1) * ext_rows]
        v = v_all[s * ext_rows : (s + 1) * ext_rows]
        stacked = jnp.concatenate(
            [q * head_masks[h].astype(bf16) for h in range(ATOM_HEADS)], axis=0
        )
        sc = lax.dot_general(
            stacked, k, (((1,), (1,)), ((), ())), preferred_element_type=f32
        ) / root
        sc = jnp.where(keep_all, sc, -1e30)
        top = jnp.max(sc, axis=-1, keepdims=True)
        e = jnp.where(keep_all, jnp.exp(sc - top), 0.0)
        tot = jnp.sum(e, axis=-1, keepdims=True)
        o = jnp.dot(e.astype(bf16), v, preferred_element_type=f32) / tot
        acc = o[0:rows] * head_masks[0]
        for h in range(1, ATOM_HEADS):
            acc = acc + o[h * rows : (h + 1) * rows] * head_masks[h]
        mixed.append(acc.astype(bf16))
    base = jnp.concatenate([x[low_rows : low_rows + rows] for x in xs], axis=0)
    out = (
        base + jnp.dot(jnp.concatenate(mixed, axis=0), wo_ref[...], preferred_element_type=f32)
    ).astype(bf16)
    for s in range(samples):
        atom_ref[:, s, :] = out[s * rows : s * rows + atom_dev]
    hidden = jnp.maximum(jnp.dot(out, wt_ref[...], preferred_element_type=f32), 0.0)
    top_part = hidden.astype(bf16)
    rest = hidden - top_part.astype(f32)
    mid_part = rest.astype(bf16)
    low_part = (rest - mid_part.astype(f32)).astype(bf16)
    zero = jnp.zeros_like(onehot)
    diagonal = jnp.concatenate(
        [
            jnp.concatenate([onehot if c == r else zero for c in range(samples)], axis=1)
            for r in range(samples)
        ],
        axis=0,
    )
    sums = (
        jnp.dot(diagonal, top_part, preferred_element_type=f32)
        + jnp.dot(diagonal, mid_part, preferred_element_type=f32)
        + jnp.dot(diagonal, low_part, preferred_element_type=f32)
    )
    tns = []
    for s in range(samples):
        st = (token_ref[:, s, :].astype(f32) + sums[s * tok_dev : (s + 1) * tok_dev] / counts)
        st = st.astype(bf16)
        state_ref[s] = st
        st = st.astype(f32)
        mean = jnp.mean(st, axis=-1, keepdims=True)
        var = jnp.mean((st - mean) ** 2, axis=-1, keepdims=True)
        tns.append(((st - mean) / jnp.sqrt(var + 1e-05)).astype(bf16))
    copies[0].wait()
    query = jnp.dot(jnp.concatenate(tns, axis=0), wtq_ref[...], preferred_element_type=f32)
    query = query.astype(bf16)
    for s in range(samples):
        query_ref[s] = query[s * tok_dev : (s + 1) * tok_dev]


def token_kernel(
    every_ref,
    own_ref,
    query_ref,
    bias_ref,
    flags_ref,
    wk_hbm,
    wv_hbm,
    wo_hbm,
    out_ref,
    wk_ref,
    wv_ref,
    wo_ref,
    sems,
    *,
    heads,
):
    copies = [
        pltpu.make_async_copy(src, dst, sems.at[i])
        for i, (src, dst) in enumerate([(wk_hbm, wk_ref), (wv_hbm, wv_ref), (wo_hbm, wo_ref)])
    ]
    for copy in copies:
        copy.start()
    f32, bf16 = jnp.float32, jnp.bfloat16
    samples, tok_dev, width = own_ref.shape
    head_dim = width // heads
    lane = lax.broadcasted_iota(jnp.int32, (1, width), 1) // head_dim
    head_masks = [(lane == h).astype(f32) for h in range(heads)]
    root = jnp.float32(math.sqrt(head_dim))
    keep = flags_ref[...] > 0
    mask_rows = jnp.concatenate(head_masks, axis=0)

    def normed(x):
        mean = jnp.mean(x, axis=-1, keepdims=True)
        var = jnp.mean((x - mean) ** 2, axis=-1, keepdims=True)
        return ((x - mean) / jnp.sqrt(var + 1e-05)).astype(bf16)

    allx = jnp.concatenate([normed(every_ref[s].astype(f32)) for s in range(samples)], axis=0)
    count = every_ref.shape[1]
    copies[0].wait()
    k_all = jnp.dot(allx, wk_ref[...], preferred_element_type=f32).astype(bf16)
    copies[1].wait()
    v_all = jnp.dot(allx, wv_ref[...], preferred_element_type=f32).astype(bf16)
    ks = [k_all[s * count : (s + 1) * count] for s in range(samples)]
    vs = [v_all[s * count : (s + 1) * count] for s in range(samples)]
    bias = bias_ref[...]
    mixes = []
    for s in range(samples):
        q = query_ref[s]
        stacked = (q[:, None, :] * mask_rows.astype(bf16)[None, :, :]).reshape(
            tok_dev * heads, width
        )
        sc = lax.dot_general(
            stacked, ks[s], (((1,), (1,)), ((), ())), preferred_element_type=f32
        ) / root + bias
        sc = jnp.where(keep, sc, -1e30)
        top = jnp.max(sc, axis=-1, keepdims=True)
        e = jnp.where(keep, jnp.exp(sc - top), 0.0)
        tot = jnp.sum(e, axis=-1, keepdims=True)
        o = jnp.dot(e.astype(bf16), vs[s], preferred_element_type=f32) / tot
        picked = o.reshape(tok_dev, heads, width) * mask_rows[None, :, :]
        mixes.append(jnp.sum(picked, axis=1).astype(bf16))
    copies[2].wait()
    projected = jnp.dot(jnp.concatenate(mixes, axis=0), wo_ref[...], preferred_element_type=f32)
    for s in range(samples):
        own = own_ref[s].astype(f32)
        out_ref[:, s, :] = (own + projected[s * tok_dev : (s + 1) * tok_dev]).astype(bf16)


def on_device(
    atom_feat,
    window_shift,
    atom_token,
    token_in,
    pair,
    key_mask,
    w_atom_query,
    w_atom_key,
    w_atom_value,
    w_atom_out,
    w_to_token,
    w_query,
    w_key,
    w_value,
    w_out,
    w_bias,
):
    high = lax.Precision.HIGHEST
    atom_dev, samples, width = atom_feat.shape
    tok_dev = token_in.shape[0]
    tok_width = token_in.shape[2]
    devices = lax.axis_size("row")
    rank = lax.axis_index("row")
    atom_base = rank * atom_dev
    total_atoms = atom_dev * devices
    margin = (KWIN - QBLOCK) // 2
    low_rows = margin + SHIFT
    span = KWIN + 2 * SHIFT
    high_rows = span - low_rows
    blocks = atom_dev // QBLOCK + 1

    low = shifted(atom_feat, "row", 1)
    shift_row = jnp.broadcast_to(window_shift[0], (1, samples, width)).astype(jnp.bfloat16)
    upper = shifted(jnp.concatenate([atom_feat, shift_row], axis=0), "row", -1)

    head_dim = width // ATOM_HEADS
    rows = blocks * QBLOCK
    ext_rows = low_rows + atom_dev + high_rows
    kernel = functools.partial(
        atom_kernel,
        atom_dev=atom_dev,
        rows=rows,
        low_rows=low_rows,
        high_rows=high_rows,
        head_dim=head_dim,
        devices=devices,
    )
    vmem = pl.BlockSpec(memory_space=pltpu.VMEM)
    flops = 2 * samples * (
        ext_rows * width * 3 * width
        + rows * width * (width + tok_width)
        + ATOM_HEADS * rows * ext_rows * width * 2
        + 3 * tok_dev * rows * tok_width
    )
    hbm = pl.BlockSpec(memory_space=pl.ANY)
    count = tok_dev * devices
    atom_out, state_t, query_t = pl.pallas_call(
        kernel,
        out_shape=(
            jax.ShapeDtypeStruct((atom_dev, samples, width), jnp.bfloat16),
            jax.ShapeDtypeStruct((samples, tok_dev, tok_width), jnp.bfloat16),
            jax.ShapeDtypeStruct((samples, tok_dev, tok_width), jnp.bfloat16),
        ),
        in_specs=[vmem] * 3
        + [pl.BlockSpec(memory_space=pltpu.SMEM)]
        + [vmem] * 7
        + [hbm],
        out_specs=(vmem, vmem, vmem),
        scratch_shapes=[
            pltpu.VMEM(w_query.shape, w_query.dtype),
            pltpu.SemaphoreType.DMA((1,)),
        ],
        cost_estimate=pl.CostEstimate(
            flops=flops,
            transcendentals=samples * ATOM_HEADS * rows * ext_rows,
            bytes_accessed=2 * (ext_rows + atom_dev) * samples * width
            + 2 * width * (3 * width + width + tok_width)
            + 4 * samples * tok_dev * tok_width,
        ),
    )(
        atom_feat,
        low,
        upper,
        window_shift,
        w_atom_query,
        w_atom_key,
        w_atom_value,
        w_atom_out,
        w_to_token,
        atom_token[None, :],
        token_in,
        w_query,
    )
    bias = jnp.einsum("qkc,ch->qhk", pair, w_bias, preferred_element_type=jnp.float32)
    bias = bias.reshape(tok_dev * TOKEN_HEADS, count)

    every = lax.all_gather(state_t, "row", axis=1, tiled=True)
    token_out = pl.pallas_call(
        functools.partial(token_kernel, heads=TOKEN_HEADS),
        out_shape=jax.ShapeDtypeStruct((tok_dev, samples, tok_width), jnp.bfloat16),
        in_specs=[vmem, vmem, vmem, vmem, vmem, hbm, hbm, hbm],
        out_specs=vmem,
        scratch_shapes=[
            pltpu.VMEM(w_key.shape, w_key.dtype),
            pltpu.VMEM(w_value.shape, w_value.dtype),
            pltpu.VMEM(w_out.shape, w_out.dtype),
            pltpu.SemaphoreType.DMA((3,)),
        ],
        cost_estimate=pl.CostEstimate(
            flops=2 * samples * tok_width * (
                2 * count * tok_width + 2 * tok_dev * tok_width + 2 * TOKEN_HEADS * tok_dev * count
            ),
            transcendentals=samples * TOKEN_HEADS * tok_dev * count,
            bytes_accessed=2 * 4 * tok_width * tok_width
            + 2 * samples * (count + 2 * tok_dev) * tok_width
            + 4 * TOKEN_HEADS * tok_dev * count,
        ),
    )(
        every,
        state_t,
        query_t,
        bias,
        key_mask[None, :],
        w_key,
        w_value,
        w_out,
    )
    return (atom_out, token_out)


def solution(mesh):
    return jax.shard_map(
        on_device,
        mesh=mesh,
        in_specs=(
            P(("groups", "row"), None, None),
            P(("groups", "row")),
            P("groups"),
            P(("groups", "row"), None, None),
            P(("groups", "row"), None, None),
            P("groups"),
            P(),
            P(),
            P(),
            P(),
            P(),
            P(),
            P(),
            P(),
            P(),
            P(),
        ),
        out_specs=(P(("groups", "row"), None, None), P(("groups", "row"), None, None)),
        check_vma=False,
    )
```

```python
import functools
import math

import jax
import jax.numpy as jnp
from jax import lax
from jax.experimental import pallas as pl
from jax.experimental.pallas import tpu as pltpu
from jax.sharding import PartitionSpec as P

ATOM_HEADS = 4
QBLOCK = 32
KWIN = 128
SHIFT = 16
TOKEN_HEADS = 16


def layer_norm(values):
    values = values.astype(jnp.float32)
    mean = jnp.mean(values, axis=-1, keepdims=True)
    var = jnp.mean((values - mean) ** 2, axis=-1, keepdims=True)
    return (values - mean) / jnp.sqrt(var + 1e-05)


def project(values, weight):
    return jnp.einsum("asc,cd->asd", values, weight, preferred_element_type=jnp.float32)


def shifted(block, axis, step):
    count = lax.axis_size(axis)
    route = [(i, i + step) for i in range(count) if 0 <= i + step < count]
    return lax.ppermute(block, axis, route)


def atom_kernel(
    own_ref,
    low_ref,
    upper_ref,
    shift_ref,
    wq_ref,
    wk_ref,
    wv_ref,
    wo_ref,
    wt_ref,
    ids_ref,
    token_ref,
    wq_hbm,
    atom_ref,
    state_ref,
    query_ref,
    wtq_ref,
    sems,
    *,
    atom_dev,
    rows,
    low_rows,
    high_rows,
    head_dim,
    devices,
):
    f32, bf16 = jnp.float32, jnp.bfloat16
    copies = [pltpu.make_async_copy(wq_hbm, wtq_ref, sems.at[0])]
    for copy in copies:
        copy.start()
    _, samples, width = own_ref.shape
    ext_rows = low_rows + atom_dev + high_rows
    lane = lax.broadcasted_iota(jnp.int32, (1, width), 1) // head_dim
    head_block = (
        lax.broadcasted_iota(jnp.int32, (ATOM_HEADS, 1, width), 2) // head_dim
        == lax.broadcasted_iota(jnp.int32, (ATOM_HEADS, 1, width), 0)
    ).astype(f32)
    root = jnp.float32(math.sqrt(head_dim))
    rank = lax.axis_index("row")
    base = rank * atom_dev
    total = devices * atom_dev
    tok_dev = token_ref.shape[0]
    row_block = lax.broadcasted_iota(jnp.int32, (rows, 1), 0) // QBLOCK
    next_shift = upper_ref[pl.ds(atom_dev, 1), 0, :].astype(f32)[:, 0:1].astype(jnp.int32)
    shift = jnp.where(row_block == rows // QBLOCK - 1, next_shift, 0)
    for j in range(rows // QBLOCK - 1):
        shift = shift + jnp.where(row_block == j, shift_ref[j], 0)
    first = row_block * QBLOCK + SHIFT + shift
    lo = jnp.maximum(first, low_rows - base)
    hi = jnp.minimum(first + KWIN, total - base + low_rows)
    column = lax.broadcasted_iota(jnp.int32, (rows, ext_rows), 1)
    keep = (column >= lo) & (column < hi)
    keep_all = jnp.concatenate([keep] * ATOM_HEADS, axis=0)
    own_start = pl.multiple_of(base, atom_dev)
    next_start = pl.multiple_of(jnp.minimum(base + atom_dev, total - atom_dev), atom_dev)
    next_ids = ids_ref[:, pl.ds(next_start, atom_dev)][:, 0 : rows - atom_dev]
    next_ids = jnp.where(rank < devices - 1, next_ids, -1)
    row_ids = jnp.concatenate([ids_ref[:, pl.ds(own_start, atom_dev)], next_ids], axis=1)
    own_ids = rank * tok_dev + lax.broadcasted_iota(jnp.int32, (tok_dev, 1), 0)
    onehot = (own_ids == row_ids).astype(f32)
    counts = jnp.sum(onehot, axis=1, keepdims=True)
    onehot = onehot.astype(bf16)
    xs, xns = [], []
    for s in range(samples):
        x = jnp.concatenate(
            [
                low_ref[atom_dev - low_rows : atom_dev, s, :],
                own_ref[:, s, :],
                upper_ref[0:high_rows, s, :],
            ],
            axis=0,
        ).astype(f32)
        mean = jnp.mean(x, axis=-1, keepdims=True)
        var = jnp.mean((x - mean) ** 2, axis=-1, keepdims=True)
        xs.append(x)
        xns.append(((x - mean) / jnp.sqrt(var + 1e-05)).astype(bf16))
    xn_all = jnp.concatenate(xns, axis=0)
    q_all = jnp.dot(
        jnp.concatenate([xn[low_rows : low_rows + rows] for xn in xns], axis=0),
        wq_ref[...],
        preferred_element_type=f32,
    ).astype(bf16)
    k_all = jnp.dot(xn_all, wk_ref[...], preferred_element_type=f32).astype(bf16)
    v_all = jnp.dot(xn_all, wv_ref[...], preferred_element_type=f32).astype(bf16)
    mixed = []
    for s in range(samples):
        q = q_all[s * rows : (s + 1) * rows]
        k = k_all[s * ext_rows : (s + 1) * ext_rows]
        v = v_all[s * ext_rows : (s + 1) * ext_rows]
        stacked = (q[None, :, :] * head_block.astype(bf16)).reshape(ATOM_HEADS * rows, width)
        sc = lax.dot_general(
            stacked, k, (((1,), (1,)), ((), ())), preferred_element_type=f32
        ) / root
        sc = jnp.where(keep_all, sc, -1e30)
        top = jnp.max(sc, axis=-1, keepdims=True)
        e = jnp.where(keep_all, jnp.exp(sc - top), 0.0)
        tot = jnp.sum(e, axis=-1, keepdims=True)
        o = jnp.dot(e.astype(bf16), v, preferred_element_type=f32) / tot
        acc = jnp.sum(o.reshape(ATOM_HEADS, rows, width) * head_block, axis=0)
        mixed.append(acc.astype(bf16))
    base = jnp.concatenate([x[low_rows : low_rows + rows] for x in xs], axis=0)
    out = (
        base + jnp.dot(jnp.concatenate(mixed, axis=0), wo_ref[...], preferred_element_type=f32)
    ).astype(bf16)
    for s in range(samples):
        atom_ref[:, s, :] = out[s * rows : s * rows + atom_dev]
    hidden = jnp.maximum(jnp.dot(out, wt_ref[...], preferred_element_type=f32), 0.0)
    top_part = hidden.astype(bf16)
    rest = hidden - top_part.astype(f32)
    mid_part = rest.astype(bf16)
    low_part = (rest - mid_part.astype(f32)).astype(bf16)
    zero = jnp.zeros_like(onehot)
    diagonal = jnp.concatenate(
        [
            jnp.concatenate([onehot if c == r else zero for c in range(samples)], axis=1)
            for r in range(samples)
        ],
        axis=0,
    )
    sums = (
        jnp.dot(diagonal, top_part, preferred_element_type=f32)
        + jnp.dot(diagonal, mid_part, preferred_element_type=f32)
        + jnp.dot(diagonal, low_part, preferred_element_type=f32)
    )
    tns = []
    for s in range(samples):
        st = (token_ref[:, s, :].astype(f32) + sums[s * tok_dev : (s + 1) * tok_dev] / counts)
        st = st.astype(bf16)
        state_ref[s] = st
        st = st.astype(f32)
        mean = jnp.mean(st, axis=-1, keepdims=True)
        var = jnp.mean((st - mean) ** 2, axis=-1, keepdims=True)
        tns.append(((st - mean) / jnp.sqrt(var + 1e-05)).astype(bf16))
    copies[0].wait()
    query = jnp.dot(jnp.concatenate(tns, axis=0), wtq_ref[...], preferred_element_type=f32)
    query = query.astype(bf16)
    for s in range(samples):
        query_ref[s] = query[s * tok_dev : (s + 1) * tok_dev]


def token_kernel(
    every_ref,
    own_ref,
    query_ref,
    bias_ref,
    flags_ref,
    wk_hbm,
    wv_hbm,
    wo_hbm,
    out_ref,
    wk_ref,
    wv_ref,
    wo_ref,
    sems,
    *,
    heads,
):
    copies = [
        pltpu.make_async_copy(src, dst, sems.at[i])
        for i, (src, dst) in enumerate([(wk_hbm, wk_ref), (wv_hbm, wv_ref), (wo_hbm, wo_ref)])
    ]
    for copy in copies:
        copy.start()
    f32, bf16 = jnp.float32, jnp.bfloat16
    samples, tok_dev, width = own_ref.shape
    head_dim = width // heads
    lane = lax.broadcasted_iota(jnp.int32, (1, width), 1) // head_dim
    head_masks = [(lane == h).astype(f32) for h in range(heads)]
    root = jnp.float32(math.sqrt(head_dim))
    keep = flags_ref[...] > 0
    mask_rows = jnp.concatenate(head_masks, axis=0)

    def normed(x):
        mean = jnp.mean(x, axis=-1, keepdims=True)
        var = jnp.mean((x - mean) ** 2, axis=-1, keepdims=True)
        return ((x - mean) / jnp.sqrt(var + 1e-05)).astype(bf16)

    allx = jnp.concatenate([normed(every_ref[s].astype(f32)) for s in range(samples)], axis=0)
    count = every_ref.shape[1]
    copies[0].wait()
    k_all = jnp.dot(allx, wk_ref[...], preferred_element_type=f32).astype(bf16)
    copies[1].wait()
    v_all = jnp.dot(allx, wv_ref[...], preferred_element_type=f32).astype(bf16)
    ks = [k_all[s * count : (s + 1) * count] for s in range(samples)]
    vs = [v_all[s * count : (s + 1) * count] for s in range(samples)]
    bias = bias_ref[...]
    mixes = []
    for s in range(samples):
        q = query_ref[s]
        stacked = (q[:, None, :] * mask_rows.astype(bf16)[None, :, :]).reshape(
            tok_dev * heads, width
        )
        sc = lax.dot_general(
            stacked, ks[s], (((1,), (1,)), ((), ())), preferred_element_type=f32
        ) / root + bias
        sc = jnp.where(keep, sc, -1e30)
        top = jnp.max(sc, axis=-1, keepdims=True)
        e = jnp.where(keep, jnp.exp(sc - top), 0.0)
        tot = jnp.sum(e, axis=-1, keepdims=True)
        o = jnp.dot(e.astype(bf16), vs[s], preferred_element_type=f32) / tot
        picked = o.reshape(tok_dev, heads, width) * mask_rows[None, :, :]
        mixes.append(jnp.sum(picked, axis=1).astype(bf16))
    copies[2].wait()
    projected = jnp.dot(jnp.concatenate(mixes, axis=0), wo_ref[...], preferred_element_type=f32)
    for s in range(samples):
        own = own_ref[s].astype(f32)
        out_ref[:, s, :] = (own + projected[s * tok_dev : (s + 1) * tok_dev]).astype(bf16)


def on_device(
    atom_feat,
    window_shift,
    atom_token,
    token_in,
    pair,
    key_mask,
    w_atom_query,
    w_atom_key,
    w_atom_value,
    w_atom_out,
    w_to_token,
    w_query,
    w_key,
    w_value,
    w_out,
    w_bias,
):
    high = lax.Precision.HIGHEST
    atom_dev, samples, width = atom_feat.shape
    tok_dev = token_in.shape[0]
    tok_width = token_in.shape[2]
    devices = lax.axis_size("row")
    rank = lax.axis_index("row")
    atom_base = rank * atom_dev
    total_atoms = atom_dev * devices
    margin = (KWIN - QBLOCK) // 2
    low_rows = margin + SHIFT
    span = KWIN + 2 * SHIFT
    high_rows = span - low_rows
    blocks = atom_dev // QBLOCK + 1

    low = shifted(atom_feat, "row", 1)
    shift_row = jnp.broadcast_to(window_shift[0], (1, samples, width)).astype(jnp.bfloat16)
    upper = shifted(jnp.concatenate([atom_feat, shift_row], axis=0), "row", -1)

    head_dim = width // ATOM_HEADS
    rows = blocks * QBLOCK
    ext_rows = low_rows + atom_dev + high_rows
    kernel = functools.partial(
        atom_kernel,
        atom_dev=atom_dev,
        rows=rows,
        low_rows=low_rows,
        high_rows=high_rows,
        head_dim=head_dim,
        devices=devices,
    )
    vmem = pl.BlockSpec(memory_space=pltpu.VMEM)
    flops = 2 * samples * (
        ext_rows * width * 3 * width
        + rows * width * (width + tok_width)
        + ATOM_HEADS * rows * ext_rows * width * 2
        + 3 * tok_dev * rows * tok_width
    )
    hbm = pl.BlockSpec(memory_space=pl.ANY)
    count = tok_dev * devices
    atom_out, state_t, query_t = pl.pallas_call(
        kernel,
        out_shape=(
            jax.ShapeDtypeStruct((atom_dev, samples, width), jnp.bfloat16),
            jax.ShapeDtypeStruct((samples, tok_dev, tok_width), jnp.bfloat16),
            jax.ShapeDtypeStruct((samples, tok_dev, tok_width), jnp.bfloat16),
        ),
        in_specs=[vmem] * 3
        + [pl.BlockSpec(memory_space=pltpu.SMEM)]
        + [vmem] * 7
        + [hbm],
        out_specs=(vmem, vmem, vmem),
        scratch_shapes=[
            pltpu.VMEM(w_query.shape, w_query.dtype),
            pltpu.SemaphoreType.DMA((1,)),
        ],
        cost_estimate=pl.CostEstimate(
            flops=flops,
            transcendentals=samples * ATOM_HEADS * rows * ext_rows,
            bytes_accessed=2 * (ext_rows + atom_dev) * samples * width
            + 2 * width * (3 * width + width + tok_width)
            + 4 * samples * tok_dev * tok_width,
        ),
    )(
        atom_feat,
        low,
        upper,
        window_shift,
        w_atom_query,
        w_atom_key,
        w_atom_value,
        w_atom_out,
        w_to_token,
        atom_token[None, :],
        token_in,
        w_query,
    )
    bias = jnp.einsum("qkc,ch->qhk", pair, w_bias, preferred_element_type=jnp.float32)
    bias = bias.reshape(tok_dev * TOKEN_HEADS, count)

    every = lax.all_gather(state_t, "row", axis=1, tiled=True)
    token_out = pl.pallas_call(
        functools.partial(token_kernel, heads=TOKEN_HEADS),
        out_shape=jax.ShapeDtypeStruct((tok_dev, samples, tok_width), jnp.bfloat16),
        in_specs=[vmem, vmem, vmem, vmem, vmem, hbm, hbm, hbm],
        out_specs=vmem,
        scratch_shapes=[
            pltpu.VMEM(w_key.shape, w_key.dtype),
            pltpu.VMEM(w_value.shape, w_value.dtype),
            pltpu.VMEM(w_out.shape, w_out.dtype),
            pltpu.SemaphoreType.DMA((3,)),
        ],
        cost_estimate=pl.CostEstimate(
            flops=2 * samples * tok_width * (
                2 * count * tok_width + 2 * tok_dev * tok_width + 2 * TOKEN_HEADS * tok_dev * count
            ),
            transcendentals=samples * TOKEN_HEADS * tok_dev * count,
            bytes_accessed=2 * 4 * tok_width * tok_width
            + 2 * samples * (count + 2 * tok_dev) * tok_width
            + 4 * TOKEN_HEADS * tok_dev * count,
        ),
    )(
        every,
        state_t,
        query_t,
        bias,
        key_mask[None, :],
        w_key,
        w_value,
        w_out,
    )
    return (atom_out, token_out)


def solution(mesh):
    return jax.shard_map(
        on_device,
        mesh=mesh,
        in_specs=(
            P(("groups", "row"), None, None),
            P(("groups", "row")),
            P("groups"),
            P(("groups", "row"), None, None),
            P(("groups", "row"), None, None),
            P("groups"),
            P(),
            P(),
            P(),
            P(),
            P(),
            P(),
            P(),
            P(),
            P(),
            P(),
        ),
        out_specs=(P(("groups", "row"), None, None), P(("groups", "row"), None, None)),
        check_vma=False,
    )
```

```python
import functools
import math

import jax
import jax.numpy as jnp
from jax import lax
from jax.experimental import pallas as pl
from jax.experimental.pallas import tpu as pltpu
from jax.sharding import PartitionSpec as P

ATOM_HEADS = 4
QBLOCK = 32
KWIN = 128
SHIFT = 16
TOKEN_HEADS = 16


def layer_norm(values):
    values = values.astype(jnp.float32)
    mean = jnp.mean(values, axis=-1, keepdims=True)
    var = jnp.mean((values - mean) ** 2, axis=-1, keepdims=True)
    return (values - mean) / jnp.sqrt(var + 1e-05)


def project(values, weight):
    return jnp.einsum("asc,cd->asd", values, weight, preferred_element_type=jnp.float32)


def shifted(block, axis, step):
    count = lax.axis_size(axis)
    route = [(i, i + step) for i in range(count) if 0 <= i + step < count]
    return lax.ppermute(block, axis, route)


def atom_kernel(
    own_ref,
    low_ref,
    upper_ref,
    shift_ref,
    wq_ref,
    wk_ref,
    wv_ref,
    wo_ref,
    wt_ref,
    ids_ref,
    token_ref,
    wq_hbm,
    atom_ref,
    state_ref,
    query_ref,
    wtq_ref,
    sems,
    *,
    atom_dev,
    rows,
    low_rows,
    high_rows,
    head_dim,
    devices,
):
    f32, bf16 = jnp.float32, jnp.bfloat16
    copies = [pltpu.make_async_copy(wq_hbm, wtq_ref, sems.at[0])]
    for copy in copies:
        copy.start()
    _, samples, width = own_ref.shape
    ext_rows = low_rows + atom_dev + high_rows
    lane = lax.broadcasted_iota(jnp.int32, (1, width), 1) // head_dim
    head_masks = [(lane == h).astype(f32) for h in range(ATOM_HEADS)]
    root = jnp.float32(math.sqrt(head_dim))
    rank = lax.axis_index("row")
    base = rank * atom_dev
    total = devices * atom_dev
    tok_dev = token_ref.shape[0]
    row_block = lax.broadcasted_iota(jnp.int32, (rows, 1), 0) // QBLOCK
    next_shift = upper_ref[pl.ds(atom_dev, 1), 0, :].astype(f32)[:, 0:1].astype(jnp.int32)
    shift = jnp.where(row_block == rows // QBLOCK - 1, next_shift, 0)
    for j in range(rows // QBLOCK - 1):
        shift = shift + jnp.where(row_block == j, shift_ref[j], 0)
    first = row_block * QBLOCK + SHIFT + shift
    lo = jnp.maximum(first, low_rows - base)
    hi = jnp.minimum(first + KWIN, total - base + low_rows)
    column = lax.broadcasted_iota(jnp.int32, (rows, ext_rows), 1)
    keep = (column >= lo) & (column < hi)
    keep_all = jnp.concatenate([keep] * ATOM_HEADS, axis=0)
    own_start = pl.multiple_of(base, atom_dev)
    next_start = pl.multiple_of(jnp.minimum(base + atom_dev, total - atom_dev), atom_dev)
    next_ids = ids_ref[:, pl.ds(next_start, atom_dev)][:, 0 : rows - atom_dev]
    next_ids = jnp.where(rank < devices - 1, next_ids, -1)
    row_ids = jnp.concatenate([ids_ref[:, pl.ds(own_start, atom_dev)], next_ids], axis=1)
    own_ids = rank * tok_dev + lax.broadcasted_iota(jnp.int32, (tok_dev, 1), 0)
    onehot = (own_ids == row_ids).astype(f32)
    counts = jnp.sum(onehot, axis=1, keepdims=True)
    onehot = onehot.astype(bf16)
    xs, xns = [], []
    for s in range(samples):
        x = jnp.concatenate(
            [
                low_ref[atom_dev - low_rows : atom_dev, s, :],
                own_ref[:, s, :],
                upper_ref[0:high_rows, s, :],
            ],
            axis=0,
        ).astype(f32)
        mean = jnp.mean(x, axis=-1, keepdims=True)
        var = jnp.mean((x - mean) ** 2, axis=-1, keepdims=True)
        xs.append(x)
        xns.append(((x - mean) / jnp.sqrt(var + 1e-05)).astype(bf16))
    xn_all = jnp.concatenate(xns, axis=0)
    q_all = jnp.dot(
        jnp.concatenate([xn[low_rows : low_rows + rows] for xn in xns], axis=0),
        wq_ref[...],
        preferred_element_type=f32,
    ).astype(bf16)
    kv_all = jnp.dot(
        xn_all,
        jnp.concatenate([wk_ref[...], wv_ref[...]], axis=1),
        preferred_element_type=f32,
    ).astype(bf16)
    k_all = kv_all[:, 0:width]
    v_all = kv_all[:, width:]
    mixed = []
    for s in range(samples):
        q = q_all[s * rows : (s + 1) * rows]
        k = k_all[s * ext_rows : (s + 1) * ext_rows]
        v = v_all[s * ext_rows : (s + 1) * ext_rows]
        stacked = jnp.concatenate(
            [q * head_masks[h].astype(bf16) for h in range(ATOM_HEADS)], axis=0
        )
        sc = lax.dot_general(
            stacked, k, (((1,), (1,)), ((), ())), preferred_element_type=f32
        ) / root
        sc = jnp.where(keep_all, sc, -1e30)
        top = jnp.max(sc, axis=-1, keepdims=True)
        e = jnp.where(keep_all, jnp.exp(sc - top), 0.0)
        tot = jnp.sum(e, axis=-1, keepdims=True)
        o = jnp.dot(e.astype(bf16), v, preferred_element_type=f32) / tot
        acc = o[0:rows] * head_masks[0]
        for h in range(1, ATOM_HEADS):
            acc = acc + o[h * rows : (h + 1) * rows] * head_masks[h]
        mixed.append(acc.astype(bf16))
    base = jnp.concatenate([x[low_rows : low_rows + rows] for x in xs], axis=0)
    out = (
        base + jnp.dot(jnp.concatenate(mixed, axis=0), wo_ref[...], preferred_element_type=f32)
    ).astype(bf16)
    for s in range(samples):
        atom_ref[:, s, :] = out[s * rows : s * rows + atom_dev]
    hidden = jnp.maximum(jnp.dot(out, wt_ref[...], preferred_element_type=f32), 0.0)
    top_part = hidden.astype(bf16)
    rest = hidden - top_part.astype(f32)
    mid_part = rest.astype(bf16)
    low_part = (rest - mid_part.astype(f32)).astype(bf16)
    zero = jnp.zeros_like(onehot)
    diagonal = jnp.concatenate(
        [
            jnp.concatenate([onehot if c == r else zero for c in range(samples)], axis=1)
            for r in range(samples)
        ],
        axis=0,
    )
    sums = (
        jnp.dot(diagonal, top_part, preferred_element_type=f32)
        + jnp.dot(diagonal, mid_part, preferred_element_type=f32)
        + jnp.dot(diagonal, low_part, preferred_element_type=f32)
    )
    tns = []
    for s in range(samples):
        st = (token_ref[:, s, :].astype(f32) + sums[s * tok_dev : (s + 1) * tok_dev] / counts)
        st = st.astype(bf16)
        state_ref[s] = st
        st = st.astype(f32)
        mean = jnp.mean(st, axis=-1, keepdims=True)
        var = jnp.mean((st - mean) ** 2, axis=-1, keepdims=True)
        tns.append(((st - mean) / jnp.sqrt(var + 1e-05)).astype(bf16))
    copies[0].wait()
    query = jnp.dot(jnp.concatenate(tns, axis=0), wtq_ref[...], preferred_element_type=f32)
    query = query.astype(bf16)
    for s in range(samples):
        query_ref[s] = query[s * tok_dev : (s + 1) * tok_dev]


def token_kernel(
    every_ref,
    own_ref,
    query_ref,
    bias_ref,
    flags_ref,
    wk_hbm,
    wv_hbm,
    wo_hbm,
    out_ref,
    wk_ref,
    wv_ref,
    wo_ref,
    sems,
    *,
    heads,
):
    copies = [
        pltpu.make_async_copy(src, dst, sems.at[i])
        for i, (src, dst) in enumerate([(wk_hbm, wk_ref), (wv_hbm, wv_ref), (wo_hbm, wo_ref)])
    ]
    for copy in copies:
        copy.start()
    f32, bf16 = jnp.float32, jnp.bfloat16
    samples, tok_dev, width = own_ref.shape
    head_dim = width // heads
    lane = lax.broadcasted_iota(jnp.int32, (1, width), 1) // head_dim
    head_masks = [(lane == h).astype(f32) for h in range(heads)]
    root = jnp.float32(math.sqrt(head_dim))
    keep = flags_ref[...] > 0
    mask_rows = jnp.concatenate(head_masks, axis=0)

    def normed(x):
        mean = jnp.mean(x, axis=-1, keepdims=True)
        var = jnp.mean((x - mean) ** 2, axis=-1, keepdims=True)
        return ((x - mean) / jnp.sqrt(var + 1e-05)).astype(bf16)

    allx = jnp.concatenate([normed(every_ref[s].astype(f32)) for s in range(samples)], axis=0)
    count = every_ref.shape[1]
    copies[0].wait()
    k_all = jnp.dot(allx, wk_ref[...], preferred_element_type=f32).astype(bf16)
    copies[1].wait()
    v_all = jnp.dot(allx, wv_ref[...], preferred_element_type=f32).astype(bf16)
    ks = [k_all[s * count : (s + 1) * count] for s in range(samples)]
    vs = [v_all[s * count : (s + 1) * count] for s in range(samples)]
    bias = bias_ref[...]
    mixes = []
    for s in range(samples):
        q = query_ref[s]
        stacked = (q[:, None, :] * mask_rows.astype(bf16)[None, :, :]).reshape(
            tok_dev * heads, width
        )
        sc = lax.dot_general(
            stacked, ks[s], (((1,), (1,)), ((), ())), preferred_element_type=f32
        ) / root + bias
        sc = jnp.where(keep, sc, -1e30)
        top = jnp.max(sc, axis=-1, keepdims=True)
        e = jnp.where(keep, jnp.exp(sc - top), 0.0)
        tot = jnp.sum(e, axis=-1, keepdims=True)
        o = jnp.dot(e.astype(bf16), vs[s], preferred_element_type=f32) / tot
        picked = o.reshape(tok_dev, heads, width) * mask_rows[None, :, :]
        mixes.append(jnp.sum(picked, axis=1).astype(bf16))
    copies[2].wait()
    projected = jnp.dot(jnp.concatenate(mixes, axis=0), wo_ref[...], preferred_element_type=f32)
    for s in range(samples):
        own = own_ref[s].astype(f32)
        out_ref[:, s, :] = (own + projected[s * tok_dev : (s + 1) * tok_dev]).astype(bf16)


def on_device(
    atom_feat,
    window_shift,
    atom_token,
    token_in,
    pair,
    key_mask,
    w_atom_query,
    w_atom_key,
    w_atom_value,
    w_atom_out,
    w_to_token,
    w_query,
    w_key,
    w_value,
    w_out,
    w_bias,
):
    high = lax.Precision.HIGHEST
    atom_dev, samples, width = atom_feat.shape
    tok_dev = token_in.shape[0]
    tok_width = token_in.shape[2]
    devices = lax.axis_size("row")
    rank = lax.axis_index("row")
    atom_base = rank * atom_dev
    total_atoms = atom_dev * devices
    margin = (KWIN - QBLOCK) // 2
    low_rows = margin + SHIFT
    span = KWIN + 2 * SHIFT
    high_rows = span - low_rows
    blocks = atom_dev // QBLOCK + 1

    low = shifted(atom_feat, "row", 1)
    shift_row = jnp.broadcast_to(window_shift[0], (1, samples, width)).astype(jnp.bfloat16)
    upper = shifted(jnp.concatenate([atom_feat, shift_row], axis=0), "row", -1)

    head_dim = width // ATOM_HEADS
    rows = blocks * QBLOCK
    ext_rows = low_rows + atom_dev + high_rows
    kernel = functools.partial(
        atom_kernel,
        atom_dev=atom_dev,
        rows=rows,
        low_rows=low_rows,
        high_rows=high_rows,
        head_dim=head_dim,
        devices=devices,
    )
    vmem = pl.BlockSpec(memory_space=pltpu.VMEM)
    flops = 2 * samples * (
        ext_rows * width * 3 * width
        + rows * width * (width + tok_width)
        + ATOM_HEADS * rows * ext_rows * width * 2
        + 3 * tok_dev * rows * tok_width
    )
    hbm = pl.BlockSpec(memory_space=pl.ANY)
    count = tok_dev * devices
    atom_out, state_t, query_t = pl.pallas_call(
        kernel,
        out_shape=(
            jax.ShapeDtypeStruct((atom_dev, samples, width), jnp.bfloat16),
            jax.ShapeDtypeStruct((samples, tok_dev, tok_width), jnp.bfloat16),
            jax.ShapeDtypeStruct((samples, tok_dev, tok_width), jnp.bfloat16),
        ),
        in_specs=[vmem] * 3
        + [pl.BlockSpec(memory_space=pltpu.SMEM)]
        + [vmem] * 7
        + [hbm],
        out_specs=(vmem, vmem, vmem),
        scratch_shapes=[
            pltpu.VMEM(w_query.shape, w_query.dtype),
            pltpu.SemaphoreType.DMA((1,)),
        ],
        cost_estimate=pl.CostEstimate(
            flops=flops,
            transcendentals=samples * ATOM_HEADS * rows * ext_rows,
            bytes_accessed=2 * (ext_rows + atom_dev) * samples * width
            + 2 * width * (3 * width + width + tok_width)
            + 4 * samples * tok_dev * tok_width,
        ),
    )(
        atom_feat,
        low,
        upper,
        window_shift,
        w_atom_query,
        w_atom_key,
        w_atom_value,
        w_atom_out,
        w_to_token,
        atom_token[None, :],
        token_in,
        w_query,
    )
    bias = jnp.einsum("qkc,ch->qhk", pair, w_bias, preferred_element_type=jnp.float32)
    bias = bias.reshape(tok_dev * TOKEN_HEADS, count)

    every = lax.all_gather(state_t, "row", axis=1, tiled=True)
    token_out = pl.pallas_call(
        functools.partial(token_kernel, heads=TOKEN_HEADS),
        out_shape=jax.ShapeDtypeStruct((tok_dev, samples, tok_width), jnp.bfloat16),
        in_specs=[vmem, vmem, vmem, vmem, vmem, hbm, hbm, hbm],
        out_specs=vmem,
        scratch_shapes=[
            pltpu.VMEM(w_key.shape, w_key.dtype),
            pltpu.VMEM(w_value.shape, w_value.dtype),
            pltpu.VMEM(w_out.shape, w_out.dtype),
            pltpu.SemaphoreType.DMA((3,)),
        ],
        cost_estimate=pl.CostEstimate(
            flops=2 * samples * tok_width * (
                2 * count * tok_width + 2 * tok_dev * tok_width + 2 * TOKEN_HEADS * tok_dev * count
            ),
            transcendentals=samples * TOKEN_HEADS * tok_dev * count,
            bytes_accessed=2 * 4 * tok_width * tok_width
            + 2 * samples * (count + 2 * tok_dev) * tok_width
            + 4 * TOKEN_HEADS * tok_dev * count,
        ),
    )(
        every,
        state_t,
        query_t,
        bias,
        key_mask[None, :],
        w_key,
        w_value,
        w_out,
    )
    return (atom_out, token_out)


def solution(mesh):
    return jax.shard_map(
        on_device,
        mesh=mesh,
        in_specs=(
            P(("groups", "row"), None, None),
            P(("groups", "row")),
            P("groups"),
            P(("groups", "row"), None, None),
            P(("groups", "row"), None, None),
            P("groups"),
            P(),
            P(),
            P(),
            P(),
            P(),
            P(),
            P(),
            P(),
            P(),
            P(),
        ),
        out_specs=(P(("groups", "row"), None, None), P(("groups", "row"), None, None)),
        check_vma=False,
    )
```

```python
import functools
import math

import jax
import jax.numpy as jnp
from jax import lax
from jax.experimental import pallas as pl
from jax.experimental.pallas import tpu as pltpu
from jax.sharding import PartitionSpec as P

ATOM_HEADS = 4
QBLOCK = 32
KWIN = 128
SHIFT = 16
TOKEN_HEADS = 16


def layer_norm(values):
    values = values.astype(jnp.float32)
    mean = jnp.mean(values, axis=-1, keepdims=True)
    var = jnp.mean((values - mean) ** 2, axis=-1, keepdims=True)
    return (values - mean) / jnp.sqrt(var + 1e-05)


def project(values, weight):
    return jnp.einsum("asc,cd->asd", values, weight, preferred_element_type=jnp.float32)


def shifted(block, axis, step):
    count = lax.axis_size(axis)
    route = [(i, i + step) for i in range(count) if 0 <= i + step < count]
    return lax.ppermute(block, axis, route)


def atom_kernel(
    own_ref,
    low_ref,
    upper_ref,
    shift_ref,
    wq_ref,
    wk_ref,
    wv_ref,
    wo_ref,
    wt_ref,
    ids_ref,
    token_ref,
    wq_hbm,
    atom_ref,
    state_ref,
    query_ref,
    wtq_ref,
    sems,
    *,
    atom_dev,
    rows,
    low_rows,
    high_rows,
    head_dim,
    devices,
):
    f32, bf16 = jnp.float32, jnp.bfloat16
    copies = [pltpu.make_async_copy(wq_hbm, wtq_ref, sems.at[0])]
    for copy in copies:
        copy.start()
    _, samples, width = own_ref.shape
    ext_rows = low_rows + atom_dev + high_rows
    lane = lax.broadcasted_iota(jnp.int32, (1, width), 1) // head_dim
    head_masks = [(lane == h).astype(f32) for h in range(ATOM_HEADS)]
    root = jnp.float32(math.sqrt(head_dim))
    rank = lax.axis_index("row")
    base = rank * atom_dev
    total = devices * atom_dev
    tok_dev = token_ref.shape[0]
    row_block = lax.broadcasted_iota(jnp.int32, (rows, 1), 0) // QBLOCK
    next_shift = upper_ref[pl.ds(atom_dev, 1), 0, :].astype(f32)[:, 0:1].astype(jnp.int32)
    shift = jnp.where(row_block == rows // QBLOCK - 1, next_shift, 0)
    for j in range(rows // QBLOCK - 1):
        shift = shift + jnp.where(row_block == j, shift_ref[j], 0)
    first = row_block * QBLOCK + SHIFT + shift
    lo = jnp.maximum(first, low_rows - base)
    hi = jnp.minimum(first + KWIN, total - base + low_rows)
    column = lax.broadcasted_iota(jnp.int32, (rows, ext_rows), 1)
    keep = (column >= lo) & (column < hi)
    keep_all = jnp.concatenate([keep] * ATOM_HEADS, axis=0)
    own_start = pl.multiple_of(base, atom_dev)
    next_start = pl.multiple_of(jnp.minimum(base + atom_dev, total - atom_dev), atom_dev)
    next_ids = ids_ref[:, pl.ds(next_start, atom_dev)][:, 0 : rows - atom_dev]
    next_ids = jnp.where(rank < devices - 1, next_ids, -1)
    row_ids = jnp.concatenate([ids_ref[:, pl.ds(own_start, atom_dev)], next_ids], axis=1)
    own_ids = rank * tok_dev + lax.broadcasted_iota(jnp.int32, (tok_dev, 1), 0)
    onehot = (own_ids == row_ids).astype(f32)
    counts = jnp.sum(onehot, axis=1, keepdims=True)
    onehot = onehot.astype(bf16)
    xs, xns = [], []
    for s in range(samples):
        x = jnp.concatenate(
            [
                low_ref[atom_dev - low_rows : atom_dev, s, :],
                own_ref[:, s, :],
                upper_ref[0:high_rows, s, :],
            ],
            axis=0,
        ).astype(f32)
        mean = jnp.mean(x, axis=-1, keepdims=True)
        var = jnp.mean((x - mean) ** 2, axis=-1, keepdims=True)
        xs.append(x)
        xns.append(((x - mean) / jnp.sqrt(var + 1e-05)).astype(bf16))
    xn_all = jnp.concatenate(xns, axis=0)
    q_all = jnp.dot(
        jnp.concatenate([xn[low_rows : low_rows + rows] for xn in xns], axis=0),
        wq_ref[...],
        preferred_element_type=f32,
    ).astype(bf16)
    k_all = jnp.dot(xn_all, wk_ref[...], preferred_element_type=f32).astype(bf16)
    v_all = jnp.dot(xn_all, wv_ref[...], preferred_element_type=f32).astype(bf16)
    mixed = []
    for s in range(samples):
        q = q_all[s * rows : (s + 1) * rows]
        k = k_all[s * ext_rows : (s + 1) * ext_rows]
        v = v_all[s * ext_rows : (s + 1) * ext_rows]
        stacked = jnp.concatenate(
            [q * head_masks[h].astype(bf16) for h in range(ATOM_HEADS)], axis=0
        )
        sc = lax.dot_general(
            stacked, k, (((1,), (1,)), ((), ())), preferred_element_type=f32
        ) / root
        sc = jnp.where(keep_all, sc, -1e30)
        top = jnp.max(sc, axis=-1, keepdims=True)
        e = jnp.where(keep_all, jnp.exp(sc - top), 0.0)
        tot = jnp.sum(e, axis=-1, keepdims=True)
        o = jnp.dot(e.astype(bf16), v, preferred_element_type=f32) / tot
        acc = o[0:rows] * head_masks[0]
        for h in range(1, ATOM_HEADS):
            acc = acc + o[h * rows : (h + 1) * rows] * head_masks[h]
        mixed.append(acc.astype(bf16))
    base = jnp.concatenate([x[low_rows : low_rows + rows] for x in xs], axis=0)
    out = (
        base + jnp.dot(jnp.concatenate(mixed, axis=0), wo_ref[...], preferred_element_type=f32)
    ).astype(bf16)
    for s in range(samples):
        atom_ref[:, s, :] = out[s * rows : s * rows + atom_dev]
    hidden = jnp.maximum(jnp.dot(out, wt_ref[...], preferred_element_type=f32), 0.0)
    top_part = hidden.astype(bf16)
    rest = hidden - top_part.astype(f32)
    mid_part = rest.astype(bf16)
    zero = jnp.zeros_like(onehot)
    diagonal = jnp.concatenate(
        [
            jnp.concatenate([onehot if c == r else zero for c in range(samples)], axis=1)
            for r in range(samples)
        ],
        axis=0,
    )
    sums = (
        jnp.dot(diagonal, top_part, preferred_element_type=f32)
        + jnp.dot(diagonal, mid_part, preferred_element_type=f32)
    )
    tns = []
    for s in range(samples):
        st = (token_ref[:, s, :].astype(f32) + sums[s * tok_dev : (s + 1) * tok_dev] / counts)
        st = st.astype(bf16)
        state_ref[s] = st
        st = st.astype(f32)
        mean = jnp.mean(st, axis=-1, keepdims=True)
        var = jnp.mean((st - mean) ** 2, axis=-1, keepdims=True)
        tns.append(((st - mean) / jnp.sqrt(var + 1e-05)).astype(bf16))
    copies[0].wait()
    query = jnp.dot(jnp.concatenate(tns, axis=0), wtq_ref[...], preferred_element_type=f32)
    query = query.astype(bf16)
    for s in range(samples):
        query_ref[s] = query[s * tok_dev : (s + 1) * tok_dev]


def token_kernel(
    every_ref,
    own_ref,
    query_ref,
    bias_ref,
    flags_ref,
    wk_hbm,
    wv_hbm,
    wo_hbm,
    out_ref,
    wk_ref,
    wv_ref,
    wo_ref,
    sems,
    *,
    heads,
):
    copies = [
        pltpu.make_async_copy(src, dst, sems.at[i])
        for i, (src, dst) in enumerate([(wk_hbm, wk_ref), (wv_hbm, wv_ref), (wo_hbm, wo_ref)])
    ]
    for copy in copies:
        copy.start()
    f32, bf16 = jnp.float32, jnp.bfloat16
    samples, tok_dev, width = own_ref.shape
    head_dim = width // heads
    lane = lax.broadcasted_iota(jnp.int32, (1, width), 1) // head_dim
    head_masks = [(lane == h).astype(f32) for h in range(heads)]
    root = jnp.float32(math.sqrt(head_dim))
    keep = flags_ref[...] > 0
    mask_rows = jnp.concatenate(head_masks, axis=0)

    def normed(x):
        mean = jnp.mean(x, axis=-1, keepdims=True)
        var = jnp.mean((x - mean) ** 2, axis=-1, keepdims=True)
        return ((x - mean) / jnp.sqrt(var + 1e-05)).astype(bf16)

    allx = jnp.concatenate([normed(every_ref[s].astype(f32)) for s in range(samples)], axis=0)
    count = every_ref.shape[1]
    copies[0].wait()
    k_all = jnp.dot(allx, wk_ref[...], preferred_element_type=f32).astype(bf16)
    copies[1].wait()
    v_all = jnp.dot(allx, wv_ref[...], preferred_element_type=f32).astype(bf16)
    ks = [k_all[s * count : (s + 1) * count] for s in range(samples)]
    vs = [v_all[s * count : (s + 1) * count] for s in range(samples)]
    bias = bias_ref[...]
    mixes = []
    for s in range(samples):
        q = query_ref[s]
        stacked = (q[:, None, :] * mask_rows.astype(bf16)[None, :, :]).reshape(
            tok_dev * heads, width
        )
        sc = lax.dot_general(
            stacked, ks[s], (((1,), (1,)), ((), ())), preferred_element_type=f32
        ) / root + bias
        sc = jnp.where(keep, sc, -1e30)
        top = jnp.max(sc, axis=-1, keepdims=True)
        e = jnp.where(keep, jnp.exp(sc - top), 0.0)
        tot = jnp.sum(e, axis=-1, keepdims=True)
        o = jnp.dot(e.astype(bf16), vs[s], preferred_element_type=f32) / tot
        picked = o.reshape(tok_dev, heads, width) * mask_rows[None, :, :]
        mixes.append(jnp.sum(picked, axis=1).astype(bf16))
    copies[2].wait()
    projected = jnp.dot(jnp.concatenate(mixes, axis=0), wo_ref[...], preferred_element_type=f32)
    for s in range(samples):
        own = own_ref[s].astype(f32)
        out_ref[:, s, :] = (own + projected[s * tok_dev : (s + 1) * tok_dev]).astype(bf16)


def on_device(
    atom_feat,
    window_shift,
    atom_token,
    token_in,
    pair,
    key_mask,
    w_atom_query,
    w_atom_key,
    w_atom_value,
    w_atom_out,
    w_to_token,
    w_query,
    w_key,
    w_value,
    w_out,
    w_bias,
):
    high = lax.Precision.HIGHEST
    atom_dev, samples, width = atom_feat.shape
    tok_dev = token_in.shape[0]
    tok_width = token_in.shape[2]
    devices = lax.axis_size("row")
    rank = lax.axis_index("row")
    atom_base = rank * atom_dev
    total_atoms = atom_dev * devices
    margin = (KWIN - QBLOCK) // 2
    low_rows = margin + SHIFT
    span = KWIN + 2 * SHIFT
    high_rows = span - low_rows
    blocks = atom_dev // QBLOCK + 1

    low = shifted(atom_feat, "row", 1)
    shift_row = jnp.broadcast_to(window_shift[0], (1, samples, width)).astype(jnp.bfloat16)
    upper = shifted(jnp.concatenate([atom_feat, shift_row], axis=0), "row", -1)

    head_dim = width // ATOM_HEADS
    rows = blocks * QBLOCK
    ext_rows = low_rows + atom_dev + high_rows
    kernel = functools.partial(
        atom_kernel,
        atom_dev=atom_dev,
        rows=rows,
        low_rows=low_rows,
        high_rows=high_rows,
        head_dim=head_dim,
        devices=devices,
    )
    vmem = pl.BlockSpec(memory_space=pltpu.VMEM)
    flops = 2 * samples * (
        ext_rows * width * 3 * width
        + rows * width * (width + tok_width)
        + ATOM_HEADS * rows * ext_rows * width * 2
        + 3 * tok_dev * rows * tok_width
    )
    hbm = pl.BlockSpec(memory_space=pl.ANY)
    count = tok_dev * devices
    atom_out, state_t, query_t = pl.pallas_call(
        kernel,
        out_shape=(
            jax.ShapeDtypeStruct((atom_dev, samples, width), jnp.bfloat16),
            jax.ShapeDtypeStruct((samples, tok_dev, tok_width), jnp.bfloat16),
            jax.ShapeDtypeStruct((samples, tok_dev, tok_width), jnp.bfloat16),
        ),
        in_specs=[vmem] * 3
        + [pl.BlockSpec(memory_space=pltpu.SMEM)]
        + [vmem] * 7
        + [hbm],
        out_specs=(vmem, vmem, vmem),
        scratch_shapes=[
            pltpu.VMEM(w_query.shape, w_query.dtype),
            pltpu.SemaphoreType.DMA((1,)),
        ],
        cost_estimate=pl.CostEstimate(
            flops=flops,
            transcendentals=samples * ATOM_HEADS * rows * ext_rows,
            bytes_accessed=2 * (ext_rows + atom_dev) * samples * width
            + 2 * width * (3 * width + width + tok_width)
            + 4 * samples * tok_dev * tok_width,
        ),
    )(
        atom_feat,
        low,
        upper,
        window_shift,
        w_atom_query,
        w_atom_key,
        w_atom_value,
        w_atom_out,
        w_to_token,
        atom_token[None, :],
        token_in,
        w_query,
    )
    bias = jnp.einsum("qkc,ch->qhk", pair, w_bias, preferred_element_type=jnp.float32)
    bias = bias.reshape(tok_dev * TOKEN_HEADS, count)

    every = lax.all_gather(state_t, "row", axis=1, tiled=True)
    token_out = pl.pallas_call(
        functools.partial(token_kernel, heads=TOKEN_HEADS),
        out_shape=jax.ShapeDtypeStruct((tok_dev, samples, tok_width), jnp.bfloat16),
        in_specs=[vmem, vmem, vmem, vmem, vmem, hbm, hbm, hbm],
        out_specs=vmem,
        scratch_shapes=[
            pltpu.VMEM(w_key.shape, w_key.dtype),
            pltpu.VMEM(w_value.shape, w_value.dtype),
            pltpu.VMEM(w_out.shape, w_out.dtype),
            pltpu.SemaphoreType.DMA((3,)),
        ],
        cost_estimate=pl.CostEstimate(
            flops=2 * samples * tok_width * (
                2 * count * tok_width + 2 * tok_dev * tok_width + 2 * TOKEN_HEADS * tok_dev * count
            ),
            transcendentals=samples * TOKEN_HEADS * tok_dev * count,
            bytes_accessed=2 * 4 * tok_width * tok_width
            + 2 * samples * (count + 2 * tok_dev) * tok_width
            + 4 * TOKEN_HEADS * tok_dev * count,
        ),
    )(
        every,
        state_t,
        query_t,
        bias,
        key_mask[None, :],
        w_key,
        w_value,
        w_out,
    )
    return (atom_out, token_out)


def solution(mesh):
    return jax.shard_map(
        on_device,
        mesh=mesh,
        in_specs=(
            P(("groups", "row"), None, None),
            P(("groups", "row")),
            P("groups"),
            P(("groups", "row"), None, None),
            P(("groups", "row"), None, None),
            P("groups"),
            P(),
            P(),
            P(),
            P(),
            P(),
            P(),
            P(),
            P(),
            P(),
            P(),
        ),
        out_specs=(P(("groups", "row"), None, None), P(("groups", "row"), None, None)),
        check_vma=False,
    )
```
